32 devices in a mesh: grp: 2 (over x), tm: 8 (over z, y), row: 2 (over core).
Axes of the slice: x: 2, y: 2, z: 4, core: 2. Of those that a mesh axis runs over, the one named last changes fastest.
Arguments:
- frames: bfloat16 [16, 256, 64, 48], P(('grp', 'tm'), None, 'row'), parts along dimension 0, may hold values from 0 to 31, as said below
- clip_start: int32 [16], P('grp'), parts along dimension 0, may hold values 0 or 1
- semantic: int32 [16, 64, 48], P(('grp', 'tm'), 'row'), parts along dimension 0, may hold values from 0 to 18
- instance: int32 [16, 64, 48], P(('grp', 'tm'), 'row'), parts along dimension 0, may hold values from 0 to 63
- aspp_point: bfloat16 [256, 512], replicated, may hold values from -0.25 to 0.25
- aspp_dilated: bfloat16 [3, 9, 256, 512], replicated, may hold values from -0.09375 to 0.09375
- pool_weight: bfloat16 [256, 512], replicated, may hold values from -0.25 to 0.25
- proj_weight: bfloat16 [256, 1280], replicated, may hold values from -0.15625 to 0.15625
- head_weight: bfloat16 [25, 96, 256], replicated, may hold values from -0.078125 to 0.078125
- out_weight: bfloat16 [4, 32], replicated, may hold values from -1 to 1
Outputs:
- predictions: float32 [16, 4, 64, 48], P(('grp', 'tm'), None, 'row'), parts along dimension 0
- losses: float32 [4], P('grp'), parts along dimension 0
The draws below stay inside these ranges and needn't reach their ends.
There are 2 independent parts, one for each index of `grp`. The reference program is written for one: setup_inputs(seed, part) draws one part's arguments, and reference() takes and returns one part's arrays. A program takes and returns all parts, laid end to end along the dimension named above; an argument that names none is the same for every part. Nothing has to cross between parts.
Inputs may be any that keep to these rules, and one draw needn't show every extreme that they name: `frames`: every entry is zero or positive.
All inputs are finite; a program needn't handle non-finite values.
Results may differ from the reference program's by a relative error of at most 0.0075.
Values may be sent and summed in bfloat16 or wider, within the bound.
No kernel may reach another device: no remote copies, remote signals or barrier semaphores. Data moves between devices by JAX's collectives and lax.ppermute only.
A program may use at most 128 MiB of HBM per device.

```python
import jax
import jax.numpy as jnp
from jax import lax

CHANNELS = 256
ASPP = 256
HEAD = 32
CLASSES = 19
THING_FIRST = 11
INSTANCES = 64
W = 48
FRAMES = 8
HEIGHT = 64


def draw_frames(key, part):
    keys = jax.random.split(key, 2)
    shape = (FRAMES, CHANNELS, HEIGHT, W)
    channel_scale = jnp.exp(jax.random.uniform(keys[0], (1, CHANNELS, 1, 1), jnp.float32, jnp.log(0.3), jnp.log(3.0)))
    frame_pos = jnp.arange(FRAMES, dtype=jnp.float32).reshape(FRAMES, 1, 1, 1) / max(FRAMES - 1, 1)
    row_pos = jnp.arange(HEIGHT, dtype=jnp.float32).reshape(1, 1, HEIGHT, 1) / max(HEIGHT - 1, 1)
    scaling = channel_scale * (0.6 + 1.2 * frame_pos) * (0.6 + 0.8 * row_pos)
    values = jnp.minimum(jnp.abs(jax.random.normal(keys[1], shape, jnp.float32)), 4.0)
    return (values * scaling).astype(jnp.bfloat16)


def set_ends(drawn, rng, smallest, top_value):
    extent = drawn.shape
    spot = [jax.random.randint(jax.random.fold_in(rng, axis), (), 0, extent[axis]) for axis in range(len(extent))]
    drawn = drawn.at[tuple(spot)].set(smallest)
    longest = extent.index(max(extent))
    spot[longest] = (spot[longest] + 1) % extent[longest]
    return drawn.at[tuple(spot)].set(top_value)


def normal_values(stream_key, extent, scale, reach, kind=jnp.bfloat16):
    result = scale * jax.random.normal(stream_key, extent, jnp.float32)
    return jnp.clip(result, min=-reach, max=reach).astype(kind)


def setup_inputs(seed: int = 0, part: int = 0) -> dict:
    streams_of = jax.random.split(jax.random.key(seed), 11)
    part_splits = jax.random.split(jax.random.fold_in(streams_of[10], part), 11)
    frames = draw_frames(jax.random.fold_in(jax.random.fold_in(streams_of[10], part), 71), part)
    clip_start = set_ends((jax.random.randint(part_splits[1], (FRAMES,), 0, 6) < 1).astype(jnp.int32), jax.random.fold_in(part_splits[1], 1), 0, 1)
    semantic = set_ends(jax.random.randint(part_splits[2], (FRAMES, HEIGHT, W), 0, CLASSES), jax.random.fold_in(part_splits[2], 1), 0, CLASSES - 1).astype(jnp.int32)
    instance = set_ends(jax.random.randint(part_splits[3], (FRAMES, HEIGHT, W), 0, INSTANCES), jax.random.fold_in(part_splits[3], 1), 0, INSTANCES - 1).astype(jnp.int32)
    aspp_point = normal_values(streams_of[4], (ASPP, 2 * CHANNELS), (2 * CHANNELS) ** -0.5, 0.25)
    aspp_dilated = normal_values(streams_of[5], (3, 9, ASPP, 2 * CHANNELS), (18 * CHANNELS) ** -0.5, 0.09375)
    pool_weight = normal_values(streams_of[6], (ASPP, 2 * CHANNELS), (2 * CHANNELS) ** -0.5, 0.25)
    proj_weight = normal_values(streams_of[7], (ASPP, 5 * ASPP), (5 * ASPP) ** -0.5, 0.15625)
    head_weight = normal_values(streams_of[8], (25, 3 * HEAD, ASPP), (25 * ASPP) ** -0.5, 0.078125)
    out_weight = normal_values(streams_of[9], (4, HEAD), HEAD ** -0.5, 1.0)
    return {"frames": frames, "clip_start": clip_start, "semantic": semantic, "instance": instance, "aspp_point": aspp_point, "aspp_dilated": aspp_dilated, "pool_weight": pool_weight, "proj_weight": proj_weight, "head_weight": head_weight, "out_weight": out_weight}


DILATIONS = (6, 12, 18)
aspp_reach = 18
center_sigma = 8.0
offset_weight = 0.01


def conv_taps(padded, filters, margin, spread, kernel, row_count, col_count):
    running = None
    middle = kernel // 2
    for vertical in range(kernel):
        for lateral in range(kernel):
            row_top = margin + (vertical - middle) * spread
            col_left = margin + (lateral - middle) * spread
            window = padded[:, row_top:row_top + row_count, col_left:col_left + col_count]
            flattened = window.reshape(window.shape[0], row_count * col_count)
            partial_value = jnp.dot(filters[kernel * vertical + lateral], flattened, preferred_element_type=jnp.float32)
            running = partial_value if running is None else running + partial_value
    return running.reshape(-1, row_count, col_count)


def relu_bf16(values):
    return jnp.maximum(values, 0.0).astype(jnp.bfloat16)


def emit_heads(head_out, out_weight):
    groups = head_out.astype(jnp.float32).reshape(3, -1, head_out.shape[1], head_out.shape[2])
    weights32 = out_weight.astype(jnp.float32)
    center_map = jnp.einsum("c,crw->rw", weights32[0], groups[0])
    offset_map = jnp.einsum("oc,crw->orw", weights32[1:3], groups[1])
    depth_map = jnp.einsum("c,crw->rw", weights32[3], groups[2])
    return jnp.concatenate([center_map[None], offset_map, depth_map[None]], 0)


def reference(frames, clip_start, semantic, instance, aspp_point, aspp_dilated, pool_weight, proj_weight, head_weight, out_weight):
    ahead_index = ((jnp.arange(FRAMES, dtype=jnp.int32) + 1) % FRAMES).astype(jnp.int32)
    at_end = clip_start[ahead_index] == 1
    later = jnp.where(at_end[:, None, None, None], frames, frames[ahead_index])

    def frame_heads(paired):
        own_frame, later_frame = paired
        joined = jnp.concatenate([own_frame, later_frame], 0)
        channel_count = joined.shape[0]
        padded = jnp.pad(joined, ((0, 0), (aspp_reach, aspp_reach), (aspp_reach, aspp_reach)))
        flattened = joined.reshape(channel_count, HEIGHT * W)
        branches = [relu_bf16(jnp.dot(aspp_point, flattened, preferred_element_type=jnp.float32)).reshape(ASPP, HEIGHT, W)]
        for branch_index, spread in enumerate(DILATIONS):
            branches.append(relu_bf16(conv_taps(padded, aspp_dilated[branch_index], aspp_reach, spread, 3, HEIGHT, W)))
        pooled = (jnp.sum(joined, axis=(1, 2), dtype=jnp.float32) / (HEIGHT * W)).astype(jnp.bfloat16)
        pool_feature = relu_bf16(jnp.dot(pool_weight, pooled, preferred_element_type=jnp.float32))
        stacked = jnp.concatenate(branches, 0).reshape(4 * ASPP, HEIGHT * W)
        mixed = jnp.dot(proj_weight[:, :4 * ASPP], stacked, preferred_element_type=jnp.float32)
        mixed = mixed + jnp.dot(proj_weight[:, 4 * ASPP:], pool_feature, preferred_element_type=jnp.float32)[:, None]
        projected = relu_bf16(mixed).reshape(ASPP, HEIGHT, W)
        head_in = jnp.pad(projected, ((0, 0), (2, 2), (2, 2)))
        head_out = relu_bf16(conv_taps(head_in, head_weight, 2, 1, 5, HEIGHT, W))
        return emit_heads(head_out, out_weight)

    predictions = lax.map(frame_heads, (frames, later))

    counted = (semantic >= THING_FIRST) & (instance > 0)
    labels = jnp.arange(INSTANCES, dtype=jnp.int32)
    onehot = ((instance[:, None] == labels[None, :, None, None]) & counted[:, None]).astype(jnp.float32)
    row_pos = jnp.arange(HEIGHT, dtype=jnp.float32)[:, None] * jnp.ones((1, W), jnp.float32)
    col_pos = jnp.arange(W, dtype=jnp.float32)[None, :] * jnp.ones((HEIGHT, 1), jnp.float32)
    inst_stats = jnp.stack([jnp.sum(onehot, axis=(2, 3)), jnp.sum(onehot * row_pos, axis=(2, 3)), jnp.sum(onehot * col_pos, axis=(2, 3))], 1)
    pixel = jnp.einsum("fsk,fkhw->fshw", inst_stats, onehot, precision=lax.Precision.HIGHEST)
    counts = jnp.where(counted, pixel[:, 0], 1.0)
    centre_row = pixel[:, 1] / counts
    centre_col = pixel[:, 2] / counts
    distance = (row_pos - centre_row) * (row_pos - centre_row) + (col_pos - centre_col) * (col_pos - centre_col)
    heat = jnp.where(counted, jnp.exp(-distance / (2.0 * center_sigma * center_sigma)), 0.0)
    center_err = jnp.sum(jnp.square(predictions[:, 0] - heat))
    offset_err = jnp.sum(jnp.where(counted, jnp.abs(predictions[:, 1] - (centre_row - row_pos)) + jnp.abs(predictions[:, 2] - (centre_col - col_pos)), 0.0))
    counted_total = jnp.sum(counted.astype(jnp.float32))
    losses = jnp.stack([center_err / (FRAMES * HEIGHT * W), offset_weight * offset_err / jnp.maximum(counted_total, 1.0)])
    return predictions, losses
```

```python
import jax
import jax.numpy as jnp
from jax import lax
from jax.sharding import PartitionSpec as P

THING_FIRST = 11
INSTANCES = 64


DILATIONS = (6, 12, 18)
aspp_reach = 18
center_sigma = 8.0
offset_weight = 0.01


def padded_2(block, sides, width):
    for axis, dim in sides:
        count = lax.axis_size(axis)
        forward = [(i, i + 1) for i in range(count - 1)]
        backward = [(target, source) for source, target in forward]
        low = lax.ppermute(
            lax.slice_in_dim(block, block.shape[dim] - width, None, axis=dim), axis, forward
        )
        high = lax.ppermute(lax.slice_in_dim(block, 0, width, axis=dim), axis, backward)
        block = jnp.concatenate([low, block, high], axis=dim)
    return block


def shifted(value, axis, steps):
    count = lax.axis_size(axis)
    pairs = [(source, (source + steps) % count) for source in range(count)]
    return lax.ppermute(value, axis, pairs)


def all_sum(value, axes):
    for axis in axes:
        count = lax.axis_size(axis)
        if count & (count - 1):
            value = jax.tree.map(lambda v: lax.psum(v, axis), value)
            continue
        step = 1
        while step < count:
            pairs = [(i, i ^ step) for i in range(count)]
            other = lax.ppermute(value, axis, pairs)
            value = jax.tree.map(jnp.add, value, other)
            step *= 2
    return value


def dilated_conv(wide, kernel, spread, margin, band_rows):
    rows = wide[None, :, margin - spread : margin + band_rows + spread]
    return lax.conv_general_dilated(
        rows,
        kernel,
        window_strides=(1, 1),
        padding=((0, 0), (spread, spread)),
        rhs_dilation=(spread, spread),
        dimension_numbers=("NCHW", "HWOI", "NCHW"),
        preferred_element_type=jnp.float32,
    )[0]


def relu_bf16(values):
    return jnp.maximum(values, 0.0).astype(jnp.bfloat16)


def emit_heads(head_out, out_weight):
    groups = head_out.reshape(3, -1, head_out.shape[1], head_out.shape[2])
    center_map = jnp.einsum(
        "c,crw->rw", out_weight[0], groups[0], preferred_element_type=jnp.float32
    )
    offset_map = jnp.einsum(
        "oc,crw->orw", out_weight[1:3], groups[1], preferred_element_type=jnp.float32
    )
    depth_map = jnp.einsum(
        "c,crw->rw", out_weight[3], groups[2], preferred_element_type=jnp.float32
    )
    return jnp.concatenate([center_map[None], offset_map, depth_map[None]], 0)


def shards(
    frames,
    clip_start,
    semantic,
    instance,
    aspp_point,
    aspp_dilated,
    pool_weight,
    proj_weight,
    head_weight,
    out_weight,
):
    own_band = frames[0]
    channel_count, band_rows, columns = own_band.shape
    frame_count = clip_start.shape[0]
    height = band_rows * lax.axis_size("row")
    time_index = lax.axis_index("tm")
    row_index = lax.axis_index("row")
    ahead = (time_index + 1) % frame_count
    at_end = lax.dynamic_index_in_dim(clip_start, ahead, 0, keepdims=False) == 1
    later_band = jnp.where(at_end, own_band, shifted(own_band, "tm", -1))
    rim_rows = min(aspp_reach, band_rows)
    extra_rows = aspp_reach - rim_rows

    def widen(band):
        wide = padded_2(band, (("row", 1),), rim_rows)
        return jnp.pad(wide, ((0, 0), (extra_rows, extra_rows), (0, 0)))

    own_wide = widen(own_band)
    later_wide = widen(later_band)
    halves = ((own_wide, own_band, slice(0, channel_count)),
              (later_wide, later_band, slice(channel_count, 2 * channel_count)))

    point = None
    for wide, band, part in halves:
        term = jnp.einsum(
            "oc,crw->orw", aspp_point[:, part], band, preferred_element_type=jnp.float32
        )
        point = term if point is None else point + term
    branches = [relu_bf16(point)]
    for branch_index, spread in enumerate(DILATIONS):
        kernel = aspp_dilated[branch_index].reshape(3, 3, *aspp_dilated.shape[2:])
        total = None
        for wide, band, part in halves:
            term = dilated_conv(wide, kernel[..., part], spread, aspp_reach, band_rows)
            total = term if total is None else total + term
        branches.append(relu_bf16(total))

    counted = (semantic[0] >= THING_FIRST) & (instance[0] > 0)
    labels = jnp.arange(INSTANCES, dtype=jnp.int32)
    onehot = ((instance[0][None] == labels[:, None, None]) & counted[None]).astype(jnp.float32)
    row_pos = (row_index * band_rows + jnp.arange(band_rows, dtype=jnp.int32)).astype(jnp.float32)[
        :, None
    ] * jnp.ones((1, columns), jnp.float32)
    col_pos = jnp.arange(columns, dtype=jnp.float32)[None, :] * jnp.ones(
        (band_rows, 1), jnp.float32
    )
    local_stats = jnp.stack(
        [
            jnp.sum(onehot, axis=(1, 2)),
            jnp.sum(onehot * row_pos, axis=(1, 2)),
            jnp.sum(onehot * col_pos, axis=(1, 2)),
        ],
        0,
    )
    channel_sums = jnp.concatenate(
        [jnp.sum(band, axis=(1, 2), dtype=jnp.float32) for _, band, _ in halves]
    )
    frame_totals, inst_stats = all_sum((channel_sums, local_stats), ("row",))
    pooled = (frame_totals / (height * columns)).astype(jnp.bfloat16)
    pool_feature = relu_bf16(jnp.dot(pool_weight, pooled, preferred_element_type=jnp.float32))
    stacked = jnp.concatenate(branches, 0)
    aspp_width = aspp_point.shape[0]
    mixed = jnp.einsum(
        "oc,crw->orw", proj_weight[:, : 4 * aspp_width], stacked, preferred_element_type=jnp.float32
    )
    mixed = (
        mixed
        + jnp.dot(
            proj_weight[:, 4 * aspp_width :], pool_feature, preferred_element_type=jnp.float32
        )[:, None, None]
    )
    projected = relu_bf16(mixed)
    rimmed = padded_2(projected, (("row", 1),), 2)
    head_kernel = head_weight.reshape(5, 5, *head_weight.shape[1:])
    head_sum = lax.conv_general_dilated(
        rimmed[None],
        head_kernel,
        window_strides=(1, 1),
        padding=((0, 0), (2, 2)),
        dimension_numbers=("NCHW", "HWOI", "NCHW"),
        preferred_element_type=jnp.float32,
    )[0]
    head_out = relu_bf16(head_sum)
    predictions = emit_heads(head_out, out_weight)
    pixel = jnp.einsum("sk,khw->shw", inst_stats, onehot, precision=lax.Precision.HIGHEST)
    counts = jnp.where(counted, pixel[0], 1.0)
    centre_row = pixel[1] / counts
    centre_col = pixel[2] / counts
    distance = (row_pos - centre_row) * (row_pos - centre_row) + (col_pos - centre_col) * (
        col_pos - centre_col
    )
    heat = jnp.where(counted, jnp.exp(-distance / (2.0 * center_sigma * center_sigma)), 0.0)
    center_err = jnp.sum(jnp.square(predictions[0] - heat))
    offset_err = jnp.sum(
        jnp.where(
            counted,
            jnp.abs(predictions[1] - (centre_row - row_pos))
            + jnp.abs(predictions[2] - (centre_col - col_pos)),
            0.0,
        )
    )
    counted_local = jnp.sum(counted.astype(jnp.float32))
    totals = all_sum(jnp.stack([center_err, offset_err, counted_local]), ("row", "tm"))
    center_total, offset_total, counted_total = totals[0], totals[1], totals[2]
    losses = jnp.stack(
        [
            center_total / (frame_count * height * columns),
            offset_weight * offset_total / jnp.maximum(counted_total, 1.0),
        ]
    )
    return (predictions[None], losses)


def solution(mesh):
    placed = (
        P(("grp", "tm"), None, "row", None),
        P("grp"),
        P(("grp", "tm"), "row", None),
        P(("grp", "tm"), "row", None),
        P(),
        P(),
        P(),
        P(),
        P(),
        P(),
    )
    return jax.shard_map(
        shards,
        mesh=mesh,
        in_specs=placed,
        out_specs=(P(("grp", "tm"), None, "row", None), P("grp")),
        check_vma=False,
    )
```

```python
import jax
import jax.numpy as jnp
from jax import lax
from jax.sharding import PartitionSpec as P
from jax.experimental import pallas as pl
from jax.experimental.pallas import tpu as pltpu

THING_FIRST = 11
INSTANCES = 64


DILATIONS = (6, 12, 18)
aspp_reach = 18
center_sigma = 8.0
offset_weight = 0.01


def padded_2(block, sides, width):
    for axis, dim in sides:
        count = lax.axis_size(axis)
        forward = [(i, i + 1) for i in range(count - 1)]
        backward = [(target, source) for source, target in forward]
        low = lax.ppermute(
            lax.slice_in_dim(block, block.shape[dim] - width, None, axis=dim), axis, forward
        )
        high = lax.ppermute(lax.slice_in_dim(block, 0, width, axis=dim), axis, backward)
        block = jnp.concatenate([low, block, high], axis=dim)
    return block


def shifted(value, axis, steps):
    count = lax.axis_size(axis)
    pairs = [(source, (source + steps) % count) for source in range(count)]
    return lax.ppermute(value, axis, pairs)


def all_sum(value, axes):
    for axis in axes:
        count = lax.axis_size(axis)
        if count & (count - 1):
            value = jax.tree.map(lambda v: lax.psum(v, axis), value)
            continue
        step = 1
        while step < count:
            pairs = [(i, i ^ step) for i in range(count)]
            other = lax.ppermute(value, axis, pairs)
            value = jax.tree.map(jnp.add, value, other)
            step *= 2
    return value


def aspp_projected(x, aspp_point, aspp_dilated, proj_weight, pool_term, geometry):
    front, pitch, margin, block, blocks = geometry
    width = aspp_point.shape[0]
    contract = (((1,), (1,)), ((), ()))

    def body(x_ref, point_ref, dilated_ref, proj_ref, pool_ref, out_ref):
        for index in range(blocks):
            base = front + margin * pitch + index * block

            def window(shift):
                return x_ref[pl.ds(base + shift, block), :].astype(jnp.bfloat16)

            sums = [
                lax.dot_general(
                    window(0), point_ref[...], contract, preferred_element_type=jnp.float32
                )
            ]
            for branch, spread in enumerate(DILATIONS):
                total = None
                for vertical in range(3):
                    for lateral in range(3):
                        shift = (vertical - 1) * spread * pitch + (lateral - 1) * spread
                        term = lax.dot_general(
                            window(shift),
                            dilated_ref[branch, 3 * vertical + lateral],
                            contract,
                            preferred_element_type=jnp.float32,
                        )
                        total = term if total is None else total + term
                sums.append(total)
            mixed = None
            for branch, total in enumerate(sums):
                term = lax.dot_general(
                    relu_bf16(total),
                    proj_ref[:, branch * width : (branch + 1) * width],
                    contract,
                    preferred_element_type=jnp.float32,
                )
                mixed = term if mixed is None else mixed + term
            mixed = mixed + pool_ref[...]
            out_ref[pl.ds(index * block, block), :] = relu_bf16(mixed)

    taps = 1 + 9 * len(DILATIONS)
    flops = 2 * blocks * block * x.shape[1] * width * taps + 2 * blocks * block * 4 * width * width
    return pl.pallas_call(
        body,
        out_shape=jax.ShapeDtypeStruct((blocks * block, width), jnp.bfloat16),
        compiler_params=pltpu.CompilerParams(vmem_limit_bytes=56 * 1024 * 1024),
        cost_estimate=pl.CostEstimate(
            flops=flops,
            transcendentals=0,
            bytes_accessed=x.size * 4 + aspp_dilated.size * 2 + blocks * block * width * 2,
        ),
    )(x, aspp_point, aspp_dilated, proj_weight, pool_term)


def relu_bf16(values):
    return jnp.maximum(values, 0.0).astype(jnp.bfloat16)


def emit_heads(head_out, out_weight):
    groups = head_out.reshape(3, -1, head_out.shape[1], head_out.shape[2])
    center_map = jnp.einsum(
        "c,crw->rw", out_weight[0], groups[0], preferred_element_type=jnp.float32
    )
    offset_map = jnp.einsum(
        "oc,crw->orw", out_weight[1:3], groups[1], preferred_element_type=jnp.float32
    )
    depth_map = jnp.einsum(
        "c,crw->rw", out_weight[3], groups[2], preferred_element_type=jnp.float32
    )
    return jnp.concatenate([center_map[None], offset_map, depth_map[None]], 0)


def shards(
    frames,
    clip_start,
    semantic,
    instance,
    aspp_point,
    aspp_dilated,
    pool_weight,
    proj_weight,
    head_weight,
    out_weight,
):
    own_band = frames[0]
    channel_count, band_rows, columns = own_band.shape
    frame_count = clip_start.shape[0]
    height = band_rows * lax.axis_size("row")
    time_index = lax.axis_index("tm")
    row_index = lax.axis_index("row")
    ahead = (time_index + 1) % frame_count
    at_end = lax.dynamic_index_in_dim(clip_start, ahead, 0, keepdims=False) == 1
    later_band = jnp.where(at_end, own_band, shifted(own_band, "tm", -1))
    rim_rows = min(aspp_reach, band_rows)
    extra_rows = aspp_reach - rim_rows

    def widen(band):
        wide = padded_2(band, (("row", 1),), rim_rows)
        return jnp.pad(wide, ((0, 0), (extra_rows, extra_rows), (0, 0)))

    joined_wide = jnp.concatenate([widen(own_band), widen(later_band)], 0)
    wide_rows = joined_wide.shape[1]
    pitch = columns + aspp_reach
    front = 24
    block_rows = 8 if band_rows % 8 == 0 else band_rows
    block = block_rows * pitch
    blocks = band_rows // block_rows
    length = -(-(front + wide_rows * pitch + aspp_reach) // 8) * 8
    flat = jnp.pad(
        jnp.transpose(joined_wide, (1, 2, 0)), ((0, 0), (aspp_reach, 0), (0, 0))
    ).reshape(wide_rows * pitch, 2 * channel_count)
    flat = jnp.pad(flat, ((front, length - front - wide_rows * pitch), (0, 0))).astype(
        jnp.float32
    )

    counted = (semantic[0] >= THING_FIRST) & (instance[0] > 0)
    labels = jnp.arange(INSTANCES, dtype=jnp.int32)
    onehot = ((instance[0][None] == labels[:, None, None]) & counted[None]).astype(jnp.float32)
    row_pos = (row_index * band_rows + jnp.arange(band_rows, dtype=jnp.int32)).astype(jnp.float32)[
        :, None
    ] * jnp.ones((1, columns), jnp.float32)
    col_pos = jnp.arange(columns, dtype=jnp.float32)[None, :] * jnp.ones(
        (band_rows, 1), jnp.float32
    )
    local_stats = jnp.stack(
        [
            jnp.sum(onehot, axis=(1, 2)),
            jnp.sum(onehot * row_pos, axis=(1, 2)),
            jnp.sum(onehot * col_pos, axis=(1, 2)),
        ],
        0,
    )
    channel_sums = jnp.concatenate(
        [jnp.sum(band, axis=(1, 2), dtype=jnp.float32) for band in (own_band, later_band)]
    )
    frame_totals, inst_stats = all_sum((channel_sums, local_stats), ("row",))
    pooled = (frame_totals / (height * columns)).astype(jnp.bfloat16)
    pool_feature = relu_bf16(jnp.dot(pool_weight, pooled, preferred_element_type=jnp.float32))
    aspp_width = aspp_point.shape[0]
    pool_term = jnp.dot(
        proj_weight[:, 4 * aspp_width :], pool_feature, preferred_element_type=jnp.float32
    )[None]
    projected_flat = aspp_projected(
        flat,
        aspp_point,
        aspp_dilated,
        proj_weight,
        pool_term,
        (front, pitch, aspp_reach, block, blocks),
    )
    projected = projected_flat.reshape(band_rows, pitch, aspp_width)[:, aspp_reach:]
    rimmed = padded_2(projected, (("row", 0),), 2)
    head_kernel = head_weight.reshape(5, 5, *head_weight.shape[1:])
    head_sum = lax.conv_general_dilated(
        rimmed[None],
        head_kernel,
        window_strides=(1, 1),
        padding=((0, 0), (2, 2)),
        dimension_numbers=("NHWC", "HWOI", "NCHW"),
        preferred_element_type=jnp.float32,
    )[0]
    head_out = relu_bf16(head_sum)
    predictions = emit_heads(head_out, out_weight)
    pixel = jnp.einsum("sk,khw->shw", inst_stats, onehot, precision=lax.Precision.HIGHEST)
    counts = jnp.where(counted, pixel[0], 1.0)
    centre_row = pixel[1] / counts
    centre_col = pixel[2] / counts
    distance = (row_pos - centre_row) * (row_pos - centre_row) + (col_pos - centre_col) * (
        col_pos - centre_col
    )
    heat = jnp.where(counted, jnp.exp(-distance / (2.0 * center_sigma * center_sigma)), 0.0)
    center_err = jnp.sum(jnp.square(predictions[0] - heat))
    offset_err = jnp.sum(
        jnp.where(
            counted,
            jnp.abs(predictions[1] - (centre_row - row_pos))
            + jnp.abs(predictions[2] - (centre_col - col_pos)),
            0.0,
        )
    )
    counted_local = jnp.sum(counted.astype(jnp.float32))
    totals = all_sum(jnp.stack([center_err, offset_err, counted_local]), ("row", "tm"))
    center_total, offset_total, counted_total = totals[0], totals[1], totals[2]
    losses = jnp.stack(
        [
            center_total / (frame_count * height * columns),
            offset_weight * offset_total / jnp.maximum(counted_total, 1.0),
        ]
    )
    return (predictions[None], losses)


def solution(mesh):
    placed = (
        P(("grp", "tm"), None, "row", None),
        P("grp"),
        P(("grp", "tm"), "row", None),
        P(("grp", "tm"), "row", None),
        P(),
        P(),
        P(),
        P(),
        P(),
        P(),
    )
    return jax.shard_map(
        shards,
        mesh=mesh,
        in_specs=placed,
        out_specs=(P(("grp", "tm"), None, "row", None), P("grp")),
        check_vma=False,
    )
```

```python
import jax
import jax.numpy as jnp
from jax import lax
from jax.sharding import PartitionSpec as P
from jax.experimental import pallas as pl
from jax.experimental.pallas import tpu as pltpu

THING_FIRST = 11
INSTANCES = 64


DILATIONS = (6, 12, 18)
aspp_reach = 18
center_sigma = 8.0
offset_weight = 0.01


def padded_2(block, sides, width):
    for axis, dim in sides:
        count = lax.axis_size(axis)
        forward = [(i, i + 1) for i in range(count - 1)]
        backward = [(target, source) for source, target in forward]
        low = lax.ppermute(
            lax.slice_in_dim(block, block.shape[dim] - width, None, axis=dim), axis, forward
        )
        high = lax.ppermute(lax.slice_in_dim(block, 0, width, axis=dim), axis, backward)
        block = jnp.concatenate([low, block, high], axis=dim)
    return block


def shifted(value, axis, steps):
    count = lax.axis_size(axis)
    pairs = [(source, (source + steps) % count) for source in range(count)]
    return lax.ppermute(value, axis, pairs)


def all_sum(value, axes):
    for axis in axes:
        count = lax.axis_size(axis)
        if count & (count - 1):
            value = jax.tree.map(lambda v: lax.psum(v, axis), value)
            continue
        step = 1
        while step < count:
            pairs = [(i, i ^ step) for i in range(count)]
            other = lax.ppermute(value, axis, pairs)
            value = jax.tree.map(jnp.add, value, other)
            step *= 2
    return value


def aspp_projected(x, aspp_point, aspp_dilated, proj_weight, pool_term, geometry):
    front, pitch, margin, block, blocks = geometry
    width = aspp_point.shape[0]
    contract = (((1,), (1,)), ((), ()))

    def body(x_ref, point_ref, dilated_ref, proj_ref, pool_ref, out_ref):
        for index in range(blocks):
            base = front + margin * pitch + index * block

            def window(shift):
                return x_ref[pl.ds(base + shift, block), :].astype(jnp.bfloat16)

            sums = [
                lax.dot_general(
                    window(0), point_ref[...], contract, preferred_element_type=jnp.float32
                )
            ]
            for branch, spread in enumerate(DILATIONS):
                total = None
                for vertical in range(3):
                    for lateral in range(3):
                        shift = (vertical - 1) * spread * pitch + (lateral - 1) * spread
                        term = lax.dot_general(
                            window(shift),
                            dilated_ref[branch, 3 * vertical + lateral],
                            contract,
                            preferred_element_type=jnp.float32,
                        )
                        total = term if total is None else total + term
                sums.append(total)
            mixed = None
            for branch, total in enumerate(sums):
                term = lax.dot_general(
                    relu_bf16(total),
                    proj_ref[:, branch * width : (branch + 1) * width],
                    contract,
                    preferred_element_type=jnp.float32,
                )
                mixed = term if mixed is None else mixed + term
            mixed = mixed + pool_ref[...]
            out_ref[pl.ds(index * block, block), :] = relu_bf16(mixed)

    taps = 1 + 9 * len(DILATIONS)
    flops = 2 * blocks * block * x.shape[1] * width * taps + 2 * blocks * block * 4 * width * width
    return pl.pallas_call(
        body,
        out_shape=jax.ShapeDtypeStruct((blocks * block, width), jnp.bfloat16),
        compiler_params=pltpu.CompilerParams(vmem_limit_bytes=56 * 1024 * 1024),
        cost_estimate=pl.CostEstimate(
            flops=flops,
            transcendentals=0,
            bytes_accessed=x.size * 4 + aspp_dilated.size * 2 + blocks * block * width * 2,
        ),
    )(x, aspp_point, aspp_dilated, proj_weight, pool_term)


def relu_bf16(values):
    return jnp.maximum(values, 0.0).astype(jnp.bfloat16)


def emit_heads(head_out, out_weight):
    groups = head_out.reshape(3, -1, head_out.shape[1], head_out.shape[2])
    center_map = jnp.einsum(
        "c,crw->rw", out_weight[0], groups[0], preferred_element_type=jnp.float32
    )
    offset_map = jnp.einsum(
        "oc,crw->orw", out_weight[1:3], groups[1], preferred_element_type=jnp.float32
    )
    depth_map = jnp.einsum(
        "c,crw->rw", out_weight[3], groups[2], preferred_element_type=jnp.float32
    )
    return jnp.concatenate([center_map[None], offset_map, depth_map[None]], 0)


def shards(
    frames,
    clip_start,
    semantic,
    instance,
    aspp_point,
    aspp_dilated,
    pool_weight,
    proj_weight,
    head_weight,
    out_weight,
):
    own_band = frames[0]
    channel_count, band_rows, columns = own_band.shape
    frame_count = clip_start.shape[0]
    height = band_rows * lax.axis_size("row")
    time_index = lax.axis_index("tm")
    row_index = lax.axis_index("row")
    ahead = (time_index + 1) % frame_count
    at_end = lax.dynamic_index_in_dim(clip_start, ahead, 0, keepdims=False) == 1
    later_band = jnp.where(at_end, own_band, shifted(own_band, "tm", -1))
    rim_rows = min(aspp_reach, band_rows)
    extra_rows = aspp_reach - rim_rows

    def widen(band):
        wide = padded_2(band, (("row", 1),), rim_rows)
        return jnp.pad(wide, ((0, 0), (extra_rows, extra_rows), (0, 0)))

    joined_wide = jnp.concatenate([widen(own_band), widen(later_band)], 0)
    wide_rows = joined_wide.shape[1]
    pitch = -(-(columns + aspp_reach) // 8) * 8
    front = pitch
    block_rows = 8 if band_rows % 8 == 0 else band_rows
    block = block_rows * pitch
    blocks = band_rows // block_rows
    flat = jnp.pad(
        jnp.transpose(joined_wide, (1, 2, 0)).astype(jnp.float32),
        ((1, 1), (pitch - columns, 0), (0, 0)),
    ).reshape((wide_rows + 2) * pitch, 2 * channel_count)

    counted = (semantic[0] >= THING_FIRST) & (instance[0] > 0)
    labels = jnp.arange(INSTANCES, dtype=jnp.int32)
    onehot = ((instance[0][None] == labels[:, None, None]) & counted[None]).astype(jnp.float32)
    row_pos = (row_index * band_rows + jnp.arange(band_rows, dtype=jnp.int32)).astype(jnp.float32)[
        :, None
    ] * jnp.ones((1, columns), jnp.float32)
    col_pos = jnp.arange(columns, dtype=jnp.float32)[None, :] * jnp.ones(
        (band_rows, 1), jnp.float32
    )
    local_stats = jnp.stack(
        [
            jnp.sum(onehot, axis=(1, 2)),
            jnp.sum(onehot * row_pos, axis=(1, 2)),
            jnp.sum(onehot * col_pos, axis=(1, 2)),
        ],
        0,
    )
    channel_sums = jnp.concatenate(
        [jnp.sum(band, axis=(1, 2), dtype=jnp.float32) for band in (own_band, later_band)]
    )
    frame_totals, inst_stats = all_sum((channel_sums, local_stats), ("row",))
    pooled = (frame_totals / (height * columns)).astype(jnp.bfloat16)
    pool_feature = relu_bf16(jnp.dot(pool_weight, pooled, preferred_element_type=jnp.float32))
    aspp_width = aspp_point.shape[0]
    pool_term = jnp.dot(
        proj_weight[:, 4 * aspp_width :], pool_feature, preferred_element_type=jnp.float32
    )[None]
    projected_flat = aspp_projected(
        flat,
        aspp_point,
        aspp_dilated,
        proj_weight,
        pool_term,
        (front, pitch, aspp_reach, block, blocks),
    )
    projected = projected_flat.reshape(band_rows, pitch, aspp_width)[:, pitch - columns :]
    rimmed = padded_2(projected, (("row", 0),), 2)
    head_kernel = head_weight.reshape(5, 5, *head_weight.shape[1:])
    head_sum = lax.conv_general_dilated(
        rimmed[None],
        head_kernel,
        window_strides=(1, 1),
        padding=((0, 0), (2, 2)),
        dimension_numbers=("NHWC", "HWOI", "NCHW"),
        preferred_element_type=jnp.float32,
    )[0]
    head_out = relu_bf16(head_sum)
    predictions = emit_heads(head_out, out_weight)
    pixel = jnp.einsum("sk,khw->shw", inst_stats, onehot, precision=lax.Precision.HIGHEST)
    counts = jnp.where(counted, pixel[0], 1.0)
    centre_row = pixel[1] / counts
    centre_col = pixel[2] / counts
    distance = (row_pos - centre_row) * (row_pos - centre_row) + (col_pos - centre_col) * (
        col_pos - centre_col
    )
    heat = jnp.where(counted, jnp.exp(-distance / (2.0 * center_sigma * center_sigma)), 0.0)
    center_err = jnp.sum(jnp.square(predictions[0] - heat))
    offset_err = jnp.sum(
        jnp.where(
            counted,
            jnp.abs(predictions[1] - (centre_row - row_pos))
            + jnp.abs(predictions[2] - (centre_col - col_pos)),
            0.0,
        )
    )
    counted_local = jnp.sum(counted.astype(jnp.float32))
    local_totals = lax.optimization_barrier(jnp.stack([center_err, offset_err, counted_local]))
    totals = all_sum(local_totals, ("row", "tm"))
    center_total, offset_total, counted_total = totals[0], totals[1], totals[2]
    losses = jnp.stack(
        [
            center_total / (frame_count * height * columns),
            offset_weight * offset_total / jnp.maximum(counted_total, 1.0),
        ]
    )
    return (predictions[None], losses)


def solution(mesh):
    placed = (
        P(("grp", "tm"), None, "row", None),
        P("grp"),
        P(("grp", "tm"), "row", None),
        P(("grp", "tm"), "row", None),
        P(),
        P(),
        P(),
        P(),
        P(),
        P(),
    )
    return jax.shard_map(
        shards,
        mesh=mesh,
        in_specs=placed,
        out_specs=(P(("grp", "tm"), None, "row", None), P("grp")),
        check_vma=False,
    )
```

```python
import jax
import jax.numpy as jnp
from jax import lax
from jax.sharding import PartitionSpec as P
from jax.experimental import pallas as pl
from jax.experimental.pallas import tpu as pltpu

THING_FIRST = 11
INSTANCES = 64


DILATIONS = (6, 12, 18)
aspp_reach = 18
center_sigma = 8.0
offset_weight = 0.01


def padded_2(block, sides, width):
    for axis, dim in sides:
        count = lax.axis_size(axis)
        forward = [(i, i + 1) for i in range(count - 1)]
        backward = [(target, source) for source, target in forward]
        low = lax.ppermute(
            lax.slice_in_dim(block, block.shape[dim] - width, None, axis=dim), axis, forward
        )
        high = lax.ppermute(lax.slice_in_dim(block, 0, width, axis=dim), axis, backward)
        block = jnp.concatenate([low, block, high], axis=dim)
    return block


def with_rims(block, axis, dim, width):
    if lax.axis_size(axis) != 2:
        return padded_2(block, ((axis, dim),), width)
    first = lax.axis_index(axis) == 0
    size = block.shape[dim]
    sent = jnp.where(
        first,
        lax.slice_in_dim(block, size - width, None, axis=dim),
        lax.slice_in_dim(block, 0, width, axis=dim),
    )
    got = lax.ppermute(sent, axis, [(0, 1), (1, 0)])
    empty = jnp.zeros_like(got)
    low = jnp.where(first, empty, got)
    high = jnp.where(first, got, empty)
    return jnp.concatenate([low, block, high], axis=dim)


def shifted(value, axis, steps):
    count = lax.axis_size(axis)
    pairs = [(source, (source + steps) % count) for source in range(count)]
    return lax.ppermute(value, axis, pairs)


def all_sum(value, axes):
    for axis in axes:
        count = lax.axis_size(axis)
        if count & (count - 1):
            value = jax.tree.map(lambda v: lax.psum(v, axis), value)
            continue
        step = 1
        while step < count:
            pairs = [(i, i ^ step) for i in range(count)]
            other = lax.ppermute(value, axis, pairs)
            value = jax.tree.map(jnp.add, value, other)
            step *= 2
    return value


def aspp_projected(x, aspp_point, aspp_dilated, proj_weight, pool_term, keep, geometry):
    front, pitch, margin, block, blocks = geometry
    width = aspp_point.shape[0]
    contract = (((1,), (1,)), ((), ()))

    def body(x_ref, point_ref, dilated_ref, proj_ref, pool_ref, keep_ref, out_ref):
        for index in range(blocks):
            base = front + margin * pitch + index * block

            def window(shift):
                return x_ref[pl.ds(base + shift, block), :].astype(jnp.bfloat16)

            sums = [
                lax.dot_general(
                    window(0), point_ref[...], contract, preferred_element_type=jnp.float32
                )
            ]
            for branch, spread in enumerate(DILATIONS):
                total = None
                for vertical in range(3):
                    for lateral in range(3):
                        shift = (vertical - 1) * spread * pitch + (lateral - 1) * spread
                        term = lax.dot_general(
                            window(shift),
                            dilated_ref[branch, 3 * vertical + lateral],
                            contract,
                            preferred_element_type=jnp.float32,
                        )
                        total = term if total is None else total + term
                sums.append(total)
            mixed = None
            for branch, total in enumerate(sums):
                term = lax.dot_general(
                    relu_bf16(total),
                    proj_ref[:, branch * width : (branch + 1) * width],
                    contract,
                    preferred_element_type=jnp.float32,
                )
                mixed = term if mixed is None else mixed + term
            mixed = mixed + pool_ref[...]
            rounded = relu_bf16(mixed).astype(jnp.float32)
            out_ref[pl.ds(index * block, block), :] = jnp.where(keep_ref[...] > 0.5, rounded, 0.0)

    taps = 1 + 9 * len(DILATIONS)
    flops = 2 * blocks * block * x.shape[1] * width * taps + 2 * blocks * block * 4 * width * width
    return pl.pallas_call(
        body,
        out_shape=jax.ShapeDtypeStruct((blocks * block, width), jnp.float32),
        compiler_params=pltpu.CompilerParams(vmem_limit_bytes=56 * 1024 * 1024),
        cost_estimate=pl.CostEstimate(
            flops=flops,
            transcendentals=0,
            bytes_accessed=x.size * 4 + aspp_dilated.size * 2 + blocks * block * width * 2,
        ),
    )(x, aspp_point, aspp_dilated, proj_weight, pool_term, keep)


def head_kernel_call(x, head_weight, geometry):
    front, pitch, reach, block, blocks = geometry
    outputs = head_weight.shape[1]
    side = 2 * reach + 1
    contract = (((1,), (1,)), ((), ()))

    def body(x_ref, weight_ref, out_ref):
        for index in range(blocks):
            base = front + reach * pitch + index * block
            total = None
            for vertical in range(side):
                for lateral in range(side):
                    shift = (vertical - reach) * pitch + (lateral - reach)
                    term = lax.dot_general(
                        x_ref[pl.ds(base + shift, block), :].astype(jnp.bfloat16),
                        weight_ref[side * vertical + lateral],
                        contract,
                        preferred_element_type=jnp.float32,
                    )
                    total = term if total is None else total + term
            out_ref[pl.ds(index * block, block), :] = relu_bf16(total)

    return pl.pallas_call(
        body,
        out_shape=jax.ShapeDtypeStruct((blocks * block, outputs), jnp.bfloat16),
        compiler_params=pltpu.CompilerParams(vmem_limit_bytes=32 * 1024 * 1024),
        cost_estimate=pl.CostEstimate(
            flops=2 * blocks * block * x.shape[1] * outputs * side * side,
            transcendentals=0,
            bytes_accessed=x.size * 4 + head_weight.size * 2 + blocks * block * outputs * 2,
        ),
    )(x, head_weight)


def relu_bf16(values):
    return jnp.maximum(values, 0.0).astype(jnp.bfloat16)


def emit_heads(head_out, out_weight):
    groups = head_out.reshape(3, -1, head_out.shape[1], head_out.shape[2])
    center_map = jnp.einsum(
        "c,crw->rw", out_weight[0], groups[0], preferred_element_type=jnp.float32
    )
    offset_map = jnp.einsum(
        "oc,crw->orw", out_weight[1:3], groups[1], preferred_element_type=jnp.float32
    )
    depth_map = jnp.einsum(
        "c,crw->rw", out_weight[3], groups[2], preferred_element_type=jnp.float32
    )
    return jnp.concatenate([center_map[None], offset_map, depth_map[None]], 0)


def shards(
    frames,
    clip_start,
    semantic,
    instance,
    aspp_point,
    aspp_dilated,
    pool_weight,
    proj_weight,
    head_weight,
    out_weight,
):
    own_band = frames[0]
    channel_count, band_rows, columns = own_band.shape
    frame_count = clip_start.shape[0]
    height = band_rows * lax.axis_size("row")
    time_index = lax.axis_index("tm")
    row_index = lax.axis_index("row")
    ahead = (time_index + 1) % frame_count
    at_end = lax.dynamic_index_in_dim(clip_start, ahead, 0, keepdims=False) == 1
    later_band = jnp.where(at_end, own_band, shifted(own_band, "tm", -1))
    rim_rows = min(aspp_reach, band_rows)
    extra_rows = aspp_reach - rim_rows

    joined_wide = jnp.pad(
        with_rims(jnp.concatenate([own_band, later_band], 0), "row", 1, rim_rows),
        ((0, 0), (extra_rows, extra_rows), (0, 0)),
    )
    wide_rows = joined_wide.shape[1]
    pitch = -(-(columns + aspp_reach) // 8) * 8
    front = pitch
    block_rows = 8 if band_rows % 8 == 0 else band_rows
    block = block_rows * pitch
    blocks = band_rows // block_rows
    flat = jnp.pad(
        jnp.transpose(joined_wide, (1, 2, 0)).astype(jnp.float32),
        ((1, 1), (pitch - columns, 0), (0, 0)),
    ).reshape((wide_rows + 2) * pitch, 2 * channel_count)

    counted = (semantic[0] >= THING_FIRST) & (instance[0] > 0)
    labels = jnp.arange(INSTANCES, dtype=jnp.int32)
    onehot = ((instance[0][None] == labels[:, None, None]) & counted[None]).astype(jnp.float32)
    row_pos = (row_index * band_rows + jnp.arange(band_rows, dtype=jnp.int32)).astype(jnp.float32)[
        :, None
    ] * jnp.ones((1, columns), jnp.float32)
    col_pos = jnp.arange(columns, dtype=jnp.float32)[None, :] * jnp.ones(
        (band_rows, 1), jnp.float32
    )
    local_stats = jnp.stack(
        [
            jnp.sum(onehot, axis=(1, 2)),
            jnp.sum(onehot * row_pos, axis=(1, 2)),
            jnp.sum(onehot * col_pos, axis=(1, 2)),
        ],
        0,
    )
    channel_sums = jnp.concatenate(
        [jnp.sum(band, axis=(1, 2), dtype=jnp.float32) for band in (own_band, later_band)]
    )
    frame_totals, inst_stats = all_sum((channel_sums, local_stats), ("row",))
    pooled = (frame_totals / (height * columns)).astype(jnp.bfloat16)
    pool_feature = relu_bf16(jnp.dot(pool_weight, pooled, preferred_element_type=jnp.float32))
    aspp_width = aspp_point.shape[0]
    pool_term = jnp.dot(
        proj_weight[:, 4 * aspp_width :], pool_feature, preferred_element_type=jnp.float32
    )[None]
    pad_columns = pitch - columns
    keep = (jnp.arange(block) % pitch >= pad_columns).astype(jnp.float32)[:, None]
    projected_flat = aspp_projected(
        flat,
        aspp_point,
        aspp_dilated,
        proj_weight,
        pool_term,
        keep,
        (front, pitch, aspp_reach, block, blocks),
    )
    head_reach = 2
    head_in = jnp.pad(
        with_rims(projected_flat, "row", 0, head_reach * pitch), ((pitch, pitch), (0, 0))
    )
    head_flat = head_kernel_call(head_in, head_weight, (pitch, pitch, head_reach, block, blocks))
    head_out = jnp.transpose(
        head_flat.reshape(band_rows, pitch, head_weight.shape[1])[:, pad_columns:], (2, 0, 1)
    )
    predictions = emit_heads(head_out, out_weight)
    pixel = jnp.einsum("sk,khw->shw", inst_stats, onehot, precision=lax.Precision.HIGHEST)
    counts = jnp.where(counted, pixel[0], 1.0)
    centre_row = pixel[1] / counts
    centre_col = pixel[2] / counts
    distance = (row_pos - centre_row) * (row_pos - centre_row) + (col_pos - centre_col) * (
        col_pos - centre_col
    )
    heat = jnp.where(counted, jnp.exp(-distance / (2.0 * center_sigma * center_sigma)), 0.0)
    center_err = jnp.sum(jnp.square(predictions[0] - heat))
    offset_err = jnp.sum(
        jnp.where(
            counted,
            jnp.abs(predictions[1] - (centre_row - row_pos))
            + jnp.abs(predictions[2] - (centre_col - col_pos)),
            0.0,
        )
    )
    counted_local = jnp.sum(counted.astype(jnp.float32))
    local_totals = lax.optimization_barrier(jnp.stack([center_err, offset_err, counted_local]))
    totals = all_sum(local_totals, ("row", "tm"))
    center_total, offset_total, counted_total = totals[0], totals[1], totals[2]
    losses = jnp.stack(
        [
            center_total / (frame_count * height * columns),
            offset_weight * offset_total / jnp.maximum(counted_total, 1.0),
        ]
    )
    return (predictions[None], losses)


def solution(mesh):
    placed = (
        P(("grp", "tm"), None, "row", None),
        P("grp"),
        P(("grp", "tm"), "row", None),
        P(("grp", "tm"), "row", None),
        P(),
        P(),
        P(),
        P(),
        P(),
        P(),
    )
    return jax.shard_map(
        shards,
        mesh=mesh,
        in_specs=placed,
        out_specs=(P(("grp", "tm"), None, "row", None), P("grp")),
        check_vma=False,
    )
```

```python
import jax
import jax.numpy as jnp
from jax import lax
from jax.sharding import PartitionSpec as P
from jax.experimental import pallas as pl
from jax.experimental.pallas import tpu as pltpu

THING_FIRST = 11
INSTANCES = 64


DILATIONS = (6, 12, 18)
aspp_reach = 18
center_sigma = 8.0
offset_weight = 0.01


def padded_2(block, sides, width):
    for axis, dim in sides:
        count = lax.axis_size(axis)
        forward = [(i, i + 1) for i in range(count - 1)]
        backward = [(target, source) for source, target in forward]
        low = lax.ppermute(
            lax.slice_in_dim(block, block.shape[dim] - width, None, axis=dim), axis, forward
        )
        high = lax.ppermute(lax.slice_in_dim(block, 0, width, axis=dim), axis, backward)
        block = jnp.concatenate([low, block, high], axis=dim)
    return block


def with_rims(block, axis, dim, width):
    if lax.axis_size(axis) != 2:
        return padded_2(block, ((axis, dim),), width)
    first = lax.axis_index(axis) == 0
    size = block.shape[dim]
    sent = jnp.where(
        first,
        lax.slice_in_dim(block, size - width, None, axis=dim),
        lax.slice_in_dim(block, 0, width, axis=dim),
    )
    got = lax.ppermute(sent, axis, [(0, 1), (1, 0)])
    empty = jnp.zeros_like(got)
    low = jnp.where(first, empty, got)
    high = jnp.where(first, got, empty)
    return jnp.concatenate([low, block, high], axis=dim)


def shifted(value, axis, steps):
    count = lax.axis_size(axis)
    pairs = [(source, (source + steps) % count) for source in range(count)]
    return lax.ppermute(value, axis, pairs)


def all_sum(value, axes):
    for axis in axes:
        count = lax.axis_size(axis)
        if count & (count - 1):
            value = jax.tree.map(lambda v: lax.psum(v, axis), value)
            continue
        step = 1
        while step < count:
            pairs = [(i, i ^ step) for i in range(count)]
            other = lax.ppermute(value, axis, pairs)
            value = jax.tree.map(jnp.add, value, other)
            step *= 2
    return value


def aspp_pass(x, aspp_point, aspp_dilated, extra, geometry, part, finish):
    front, pitch, margin, block, blocks = geometry
    width = aspp_point.shape[0]
    channels = x.shape[1]
    lanes = pl.ds(part * channels, channels)
    contract = (((1,), (1,)), ((), ()))
    branches = 1 + len(DILATIONS)

    def body(x_ref, point_ref, dilated_ref, *rest):
        if finish:
            earlier_ref, proj_ref, pool_ref, keep_ref, out_ref = rest
        else:
            (out_ref,) = rest
        for index in range(blocks):
            base = front + margin * pitch + index * block
            rows = pl.ds(index * block, block)

            def window(shift):
                return x_ref[pl.ds(base + shift, block), :].astype(jnp.bfloat16)

            sums = [
                lax.dot_general(
                    window(0), point_ref[:, lanes], contract, preferred_element_type=jnp.float32
                )
            ]
            for branch, spread in enumerate(DILATIONS):
                total = None
                for vertical in range(3):
                    for lateral in range(3):
                        shift = (vertical - 1) * spread * pitch + (lateral - 1) * spread
                        term = lax.dot_general(
                            window(shift),
                            dilated_ref[branch, 3 * vertical + lateral, :, lanes],
                            contract,
                            preferred_element_type=jnp.float32,
                        )
                        total = term if total is None else total + term
                sums.append(total)
            if not finish:
                for branch, total in enumerate(sums):
                    out_ref[branch, rows, :] = total
                continue
            mixed = None
            for branch, total in enumerate(sums):
                term = lax.dot_general(
                    relu_bf16(earlier_ref[branch, rows, :] + total),
                    proj_ref[:, branch * width : (branch + 1) * width],
                    contract,
                    preferred_element_type=jnp.float32,
                )
                mixed = term if mixed is None else mixed + term
            mixed = mixed + pool_ref[...]
            rounded = relu_bf16(mixed).astype(jnp.float32)
            out_ref[rows, :] = jnp.where(keep_ref[...] > 0.5, rounded, 0.0)

    taps = 1 + 9 * len(DILATIONS)
    flops = 2 * blocks * block * channels * width * taps
    if finish:
        flops += 2 * blocks * block * branches * width * width
        out_shape = jax.ShapeDtypeStruct((blocks * block, width), jnp.float32)
    else:
        out_shape = jax.ShapeDtypeStruct((branches, blocks * block, width), jnp.float32)
    return pl.pallas_call(
        body,
        out_shape=out_shape,
        compiler_params=pltpu.CompilerParams(vmem_limit_bytes=56 * 1024 * 1024),
        cost_estimate=pl.CostEstimate(
            flops=flops,
            transcendentals=0,
            bytes_accessed=x.size * 4
            + aspp_dilated.size
            + branches * blocks * block * width * 4,
        ),
    )(x, aspp_point, aspp_dilated, *extra)


def head_kernel_call(x, head_weight, geometry):
    front, pitch, reach, block, blocks = geometry
    outputs = head_weight.shape[1]
    side = 2 * reach + 1
    contract = (((1,), (1,)), ((), ()))

    def body(x_ref, weight_ref, out_ref):
        for index in range(blocks):
            base = front + reach * pitch + index * block
            total = None
            for vertical in range(side):
                for lateral in range(side):
                    shift = (vertical - reach) * pitch + (lateral - reach)
                    term = lax.dot_general(
                        x_ref[pl.ds(base + shift, block), :].astype(jnp.bfloat16),
                        weight_ref[side * vertical + lateral],
                        contract,
                        preferred_element_type=jnp.float32,
                    )
                    total = term if total is None else total + term
            out_ref[pl.ds(index * block, block), :] = relu_bf16(total)

    return pl.pallas_call(
        body,
        out_shape=jax.ShapeDtypeStruct((blocks * block, outputs), jnp.bfloat16),
        compiler_params=pltpu.CompilerParams(vmem_limit_bytes=32 * 1024 * 1024),
        cost_estimate=pl.CostEstimate(
            flops=2 * blocks * block * x.shape[1] * outputs * side * side,
            transcendentals=0,
            bytes_accessed=x.size * 4 + head_weight.size * 2 + blocks * block * outputs * 2,
        ),
    )(x, head_weight)


def relu_bf16(values):
    return jnp.maximum(values, 0.0).astype(jnp.bfloat16)


def emit_heads(head_out, out_weight):
    groups = head_out.reshape(3, -1, head_out.shape[1], head_out.shape[2])
    center_map = jnp.einsum(
        "c,crw->rw", out_weight[0], groups[0], preferred_element_type=jnp.float32
    )
    offset_map = jnp.einsum(
        "oc,crw->orw", out_weight[1:3], groups[1], preferred_element_type=jnp.float32
    )
    depth_map = jnp.einsum(
        "c,crw->rw", out_weight[3], groups[2], preferred_element_type=jnp.float32
    )
    return jnp.concatenate([center_map[None], offset_map, depth_map[None]], 0)


def shards(
    frames,
    clip_start,
    semantic,
    instance,
    aspp_point,
    aspp_dilated,
    pool_weight,
    proj_weight,
    head_weight,
    out_weight,
):
    own_band = frames[0]
    channel_count, band_rows, columns = own_band.shape
    frame_count = clip_start.shape[0]
    height = band_rows * lax.axis_size("row")
    time_index = lax.axis_index("tm")
    row_index = lax.axis_index("row")
    ahead = (time_index + 1) % frame_count
    at_end = lax.dynamic_index_in_dim(clip_start, ahead, 0, keepdims=False) == 1
    later_band = jnp.where(at_end, own_band, shifted(own_band, "tm", -1))
    rim_rows = min(aspp_reach, band_rows)
    extra_rows = aspp_reach - rim_rows

    wide_rows = band_rows + 2 * aspp_reach
    pitch = -(-(columns + aspp_reach) // 8) * 8
    front = pitch
    block_rows = 8 if band_rows % 8 == 0 else band_rows
    block = block_rows * pitch
    blocks = band_rows // block_rows

    def flat_of(band):
        wide = jnp.pad(
            with_rims(band, "row", 1, rim_rows), ((0, 0), (extra_rows, extra_rows), (0, 0))
        )
        return jnp.pad(
            jnp.transpose(wide, (1, 2, 0)).astype(jnp.float32),
            ((1, 1), (pitch - columns, 0), (0, 0)),
        ).reshape((wide_rows + 2) * pitch, channel_count)

    geometry = (front, pitch, aspp_reach, block, blocks)
    own_sums = aspp_pass(
        flat_of(own_band), aspp_point, aspp_dilated, (), geometry, 0, False
    )

    counted = (semantic[0] >= THING_FIRST) & (instance[0] > 0)
    labels = jnp.arange(INSTANCES, dtype=jnp.int32)
    onehot = ((instance[0][None] == labels[:, None, None]) & counted[None]).astype(jnp.float32)
    row_pos = (row_index * band_rows + jnp.arange(band_rows, dtype=jnp.int32)).astype(jnp.float32)[
        :, None
    ] * jnp.ones((1, columns), jnp.float32)
    col_pos = jnp.arange(columns, dtype=jnp.float32)[None, :] * jnp.ones(
        (band_rows, 1), jnp.float32
    )
    local_stats = jnp.stack(
        [
            jnp.sum(onehot, axis=(1, 2)),
            jnp.sum(onehot * row_pos, axis=(1, 2)),
            jnp.sum(onehot * col_pos, axis=(1, 2)),
        ],
        0,
    )
    channel_sums = jnp.concatenate(
        [jnp.sum(band, axis=(1, 2), dtype=jnp.float32) for band in (own_band, later_band)]
    )
    frame_totals, inst_stats = all_sum((channel_sums, local_stats), ("row",))
    pooled = (frame_totals / (height * columns)).astype(jnp.bfloat16)
    pool_feature = relu_bf16(jnp.dot(pool_weight, pooled, preferred_element_type=jnp.float32))
    aspp_width = aspp_point.shape[0]
    pool_term = jnp.dot(
        proj_weight[:, 4 * aspp_width :], pool_feature, preferred_element_type=jnp.float32
    )[None]
    pad_columns = pitch - columns
    keep = (jnp.arange(block) % pitch >= pad_columns).astype(jnp.float32)[:, None]
    projected_flat = aspp_pass(
        flat_of(later_band),
        aspp_point,
        aspp_dilated,
        (own_sums, proj_weight, pool_term, keep),
        geometry,
        1,
        True,
    )
    head_reach = 2
    head_in = jnp.pad(
        with_rims(projected_flat, "row", 0, head_reach * pitch), ((pitch, pitch), (0, 0))
    )
    head_flat = head_kernel_call(head_in, head_weight, (pitch, pitch, head_reach, block, blocks))
    head_out = jnp.transpose(
        head_flat.reshape(band_rows, pitch, head_weight.shape[1])[:, pad_columns:], (2, 0, 1)
    )
    predictions = emit_heads(head_out, out_weight)
    pixel = jnp.einsum("sk,khw->shw", inst_stats, onehot, precision=lax.Precision.HIGHEST)
    counts = jnp.where(counted, pixel[0], 1.0)
    centre_row = pixel[1] / counts
    centre_col = pixel[2] / counts
    distance = (row_pos - centre_row) * (row_pos - centre_row) + (col_pos - centre_col) * (
        col_pos - centre_col
    )
    heat = jnp.where(counted, jnp.exp(-distance / (2.0 * center_sigma * center_sigma)), 0.0)
    center_err = jnp.sum(jnp.square(predictions[0] - heat))
    offset_err = jnp.sum(
        jnp.where(
            counted,
            jnp.abs(predictions[1] - (centre_row - row_pos))
            + jnp.abs(predictions[2] - (centre_col - col_pos)),
            0.0,
        )
    )
    counted_local = jnp.sum(counted.astype(jnp.float32))
    local_totals = lax.optimization_barrier(jnp.stack([center_err, offset_err, counted_local]))
    totals = all_sum(local_totals, ("row", "tm"))
    center_total, offset_total, counted_total = totals[0], totals[1], totals[2]
    losses = jnp.stack(
        [
            center_total / (frame_count * height * columns),
            offset_weight * offset_total / jnp.maximum(counted_total, 1.0),
        ]
    )
    return (predictions[None], losses)


def solution(mesh):
    placed = (
        P(("grp", "tm"), None, "row", None),
        P("grp"),
        P(("grp", "tm"), "row", None),
        P(("grp", "tm"), "row", None),
        P(),
        P(),
        P(),
        P(),
        P(),
        P(),
    )
    return jax.shard_map(
        shards,
        mesh=mesh,
        in_specs=placed,
        out_specs=(P(("grp", "tm"), None, "row", None), P("grp")),
        check_vma=False,
    )
```

```python
import jax
import jax.numpy as jnp
from jax import lax
from jax.sharding import PartitionSpec as P
from jax.experimental import pallas as pl
from jax.experimental.pallas import tpu as pltpu

THING_FIRST = 11
INSTANCES = 64


DILATIONS = (6, 12, 18)
aspp_reach = 18
center_sigma = 8.0
offset_weight = 0.01


def padded_2(block, sides, width):
    for axis, dim in sides:
        count = lax.axis_size(axis)
        forward = [(i, i + 1) for i in range(count - 1)]
        backward = [(target, source) for source, target in forward]
        low = lax.ppermute(
            lax.slice_in_dim(block, block.shape[dim] - width, None, axis=dim), axis, forward
        )
        high = lax.ppermute(lax.slice_in_dim(block, 0, width, axis=dim), axis, backward)
        block = jnp.concatenate([low, block, high], axis=dim)
    return block


def with_rims(block, axis, dim, width):
    if lax.axis_size(axis) != 2:
        return padded_2(block, ((axis, dim),), width)
    first = lax.axis_index(axis) == 0
    size = block.shape[dim]
    sent = jnp.where(
        first,
        lax.slice_in_dim(block, size - width, None, axis=dim),
        lax.slice_in_dim(block, 0, width, axis=dim),
    )
    got = lax.ppermute(sent, axis, [(0, 1), (1, 0)])
    empty = jnp.zeros_like(got)
    low = jnp.where(first, empty, got)
    high = jnp.where(first, got, empty)
    return jnp.concatenate([low, block, high], axis=dim)


def shifted(value, axis, steps):
    count = lax.axis_size(axis)
    pairs = [(source, (source + steps) % count) for source in range(count)]
    return lax.ppermute(value, axis, pairs)


def all_sum(value, axes):
    for axis in axes:
        count = lax.axis_size(axis)
        if count & (count - 1):
            value = jax.tree.map(lambda v: lax.psum(v, axis), value)
            continue
        if 2 < count <= 8 and not isinstance(value, tuple):
            index = lax.axis_index(axis)
            copies = [value] + [
                lax.ppermute(value, axis, [(i, (i + k) % count) for i in range(count)])
                for k in range(1, count)
            ]
            stacked = jnp.stack(copies)
            ordered = jnp.take(stacked, (index - jnp.arange(count)) % count, axis=0)
            value = ordered[0]
            for source in range(1, count):
                value = value + ordered[source]
            continue
        step = 1
        while step < count:
            pairs = [(i, i ^ step) for i in range(count)]
            other = lax.ppermute(value, axis, pairs)
            value = jax.tree.map(jnp.add, value, other)
            step *= 2
    return value


def aspp_pass(x, aspp_point, aspp_dilated, extra, geometry, part, finish):
    front, pitch, margin, block, blocks = geometry
    width = aspp_point.shape[0]
    channels = x.shape[1]
    lanes = pl.ds(part * channels, channels)
    contract = (((1,), (1,)), ((), ()))
    branches = 1 + len(DILATIONS)

    def body(x_ref, point_ref, dilated_ref, *rest):
        if finish:
            earlier_ref, proj_ref, pool_ref, keep_ref, out_ref = rest
        else:
            (out_ref,) = rest
        for index in range(blocks):
            base = front + margin * pitch + index * block
            rows = pl.ds(index * block, block)

            def window(shift):
                return x_ref[pl.ds(base + shift, block), :].astype(jnp.bfloat16)

            sums = [
                lax.dot_general(
                    window(0), point_ref[:, lanes], contract, preferred_element_type=jnp.float32
                )
            ]
            for branch, spread in enumerate(DILATIONS):
                total = None
                for vertical in range(3):
                    for lateral in range(3):
                        shift = (vertical - 1) * spread * pitch + (lateral - 1) * spread
                        term = lax.dot_general(
                            window(shift),
                            dilated_ref[branch, 3 * vertical + lateral, :, lanes],
                            contract,
                            preferred_element_type=jnp.float32,
                        )
                        total = term if total is None else total + term
                sums.append(total)
            if not finish:
                for branch, total in enumerate(sums):
                    out_ref[branch, rows, :] = total
                continue
            mixed = None
            for branch, total in enumerate(sums):
                term = lax.dot_general(
                    relu_bf16(earlier_ref[branch, rows, :] + total),
                    proj_ref[:, branch * width : (branch + 1) * width],
                    contract,
                    preferred_element_type=jnp.float32,
                )
                mixed = term if mixed is None else mixed + term
            mixed = mixed + pool_ref[...]
            rounded = relu_bf16(mixed).astype(jnp.float32)
            out_ref[rows, :] = jnp.where(keep_ref[...] > 0.5, rounded, 0.0)

    taps = 1 + 9 * len(DILATIONS)
    flops = 2 * blocks * block * channels * width * taps
    if finish:
        flops += 2 * blocks * block * branches * width * width
        out_shape = jax.ShapeDtypeStruct((blocks * block, width), jnp.float32)
    else:
        out_shape = jax.ShapeDtypeStruct((branches, blocks * block, width), jnp.float32)
    return pl.pallas_call(
        body,
        out_shape=out_shape,
        compiler_params=pltpu.CompilerParams(vmem_limit_bytes=56 * 1024 * 1024),
        cost_estimate=pl.CostEstimate(
            flops=flops,
            transcendentals=0,
            bytes_accessed=x.size * 4
            + aspp_dilated.size
            + branches * blocks * block * width * 4,
        ),
    )(x, aspp_point, aspp_dilated, *extra)


def head_kernel_call(x, head_weight, geometry):
    front, pitch, reach, block, blocks = geometry
    outputs = head_weight.shape[1]
    side = 2 * reach + 1
    contract = (((1,), (1,)), ((), ()))

    def body(x_ref, weight_ref, out_ref):
        for index in range(blocks):
            base = front + reach * pitch + index * block
            total = None
            for vertical in range(side):
                for lateral in range(side):
                    shift = (vertical - reach) * pitch + (lateral - reach)
                    term = lax.dot_general(
                        x_ref[pl.ds(base + shift, block), :].astype(jnp.bfloat16),
                        weight_ref[side * vertical + lateral],
                        contract,
                        preferred_element_type=jnp.float32,
                    )
                    total = term if total is None else total + term
            out_ref[pl.ds(index * block, block), :] = relu_bf16(total)

    return pl.pallas_call(
        body,
        out_shape=jax.ShapeDtypeStruct((blocks * block, outputs), jnp.bfloat16),
        compiler_params=pltpu.CompilerParams(vmem_limit_bytes=32 * 1024 * 1024),
        cost_estimate=pl.CostEstimate(
            flops=2 * blocks * block * x.shape[1] * outputs * side * side,
            transcendentals=0,
            bytes_accessed=x.size * 4 + head_weight.size * 2 + blocks * block * outputs * 2,
        ),
    )(x, head_weight)


def relu_bf16(values):
    return jnp.maximum(values, 0.0).astype(jnp.bfloat16)


def emit_heads(head_out, out_weight):
    groups = head_out.reshape(3, -1, head_out.shape[1], head_out.shape[2])
    center_map = jnp.einsum(
        "c,crw->rw", out_weight[0], groups[0], preferred_element_type=jnp.float32
    )
    offset_map = jnp.einsum(
        "oc,crw->orw", out_weight[1:3], groups[1], preferred_element_type=jnp.float32
    )
    depth_map = jnp.einsum(
        "c,crw->rw", out_weight[3], groups[2], preferred_element_type=jnp.float32
    )
    return jnp.concatenate([center_map[None], offset_map, depth_map[None]], 0)


def shards(
    frames,
    clip_start,
    semantic,
    instance,
    aspp_point,
    aspp_dilated,
    pool_weight,
    proj_weight,
    head_weight,
    out_weight,
):
    own_band = frames[0]
    channel_count, band_rows, columns = own_band.shape
    frame_count = clip_start.shape[0]
    height = band_rows * lax.axis_size("row")
    time_index = lax.axis_index("tm")
    row_index = lax.axis_index("row")
    ahead = (time_index + 1) % frame_count
    at_end = lax.dynamic_index_in_dim(clip_start, ahead, 0, keepdims=False) == 1
    later_band = jnp.where(at_end, own_band, shifted(own_band, "tm", -1))
    rim_rows = min(aspp_reach, band_rows)
    extra_rows = aspp_reach - rim_rows

    wide_rows = band_rows + 2 * aspp_reach
    pitch = -(-(columns + aspp_reach) // 8) * 8
    front = pitch
    block_rows = 8 if band_rows % 8 == 0 else band_rows
    block = block_rows * pitch
    blocks = band_rows // block_rows

    def flat_of(band):
        wide = jnp.pad(
            with_rims(band, "row", 1, rim_rows), ((0, 0), (extra_rows, extra_rows), (0, 0))
        )
        return jnp.pad(
            jnp.transpose(wide, (1, 2, 0)).astype(jnp.float32),
            ((1, 1), (pitch - columns, 0), (0, 0)),
        ).reshape((wide_rows + 2) * pitch, channel_count)

    geometry = (front, pitch, aspp_reach, block, blocks)
    own_sums = aspp_pass(
        flat_of(own_band), aspp_point, aspp_dilated, (), geometry, 0, False
    )

    counted = (semantic[0] >= THING_FIRST) & (instance[0] > 0)
    labels = jnp.arange(INSTANCES, dtype=jnp.int32)
    onehot = ((instance[0][None] == labels[:, None, None]) & counted[None]).astype(jnp.float32)
    row_pos = (row_index * band_rows + jnp.arange(band_rows, dtype=jnp.int32)).astype(jnp.float32)[
        :, None
    ] * jnp.ones((1, columns), jnp.float32)
    col_pos = jnp.arange(columns, dtype=jnp.float32)[None, :] * jnp.ones(
        (band_rows, 1), jnp.float32
    )
    local_stats = jnp.stack(
        [
            jnp.sum(onehot, axis=(1, 2)),
            jnp.sum(onehot * row_pos, axis=(1, 2)),
            jnp.sum(onehot * col_pos, axis=(1, 2)),
        ],
        0,
    )
    channel_sums = jnp.concatenate(
        [jnp.sum(band, axis=(1, 2), dtype=jnp.float32) for band in (own_band, later_band)]
    )
    frame_totals, inst_stats = all_sum((channel_sums, local_stats), ("row",))
    pooled = (frame_totals / (height * columns)).astype(jnp.bfloat16)
    pool_feature = relu_bf16(jnp.dot(pool_weight, pooled, preferred_element_type=jnp.float32))
    aspp_width = aspp_point.shape[0]
    pool_term = jnp.dot(
        proj_weight[:, 4 * aspp_width :], pool_feature, preferred_element_type=jnp.float32
    )[None]
    pad_columns = pitch - columns
    keep = (jnp.arange(block) % pitch >= pad_columns).astype(jnp.float32)[:, None]
    projected_flat = aspp_pass(
        flat_of(later_band),
        aspp_point,
        aspp_dilated,
        (own_sums, proj_weight, pool_term, keep),
        geometry,
        1,
        True,
    )
    head_reach = 2
    head_in = jnp.pad(
        with_rims(projected_flat, "row", 0, head_reach * pitch), ((pitch, pitch), (0, 0))
    )
    head_flat = head_kernel_call(head_in, head_weight, (pitch, pitch, head_reach, block, blocks))
    head_out = jnp.transpose(
        head_flat.reshape(band_rows, pitch, head_weight.shape[1])[:, pad_columns:], (2, 0, 1)
    )
    predictions = emit_heads(head_out, out_weight)
    pixel = jnp.einsum("sk,khw->shw", inst_stats, onehot, precision=lax.Precision.HIGHEST)
    counts = jnp.where(counted, pixel[0], 1.0)
    centre_row = pixel[1] / counts
    centre_col = pixel[2] / counts
    distance = (row_pos - centre_row) * (row_pos - centre_row) + (col_pos - centre_col) * (
        col_pos - centre_col
    )
    heat = jnp.where(counted, jnp.exp(-distance / (2.0 * center_sigma * center_sigma)), 0.0)
    center_err = jnp.sum(jnp.square(predictions[0] - heat))
    offset_err = jnp.sum(
        jnp.where(
            counted,
            jnp.abs(predictions[1] - (centre_row - row_pos))
            + jnp.abs(predictions[2] - (centre_col - col_pos)),
            0.0,
        )
    )
    counted_local = jnp.sum(counted.astype(jnp.float32))
    local_totals = lax.optimization_barrier(jnp.stack([center_err, offset_err, counted_local]))
    totals = all_sum(local_totals, ("row", "tm"))
    center_total, offset_total, counted_total = totals[0], totals[1], totals[2]
    losses = jnp.stack(
        [
            center_total / (frame_count * height * columns),
            offset_weight * offset_total / jnp.maximum(counted_total, 1.0),
        ]
    )
    return (predictions[None], losses)


def solution(mesh):
    placed = (
        P(("grp", "tm"), None, "row", None),
        P("grp"),
        P(("grp", "tm"), "row", None),
        P(("grp", "tm"), "row", None),
        P(),
        P(),
        P(),
        P(),
        P(),
        P(),
    )
    return jax.shard_map(
        shards,
        mesh=mesh,
        in_specs=placed,
        out_specs=(P(("grp", "tm"), None, "row", None), P("grp")),
        check_vma=False,
    )
```

```python
import jax
import jax.numpy as jnp
from jax import lax
from jax.sharding import PartitionSpec as P
from jax.experimental import pallas as pl
from jax.experimental.pallas import tpu as pltpu

THING_FIRST = 11
INSTANCES = 64


DILATIONS = (6, 12, 18)
aspp_reach = 18
center_sigma = 8.0
offset_weight = 0.01


def padded_2(block, sides, width):
    for axis, dim in sides:
        count = lax.axis_size(axis)
        forward = [(i, i + 1) for i in range(count - 1)]
        backward = [(target, source) for source, target in forward]
        low = lax.ppermute(
            lax.slice_in_dim(block, block.shape[dim] - width, None, axis=dim), axis, forward
        )
        high = lax.ppermute(lax.slice_in_dim(block, 0, width, axis=dim), axis, backward)
        block = jnp.concatenate([low, block, high], axis=dim)
    return block


def with_rims(block, axis, dim, width):
    if lax.axis_size(axis) != 2:
        return padded_2(block, ((axis, dim),), width)
    first = lax.axis_index(axis) == 0
    size = block.shape[dim]
    sent = jnp.where(
        first,
        lax.slice_in_dim(block, size - width, None, axis=dim),
        lax.slice_in_dim(block, 0, width, axis=dim),
    )
    got = lax.ppermute(sent, axis, [(0, 1), (1, 0)])
    empty = jnp.zeros_like(got)
    low = jnp.where(first, empty, got)
    high = jnp.where(first, got, empty)
    return jnp.concatenate([low, block, high], axis=dim)


def shifted(value, axis, steps):
    count = lax.axis_size(axis)
    pairs = [(source, (source + steps) % count) for source in range(count)]
    return lax.ppermute(value, axis, pairs)


def all_sum(value, axes):
    for axis in axes:
        count = lax.axis_size(axis)
        if count & (count - 1):
            value = jax.tree.map(lambda v: lax.psum(v, axis), value)
            continue
        step = 1
        while step < count:
            pairs = [(i, i ^ step) for i in range(count)]
            other = lax.ppermute(value, axis, pairs)
            value = jax.tree.map(jnp.add, value, other)
            step *= 2
    return value


def aspp_pass(x, aspp_point, aspp_dilated, extra, geometry, part, finish):
    front, pitch, margin, block, blocks = geometry
    width = aspp_point.shape[0]
    channels = x.shape[1]
    lanes = pl.ds(part * channels, channels)
    contract = (((1,), (1,)), ((), ()))
    branches = 1 + len(DILATIONS)

    def body(x_ref, point_ref, dilated_ref, *rest):
        if finish:
            earlier_hbm, proj_ref, pool_ref, keep_ref, out_ref, earlier_ref, sems = rest
        else:
            out_hbm, out_ref, sems = rest

        def block_copy(index):
            rows = pl.ds(index * block, block)
            if finish:
                return pltpu.make_async_copy(
                    earlier_hbm.at[:, rows, :], earlier_ref.at[:, rows, :], sems.at[index]
                )
            return pltpu.make_async_copy(
                out_ref.at[:, rows, :], out_hbm.at[:, rows, :], sems.at[index]
            )

        if finish:
            for index in range(blocks):
                block_copy(index).start()
        for index in range(blocks):
            base = front + margin * pitch + index * block
            rows = pl.ds(index * block, block)
            if finish:
                block_copy(index).wait()

            def window(shift):
                return x_ref[pl.ds(base + shift, block), :].astype(jnp.bfloat16)

            sums = [
                lax.dot_general(
                    window(0), point_ref[:, lanes], contract, preferred_element_type=jnp.float32
                )
            ]
            for branch, spread in enumerate(DILATIONS):
                total = None
                for vertical in range(3):
                    for lateral in range(3):
                        shift = (vertical - 1) * spread * pitch + (lateral - 1) * spread
                        term = lax.dot_general(
                            window(shift),
                            dilated_ref[branch, 3 * vertical + lateral, :, lanes],
                            contract,
                            preferred_element_type=jnp.float32,
                        )
                        total = term if total is None else total + term
                sums.append(total)
            if not finish:
                for branch, total in enumerate(sums):
                    out_ref[branch, rows, :] = total
                block_copy(index).start()
                continue
            mixed = None
            for branch, total in enumerate(sums):
                term = lax.dot_general(
                    relu_bf16(earlier_ref[branch, rows, :] + total),
                    proj_ref[:, branch * width : (branch + 1) * width],
                    contract,
                    preferred_element_type=jnp.float32,
                )
                mixed = term if mixed is None else mixed + term
            mixed = mixed + pool_ref[...]
            rounded = relu_bf16(mixed).astype(jnp.float32)
            out_ref[rows, :] = jnp.where(keep_ref[...] > 0.5, rounded, 0.0)
        if not finish:
            for index in range(blocks):
                block_copy(index).wait()

    taps = 1 + 9 * len(DILATIONS)
    flops = 2 * blocks * block * channels * width * taps
    sums_shape = (branches, blocks * block, width)
    vmem = pl.BlockSpec(memory_space=pltpu.VMEM)
    hbm = pl.BlockSpec(memory_space=pl.ANY)
    scratch = [pltpu.VMEM(sums_shape, jnp.float32), pltpu.SemaphoreType.DMA((blocks,))]
    if finish:
        flops += 2 * blocks * block * branches * width * width
        out_shape = jax.ShapeDtypeStruct((blocks * block, width), jnp.float32)
        in_specs = [vmem, vmem, vmem, hbm, vmem, vmem, vmem]
        out_specs = vmem
    else:
        out_shape = jax.ShapeDtypeStruct(sums_shape, jnp.float32)
        in_specs = [vmem, vmem, vmem]
        out_specs = hbm
    return pl.pallas_call(
        body,
        out_shape=out_shape,
        in_specs=in_specs,
        out_specs=out_specs,
        scratch_shapes=scratch,
        compiler_params=pltpu.CompilerParams(vmem_limit_bytes=56 * 1024 * 1024),
        cost_estimate=pl.CostEstimate(
            flops=flops,
            transcendentals=0,
            bytes_accessed=x.size * 4
            + aspp_dilated.size
            + branches * blocks * block * width * 4,
        ),
    )(x, aspp_point, aspp_dilated, *extra)


def head_kernel_call(x, head_weight, geometry):
    front, pitch, reach, block, blocks = geometry
    outputs = head_weight.shape[1]
    side = 2 * reach + 1
    contract = (((1,), (1,)), ((), ()))

    def body(x_ref, weight_ref, out_ref):
        for index in range(blocks):
            base = front + reach * pitch + index * block
            total = None
            for vertical in range(side):
                for lateral in range(side):
                    shift = (vertical - reach) * pitch + (lateral - reach)
                    term = lax.dot_general(
                        x_ref[pl.ds(base + shift, block), :].astype(jnp.bfloat16),
                        weight_ref[side * vertical + lateral],
                        contract,
                        preferred_element_type=jnp.float32,
                    )
                    total = term if total is None else total + term
            out_ref[pl.ds(index * block, block), :] = relu_bf16(total)

    return pl.pallas_call(
        body,
        out_shape=jax.ShapeDtypeStruct((blocks * block, outputs), jnp.bfloat16),
        compiler_params=pltpu.CompilerParams(vmem_limit_bytes=32 * 1024 * 1024),
        cost_estimate=pl.CostEstimate(
            flops=2 * blocks * block * x.shape[1] * outputs * side * side,
            transcendentals=0,
            bytes_accessed=x.size * 4 + head_weight.size * 2 + blocks * block * outputs * 2,
        ),
    )(x, head_weight)


def relu_bf16(values):
    return jnp.maximum(values, 0.0).astype(jnp.bfloat16)


def emit_heads(head_out, out_weight):
    groups = head_out.reshape(3, -1, head_out.shape[1], head_out.shape[2])
    center_map = jnp.einsum(
        "c,crw->rw", out_weight[0], groups[0], preferred_element_type=jnp.float32
    )
    offset_map = jnp.einsum(
        "oc,crw->orw", out_weight[1:3], groups[1], preferred_element_type=jnp.float32
    )
    depth_map = jnp.einsum(
        "c,crw->rw", out_weight[3], groups[2], preferred_element_type=jnp.float32
    )
    return jnp.concatenate([center_map[None], offset_map, depth_map[None]], 0)


def shards(
    frames,
    clip_start,
    semantic,
    instance,
    aspp_point,
    aspp_dilated,
    pool_weight,
    proj_weight,
    head_weight,
    out_weight,
):
    own_band = frames[0]
    channel_count, band_rows, columns = own_band.shape
    frame_count = clip_start.shape[0]
    height = band_rows * lax.axis_size("row")
    time_index = lax.axis_index("tm")
    row_index = lax.axis_index("row")
    ahead = (time_index + 1) % frame_count
    at_end = lax.dynamic_index_in_dim(clip_start, ahead, 0, keepdims=False) == 1
    later_band = jnp.where(at_end, own_band, shifted(own_band, "tm", -1))
    rim_rows = min(aspp_reach, band_rows)
    extra_rows = aspp_reach - rim_rows

    wide_rows = band_rows + 2 * aspp_reach
    pitch = -(-(columns + aspp_reach) // 8) * 8
    front = pitch
    block_rows = 8 if band_rows % 8 == 0 else band_rows
    block = block_rows * pitch
    blocks = band_rows // block_rows

    def flat_of(band):
        wide = jnp.pad(
            with_rims(band, "row", 1, rim_rows), ((0, 0), (extra_rows, extra_rows), (0, 0))
        )
        return jnp.pad(
            jnp.transpose(wide, (1, 2, 0)).astype(jnp.float32),
            ((1, 1), (pitch - columns, 0), (0, 0)),
        ).reshape((wide_rows + 2) * pitch, channel_count)

    geometry = (front, pitch, aspp_reach, block, blocks)
    own_sums = aspp_pass(
        flat_of(own_band), aspp_point, aspp_dilated, (), geometry, 0, False
    )

    counted = (semantic[0] >= THING_FIRST) & (instance[0] > 0)
    labels = jnp.arange(INSTANCES, dtype=jnp.int32)
    onehot = ((instance[0][None] == labels[:, None, None]) & counted[None]).astype(jnp.float32)
    row_pos = (row_index * band_rows + jnp.arange(band_rows, dtype=jnp.int32)).astype(jnp.float32)[
        :, None
    ] * jnp.ones((1, columns), jnp.float32)
    col_pos = jnp.arange(columns, dtype=jnp.float32)[None, :] * jnp.ones(
        (band_rows, 1), jnp.float32
    )
    local_stats = jnp.stack(
        [
            jnp.sum(onehot, axis=(1, 2)),
            jnp.sum(onehot * row_pos, axis=(1, 2)),
            jnp.sum(onehot * col_pos, axis=(1, 2)),
        ],
        0,
    )
    channel_sums = jnp.concatenate(
        [jnp.sum(band, axis=(1, 2), dtype=jnp.float32) for band in (own_band, later_band)]
    )
    frame_totals, inst_stats = all_sum((channel_sums, local_stats), ("row",))
    pooled = (frame_totals / (height * columns)).astype(jnp.bfloat16)
    pool_feature = relu_bf16(jnp.dot(pool_weight, pooled, preferred_element_type=jnp.float32))
    aspp_width = aspp_point.shape[0]
    pool_term = jnp.dot(
        proj_weight[:, 4 * aspp_width :], pool_feature, preferred_element_type=jnp.float32
    )[None]
    pad_columns = pitch - columns
    keep = (jnp.arange(block) % pitch >= pad_columns).astype(jnp.float32)[:, None]
    projected_flat = aspp_pass(
        flat_of(later_band),
        aspp_point,
        aspp_dilated,
        (own_sums, proj_weight, pool_term, keep),
        geometry,
        1,
        True,
    )
    head_reach = 2
    head_in = jnp.pad(
        with_rims(projected_flat, "row", 0, head_reach * pitch), ((pitch, pitch), (0, 0))
    )
    head_flat = head_kernel_call(head_in, head_weight, (pitch, pitch, head_reach, block, blocks))
    head_out = jnp.transpose(
        head_flat.reshape(band_rows, pitch, head_weight.shape[1])[:, pad_columns:], (2, 0, 1)
    )
    predictions = emit_heads(head_out, out_weight)
    pixel = jnp.einsum("sk,khw->shw", inst_stats, onehot, precision=lax.Precision.HIGHEST)
    counts = jnp.where(counted, pixel[0], 1.0)
    centre_row = pixel[1] / counts
    centre_col = pixel[2] / counts
    distance = (row_pos - centre_row) * (row_pos - centre_row) + (col_pos - centre_col) * (
        col_pos - centre_col
    )
    heat = jnp.where(counted, jnp.exp(-distance / (2.0 * center_sigma * center_sigma)), 0.0)
    center_err = jnp.sum(jnp.square(predictions[0] - heat))
    offset_err = jnp.sum(
        jnp.where(
            counted,
            jnp.abs(predictions[1] - (centre_row - row_pos))
            + jnp.abs(predictions[2] - (centre_col - col_pos)),
            0.0,
        )
    )
    counted_local = jnp.sum(counted.astype(jnp.float32))
    local_totals = lax.optimization_barrier(jnp.stack([center_err, offset_err, counted_local]))
    totals = all_sum(local_totals, ("row", "tm"))
    center_total, offset_total, counted_total = totals[0], totals[1], totals[2]
    losses = jnp.stack(
        [
            center_total / (frame_count * height * columns),
            offset_weight * offset_total / jnp.maximum(counted_total, 1.0),
        ]
    )
    return (predictions[None], losses)


def solution(mesh):
    placed = (
        P(("grp", "tm"), None, "row", None),
        P("grp"),
        P(("grp", "tm"), "row", None),
        P(("grp", "tm"), "row", None),
        P(),
        P(),
        P(),
        P(),
        P(),
        P(),
    )
    return jax.shard_map(
        shards,
        mesh=mesh,
        in_specs=placed,
        out_specs=(P(("grp", "tm"), None, "row", None), P("grp")),
        check_vma=False,
    )
```

```python
import jax
import jax.numpy as jnp
from jax import lax
from jax.sharding import PartitionSpec as P
from jax.experimental import pallas as pl
from jax.experimental.pallas import tpu as pltpu

THING_FIRST = 11
INSTANCES = 64


DILATIONS = (6, 12, 18)
aspp_reach = 18
center_sigma = 8.0
offset_weight = 0.01


def padded_2(block, sides, width):
    for axis, dim in sides:
        count = lax.axis_size(axis)
        forward = [(i, i + 1) for i in range(count - 1)]
        backward = [(target, source) for source, target in forward]
        low = lax.ppermute(
            lax.slice_in_dim(block, block.shape[dim] - width, None, axis=dim), axis, forward
        )
        high = lax.ppermute(lax.slice_in_dim(block, 0, width, axis=dim), axis, backward)
        block = jnp.concatenate([low, block, high], axis=dim)
    return block


def with_rims(block, axis, dim, width):
    if lax.axis_size(axis) != 2:
        return padded_2(block, ((axis, dim),), width)
    first = lax.axis_index(axis) == 0
    size = block.shape[dim]
    sent = jnp.where(
        first,
        lax.slice_in_dim(block, size - width, None, axis=dim),
        lax.slice_in_dim(block, 0, width, axis=dim),
    )
    got = lax.ppermute(sent, axis, [(0, 1), (1, 0)])
    empty = jnp.zeros_like(got)
    low = jnp.where(first, empty, got)
    high = jnp.where(first, got, empty)
    return jnp.concatenate([low, block, high], axis=dim)


def shifted(value, axis, steps):
    count = lax.axis_size(axis)
    pairs = [(source, (source + steps) % count) for source in range(count)]
    return lax.ppermute(value, axis, pairs)


def all_sum(value, axes):
    for axis in axes:
        count = lax.axis_size(axis)
        if count & (count - 1):
            value = jax.tree.map(lambda v: lax.psum(v, axis), value)
            continue
        step = 1
        while step < count:
            pairs = [(i, i ^ step) for i in range(count)]
            other = lax.ppermute(value, axis, pairs)
            value = jax.tree.map(jnp.add, value, other)
            step *= 2
    return value


def aspp_pass(x, aspp_point, aspp_dilated, extra, geometry, part, finish):
    front, pitch, margin, block, blocks = geometry
    width = aspp_point.shape[0]
    channels = x.shape[1]
    lanes = pl.ds(part * channels, channels)
    contract = (((1,), (1,)), ((), ()))
    branches = 1 + len(DILATIONS)

    def body(x_ref, point_ref, dilated_ref, *rest):
        if finish:
            (earlier_hbm, proj_ref, pool_ref, keep_ref, out_ref, earlier_ref, sems,
             weight_ref, weight_sems) = rest
        else:
            out_hbm, out_ref, sems, weight_ref, weight_sems = rest

        def weight_copy(branch):
            return pltpu.make_async_copy(
                dilated_ref.at[branch, :, :, lanes], weight_ref.at[branch], weight_sems.at[branch]
            )

        for branch in range(len(DILATIONS)):
            weight_copy(branch).start()

        def block_copy(index):
            rows = pl.ds(index * block, block)
            if finish:
                return pltpu.make_async_copy(
                    earlier_hbm.at[:, rows, :], earlier_ref.at[:, rows, :], sems.at[index]
                )
            return pltpu.make_async_copy(
                out_ref.at[:, rows, :], out_hbm.at[:, rows, :], sems.at[index]
            )

        if finish:
            for index in range(blocks):
                block_copy(index).start()
        for index in range(blocks):
            base = front + margin * pitch + index * block
            rows = pl.ds(index * block, block)
            if finish:
                block_copy(index).wait()

            def window(shift):
                return x_ref[pl.ds(base + shift, block), :].astype(jnp.bfloat16)

            sums = [
                lax.dot_general(
                    window(0), point_ref[:, lanes], contract, preferred_element_type=jnp.float32
                )
            ]
            for branch, spread in enumerate(DILATIONS):
                if index == 0:
                    weight_copy(branch).wait()
                total = None
                for vertical in range(3):
                    for lateral in range(3):
                        shift = (vertical - 1) * spread * pitch + (lateral - 1) * spread
                        term = lax.dot_general(
                            window(shift),
                            weight_ref[branch, 3 * vertical + lateral],
                            contract,
                            preferred_element_type=jnp.float32,
                        )
                        total = term if total is None else total + term
                sums.append(total)
            if not finish:
                for branch, total in enumerate(sums):
                    out_ref[branch, rows, :] = total
                block_copy(index).start()
                continue
            mixed = None
            for branch, total in enumerate(sums):
                term = lax.dot_general(
                    relu_bf16(earlier_ref[branch, rows, :] + total),
                    proj_ref[:, branch * width : (branch + 1) * width],
                    contract,
                    preferred_element_type=jnp.float32,
                )
                mixed = term if mixed is None else mixed + term
            mixed = mixed + pool_ref[...]
            rounded = relu_bf16(mixed).astype(jnp.float32)
            out_ref[rows, :] = jnp.where(keep_ref[...] > 0.5, rounded, 0.0)
        if not finish:
            for index in range(blocks):
                block_copy(index).wait()

    taps = 1 + 9 * len(DILATIONS)
    flops = 2 * blocks * block * channels * width * taps
    sums_shape = (branches, blocks * block, width)
    vmem = pl.BlockSpec(memory_space=pltpu.VMEM)
    hbm = pl.BlockSpec(memory_space=pl.ANY)
    scratch = [
        pltpu.VMEM(sums_shape, jnp.float32),
        pltpu.SemaphoreType.DMA((blocks,)),
        pltpu.VMEM(aspp_dilated.shape[:3] + (channels,), aspp_dilated.dtype),
        pltpu.SemaphoreType.DMA((len(DILATIONS),)),
    ]
    if finish:
        flops += 2 * blocks * block * branches * width * width
        out_shape = jax.ShapeDtypeStruct((blocks * block, width), jnp.float32)
        in_specs = [vmem, vmem, hbm, hbm, vmem, vmem, vmem]
        out_specs = vmem
    else:
        out_shape = jax.ShapeDtypeStruct(sums_shape, jnp.float32)
        in_specs = [vmem, vmem, hbm]
        out_specs = hbm
    return pl.pallas_call(
        body,
        out_shape=out_shape,
        in_specs=in_specs,
        out_specs=out_specs,
        scratch_shapes=scratch,
        compiler_params=pltpu.CompilerParams(vmem_limit_bytes=56 * 1024 * 1024),
        cost_estimate=pl.CostEstimate(
            flops=flops,
            transcendentals=0,
            bytes_accessed=x.size * 4
            + aspp_dilated.size
            + branches * blocks * block * width * 4,
        ),
    )(x, aspp_point, aspp_dilated, *extra)


def head_kernel_call(x, head_weight, geometry):
    front, pitch, reach, block, blocks = geometry
    outputs = head_weight.shape[1]
    side = 2 * reach + 1
    contract = (((1,), (1,)), ((), ()))

    def body(x_ref, weight_ref, out_ref):
        for index in range(blocks):
            base = front + reach * pitch + index * block
            total = None
            for vertical in range(side):
                for lateral in range(side):
                    shift = (vertical - reach) * pitch + (lateral - reach)
                    term = lax.dot_general(
                        x_ref[pl.ds(base + shift, block), :].astype(jnp.bfloat16),
                        weight_ref[side * vertical + lateral],
                        contract,
                        preferred_element_type=jnp.float32,
                    )
                    total = term if total is None else total + term
            out_ref[pl.ds(index * block, block), :] = relu_bf16(total)

    return pl.pallas_call(
        body,
        out_shape=jax.ShapeDtypeStruct((blocks * block, outputs), jnp.bfloat16),
        compiler_params=pltpu.CompilerParams(vmem_limit_bytes=32 * 1024 * 1024),
        cost_estimate=pl.CostEstimate(
            flops=2 * blocks * block * x.shape[1] * outputs * side * side,
            transcendentals=0,
            bytes_accessed=x.size * 4 + head_weight.size * 2 + blocks * block * outputs * 2,
        ),
    )(x, head_weight)


def relu_bf16(values):
    return jnp.maximum(values, 0.0).astype(jnp.bfloat16)


def emit_heads(head_out, out_weight):
    groups = head_out.reshape(3, -1, head_out.shape[1], head_out.shape[2])
    center_map = jnp.einsum(
        "c,crw->rw", out_weight[0], groups[0], preferred_element_type=jnp.float32
    )
    offset_map = jnp.einsum(
        "oc,crw->orw", out_weight[1:3], groups[1], preferred_element_type=jnp.float32
    )
    depth_map = jnp.einsum(
        "c,crw->rw", out_weight[3], groups[2], preferred_element_type=jnp.float32
    )
    return jnp.concatenate([center_map[None], offset_map, depth_map[None]], 0)


def shards(
    frames,
    clip_start,
    semantic,
    instance,
    aspp_point,
    aspp_dilated,
    pool_weight,
    proj_weight,
    head_weight,
    out_weight,
):
    own_band = frames[0]
    channel_count, band_rows, columns = own_band.shape
    frame_count = clip_start.shape[0]
    height = band_rows * lax.axis_size("row")
    time_index = lax.axis_index("tm")
    row_index = lax.axis_index("row")
    ahead = (time_index + 1) % frame_count
    at_end = lax.dynamic_index_in_dim(clip_start, ahead, 0, keepdims=False) == 1
    later_band = jnp.where(at_end, own_band, shifted(own_band, "tm", -1))
    rim_rows = min(aspp_reach, band_rows)
    extra_rows = aspp_reach - rim_rows

    wide_rows = band_rows + 2 * aspp_reach
    pitch = -(-(columns + aspp_reach) // 8) * 8
    front = pitch
    block_rows = 8 if band_rows % 8 == 0 else band_rows
    block = block_rows * pitch
    blocks = band_rows // block_rows

    def flat_of(band):
        wide = jnp.pad(
            with_rims(band, "row", 1, rim_rows), ((0, 0), (extra_rows, extra_rows), (0, 0))
        )
        return jnp.pad(
            jnp.transpose(wide, (1, 2, 0)).astype(jnp.float32),
            ((1, 1), (pitch - columns, 0), (0, 0)),
        ).reshape((wide_rows + 2) * pitch, channel_count)

    geometry = (front, pitch, aspp_reach, block, blocks)
    own_sums = aspp_pass(
        flat_of(own_band), aspp_point, aspp_dilated, (), geometry, 0, False
    )

    counted = (semantic[0] >= THING_FIRST) & (instance[0] > 0)
    labels = jnp.arange(INSTANCES, dtype=jnp.int32)
    onehot = ((instance[0][None] == labels[:, None, None]) & counted[None]).astype(jnp.float32)
    row_pos = (row_index * band_rows + jnp.arange(band_rows, dtype=jnp.int32)).astype(jnp.float32)[
        :, None
    ] * jnp.ones((1, columns), jnp.float32)
    col_pos = jnp.arange(columns, dtype=jnp.float32)[None, :] * jnp.ones(
        (band_rows, 1), jnp.float32
    )
    local_stats = jnp.stack(
        [
            jnp.sum(onehot, axis=(1, 2)),
            jnp.sum(onehot * row_pos, axis=(1, 2)),
            jnp.sum(onehot * col_pos, axis=(1, 2)),
        ],
        0,
    )
    channel_sums = jnp.concatenate(
        [jnp.sum(band, axis=(1, 2), dtype=jnp.float32) for band in (own_band, later_band)]
    )
    frame_totals, inst_stats = all_sum((channel_sums, local_stats), ("row",))
    pooled = (frame_totals / (height * columns)).astype(jnp.bfloat16)
    pool_feature = relu_bf16(jnp.dot(pool_weight, pooled, preferred_element_type=jnp.float32))
    aspp_width = aspp_point.shape[0]
    pool_term = jnp.dot(
        proj_weight[:, 4 * aspp_width :], pool_feature, preferred_element_type=jnp.float32
    )[None]
    pad_columns = pitch - columns
    keep = (jnp.arange(block) % pitch >= pad_columns).astype(jnp.float32)[:, None]
    projected_flat = aspp_pass(
        flat_of(later_band),
        aspp_point,
        aspp_dilated,
        (own_sums, proj_weight, pool_term, keep),
        geometry,
        1,
        True,
    )
    head_reach = 2
    head_in = jnp.pad(
        with_rims(projected_flat, "row", 0, head_reach * pitch), ((pitch, pitch), (0, 0))
    )
    head_flat = head_kernel_call(head_in, head_weight, (pitch, pitch, head_reach, block, blocks))
    head_out = jnp.transpose(
        head_flat.reshape(band_rows, pitch, head_weight.shape[1])[:, pad_columns:], (2, 0, 1)
    )
    predictions = emit_heads(head_out, out_weight)
    pixel = jnp.einsum("sk,khw->shw", inst_stats, onehot, precision=lax.Precision.HIGHEST)
    counts = jnp.where(counted, pixel[0], 1.0)
    centre_row = pixel[1] / counts
    centre_col = pixel[2] / counts
    distance = (row_pos - centre_row) * (row_pos - centre_row) + (col_pos - centre_col) * (
        col_pos - centre_col
    )
    heat = jnp.where(counted, jnp.exp(-distance / (2.0 * center_sigma * center_sigma)), 0.0)
    center_err = jnp.sum(jnp.square(predictions[0] - heat))
    offset_err = jnp.sum(
        jnp.where(
            counted,
            jnp.abs(predictions[1] - (centre_row - row_pos))
            + jnp.abs(predictions[2] - (centre_col - col_pos)),
            0.0,
        )
    )
    counted_local = jnp.sum(counted.astype(jnp.float32))
    local_totals = lax.optimization_barrier(jnp.stack([center_err, offset_err, counted_local]))
    totals = all_sum(local_totals, ("row", "tm"))
    center_total, offset_total, counted_total = totals[0], totals[1], totals[2]
    losses = jnp.stack(
        [
            center_total / (frame_count * height * columns),
            offset_weight * offset_total / jnp.maximum(counted_total, 1.0),
        ]
    )
    return (predictions[None], losses)


def solution(mesh):
    placed = (
        P(("grp", "tm"), None, "row", None),
        P("grp"),
        P(("grp", "tm"), "row", None),
        P(("grp", "tm"), "row", None),
        P(),
        P(),
        P(),
        P(),
        P(),
        P(),
    )
    return jax.shard_map(
        shards,
        mesh=mesh,
        in_specs=placed,
        out_specs=(P(("grp", "tm"), None, "row", None), P("grp")),
        check_vma=False,
    )
```

```python
import jax
import jax.numpy as jnp
from jax import lax
from jax.sharding import PartitionSpec as P
from jax.experimental import pallas as pl
from jax.experimental.pallas import tpu as pltpu

THING_FIRST = 11
INSTANCES = 64


DILATIONS = (6, 12, 18)
aspp_reach = 18
center_sigma = 8.0
offset_weight = 0.01


def padded_2(block, sides, width):
    for axis, dim in sides:
        count = lax.axis_size(axis)
        forward = [(i, i + 1) for i in range(count - 1)]
        backward = [(target, source) for source, target in forward]
        low = lax.ppermute(
            lax.slice_in_dim(block, block.shape[dim] - width, None, axis=dim), axis, forward
        )
        high = lax.ppermute(lax.slice_in_dim(block, 0, width, axis=dim), axis, backward)
        block = jnp.concatenate([low, block, high], axis=dim)
    return block


def with_rims(block, axis, dim, width):
    if lax.axis_size(axis) != 2:
        return padded_2(block, ((axis, dim),), width)
    first = lax.axis_index(axis) == 0
    size = block.shape[dim]
    sent = jnp.where(
        first,
        lax.slice_in_dim(block, size - width, None, axis=dim),
        lax.slice_in_dim(block, 0, width, axis=dim),
    )
    got = lax.ppermute(sent, axis, [(0, 1), (1, 0)])
    empty = jnp.zeros_like(got)
    low = jnp.where(first, empty, got)
    high = jnp.where(first, got, empty)
    return jnp.concatenate([low, block, high], axis=dim)


def shifted(value, axis, steps):
    count = lax.axis_size(axis)
    pairs = [(source, (source + steps) % count) for source in range(count)]
    return lax.ppermute(value, axis, pairs)


def all_sum(value, axes):
    for axis in axes:
        count = lax.axis_size(axis)
        if count & (count - 1):
            value = jax.tree.map(lambda v: lax.psum(v, axis), value)
            continue
        step = 1
        while step < count:
            pairs = [(i, i ^ step) for i in range(count)]
            other = lax.ppermute(value, axis, pairs)
            value = jax.tree.map(jnp.add, value, other)
            step *= 2
    return value


def aspp_pass(x, aspp_point, aspp_dilated, extra, geometry, part, finish, lead=0):
    front, pitch, margin, block, blocks = geometry
    width = aspp_point.shape[0]
    channels = x.shape[1]
    lanes = pl.ds(part * channels, channels)
    contract = (((1,), (1,)), ((), ()))
    branches = 1 + len(DILATIONS)

    def body(x_ref, point_ref, dilated_ref, *rest):
        if finish:
            earlier_hbm, proj_ref, pool_ref, keep_ref, out_ref, earlier_ref, sems = rest
        else:
            out_hbm, out_ref, sems = rest

        def block_copy(index):
            rows = pl.ds(index * block, block)
            if finish:
                return pltpu.make_async_copy(
                    earlier_hbm.at[:, rows, :], earlier_ref.at[:, rows, :], sems.at[index]
                )
            return pltpu.make_async_copy(
                out_ref.at[:, rows, :], out_hbm.at[:, rows, :], sems.at[index]
            )

        if finish:
            for index in range(blocks):
                block_copy(index).start()
        for index in range(blocks):
            base = front + margin * pitch + index * block
            rows = pl.ds(index * block, block)
            if finish:
                block_copy(index).wait()

            def window(shift):
                return x_ref[pl.ds(base + shift, block), :].astype(jnp.bfloat16)

            sums = [
                lax.dot_general(
                    window(0), point_ref[:, lanes], contract, preferred_element_type=jnp.float32
                )
            ]
            for branch, spread in enumerate(DILATIONS):
                total = None
                for vertical in range(3):
                    for lateral in range(3):
                        shift = (vertical - 1) * spread * pitch + (lateral - 1) * spread
                        term = lax.dot_general(
                            window(shift),
                            dilated_ref[branch, 3 * vertical + lateral, :, lanes],
                            contract,
                            preferred_element_type=jnp.float32,
                        )
                        total = term if total is None else total + term
                sums.append(total)
            if not finish:
                for branch, total in enumerate(sums):
                    out_ref[branch, rows, :] = total
                block_copy(index).start()
                continue
            mixed = None
            for branch, total in enumerate(sums):
                term = lax.dot_general(
                    relu_bf16(earlier_ref[branch, rows, :] + total),
                    proj_ref[:, branch * width : (branch + 1) * width],
                    contract,
                    preferred_element_type=jnp.float32,
                )
                mixed = term if mixed is None else mixed + term
            mixed = mixed + pool_ref[...]
            rounded = relu_bf16(mixed).astype(jnp.float32)
            out_ref[pl.ds(lead + index * block, block), :] = jnp.where(
                keep_ref[...] > 0.5, rounded, 0.0
            )
        if finish:
            zeros = jnp.zeros((lead, width), jnp.float32)
            out_ref[pl.ds(0, lead), :] = zeros
            out_ref[pl.ds(lead + blocks * block, lead), :] = zeros
        if not finish:
            for index in range(blocks):
                block_copy(index).wait()

    taps = 1 + 9 * len(DILATIONS)
    flops = 2 * blocks * block * channels * width * taps
    sums_shape = (branches, blocks * block, width)
    vmem = pl.BlockSpec(memory_space=pltpu.VMEM)
    hbm = pl.BlockSpec(memory_space=pl.ANY)
    scratch = [pltpu.VMEM(sums_shape, jnp.float32), pltpu.SemaphoreType.DMA((blocks,))]
    if finish:
        flops += 2 * blocks * block * branches * width * width
        out_shape = jax.ShapeDtypeStruct((blocks * block + 2 * lead, width), jnp.float32)
        in_specs = [vmem, vmem, vmem, hbm, vmem, vmem, vmem]
        out_specs = vmem
    else:
        out_shape = jax.ShapeDtypeStruct(sums_shape, jnp.float32)
        in_specs = [vmem, vmem, vmem]
        out_specs = hbm
    return pl.pallas_call(
        body,
        out_shape=out_shape,
        in_specs=in_specs,
        out_specs=out_specs,
        scratch_shapes=scratch,
        compiler_params=pltpu.CompilerParams(vmem_limit_bytes=56 * 1024 * 1024),
        cost_estimate=pl.CostEstimate(
            flops=flops,
            transcendentals=0,
            bytes_accessed=x.size * 4
            + aspp_dilated.size
            + branches * blocks * block * width * 4,
        ),
    )(x, aspp_point, aspp_dilated, *extra)


def head_kernel_call(x, head_weight, geometry):
    front, pitch, reach, block, blocks = geometry
    outputs = head_weight.shape[1]
    side = 2 * reach + 1
    contract = (((1,), (1,)), ((), ()))

    def body(x_ref, weight_ref, out_ref):
        for index in range(blocks):
            base = front + reach * pitch + index * block
            total = None
            for vertical in range(side):
                for lateral in range(side):
                    shift = (vertical - reach) * pitch + (lateral - reach)
                    term = lax.dot_general(
                        x_ref[pl.ds(base + shift, block), :].astype(jnp.bfloat16),
                        weight_ref[side * vertical + lateral],
                        contract,
                        preferred_element_type=jnp.float32,
                    )
                    total = term if total is None else total + term
            out_ref[pl.ds(index * block, block), :] = relu_bf16(total)

    return pl.pallas_call(
        body,
        out_shape=jax.ShapeDtypeStruct((blocks * block, outputs), jnp.bfloat16),
        compiler_params=pltpu.CompilerParams(vmem_limit_bytes=32 * 1024 * 1024),
        cost_estimate=pl.CostEstimate(
            flops=2 * blocks * block * x.shape[1] * outputs * side * side,
            transcendentals=0,
            bytes_accessed=x.size * 4 + head_weight.size * 2 + blocks * block * outputs * 2,
        ),
    )(x, head_weight)


def relu_bf16(values):
    return jnp.maximum(values, 0.0).astype(jnp.bfloat16)


def emit_heads(head_out, out_weight):
    groups = head_out.reshape(3, -1, head_out.shape[1], head_out.shape[2])
    center_map = jnp.einsum(
        "c,crw->rw", out_weight[0], groups[0], preferred_element_type=jnp.float32
    )
    offset_map = jnp.einsum(
        "oc,crw->orw", out_weight[1:3], groups[1], preferred_element_type=jnp.float32
    )
    depth_map = jnp.einsum(
        "c,crw->rw", out_weight[3], groups[2], preferred_element_type=jnp.float32
    )
    return jnp.concatenate([center_map[None], offset_map, depth_map[None]], 0)


def shards(
    frames,
    clip_start,
    semantic,
    instance,
    aspp_point,
    aspp_dilated,
    pool_weight,
    proj_weight,
    head_weight,
    out_weight,
):
    own_band = frames[0]
    channel_count, band_rows, columns = own_band.shape
    frame_count = clip_start.shape[0]
    height = band_rows * lax.axis_size("row")
    time_index = lax.axis_index("tm")
    row_index = lax.axis_index("row")
    ahead = (time_index + 1) % frame_count
    at_end = lax.dynamic_index_in_dim(clip_start, ahead, 0, keepdims=False) == 1
    later_band = jnp.where(at_end, own_band, shifted(own_band, "tm", -1))
    rim_rows = min(aspp_reach, band_rows)
    extra_rows = aspp_reach - rim_rows

    wide_rows = band_rows + 2 * aspp_reach
    pitch = -(-(columns + aspp_reach) // 8) * 8
    front = pitch
    block_rows = 8 if band_rows % 8 == 0 else band_rows
    block = block_rows * pitch
    blocks = band_rows // block_rows

    def flat_of(band):
        wide = jnp.pad(
            with_rims(band, "row", 1, rim_rows), ((0, 0), (extra_rows, extra_rows), (0, 0))
        )
        return jnp.pad(
            jnp.transpose(wide, (1, 2, 0)).astype(jnp.float32),
            ((1, 1), (pitch - columns, 0), (0, 0)),
        ).reshape((wide_rows + 2) * pitch, channel_count)

    geometry = (front, pitch, aspp_reach, block, blocks)
    own_sums = aspp_pass(
        flat_of(own_band), aspp_point, aspp_dilated, (), geometry, 0, False
    )

    counted = (semantic[0] >= THING_FIRST) & (instance[0] > 0)
    labels = jnp.arange(INSTANCES, dtype=jnp.int32)
    onehot = ((instance[0][None] == labels[:, None, None]) & counted[None]).astype(jnp.float32)
    row_pos = (row_index * band_rows + jnp.arange(band_rows, dtype=jnp.int32)).astype(jnp.float32)[
        :, None
    ] * jnp.ones((1, columns), jnp.float32)
    col_pos = jnp.arange(columns, dtype=jnp.float32)[None, :] * jnp.ones(
        (band_rows, 1), jnp.float32
    )
    local_stats = jnp.stack(
        [
            jnp.sum(onehot, axis=(1, 2)),
            jnp.sum(onehot * row_pos, axis=(1, 2)),
            jnp.sum(onehot * col_pos, axis=(1, 2)),
        ],
        0,
    )
    channel_sums = jnp.concatenate(
        [jnp.sum(band, axis=(1, 2), dtype=jnp.float32) for band in (own_band, later_band)]
    )
    frame_totals, inst_stats = all_sum((channel_sums, local_stats), ("row",))
    pooled = (frame_totals / (height * columns)).astype(jnp.bfloat16)
    pool_feature = relu_bf16(jnp.dot(pool_weight, pooled, preferred_element_type=jnp.float32))
    aspp_width = aspp_point.shape[0]
    pool_term = jnp.dot(
        proj_weight[:, 4 * aspp_width :], pool_feature, preferred_element_type=jnp.float32
    )[None]
    pad_columns = pitch - columns
    keep = (jnp.arange(block) % pitch >= pad_columns).astype(jnp.float32)[:, None]
    projected_flat = aspp_pass(
        flat_of(later_band),
        aspp_point,
        aspp_dilated,
        (own_sums, proj_weight, pool_term, keep),
        geometry,
        1,
        True,
        lead=(1 + 2) * pitch,
    )
    head_reach = 2
    rim = head_reach * pitch
    lead = pitch + rim
    band_flat = lax.slice_in_dim(projected_flat, lead, lead + blocks * block, axis=0)
    edges = jnp.concatenate([band_flat[:rim], band_flat[-rim:]], 0)
    rimmed = with_rims(edges, "row", 0, rim)
    head_in = lax.dynamic_update_slice(projected_flat, rimmed[:rim], (pitch, 0))
    head_in = lax.dynamic_update_slice(head_in, rimmed[-rim:], (lead + blocks * block, 0))
    head_flat = head_kernel_call(head_in, head_weight, (pitch, pitch, head_reach, block, blocks))
    head_out = jnp.transpose(
        head_flat.reshape(band_rows, pitch, head_weight.shape[1])[:, pad_columns:], (2, 0, 1)
    )
    predictions = emit_heads(head_out, out_weight)
    pixel = jnp.einsum("sk,khw->shw", inst_stats, onehot, precision=lax.Precision.HIGHEST)
    counts = jnp.where(counted, pixel[0], 1.0)
    centre_row = pixel[1] / counts
    centre_col = pixel[2] / counts
    distance = (row_pos - centre_row) * (row_pos - centre_row) + (col_pos - centre_col) * (
        col_pos - centre_col
    )
    heat = jnp.where(counted, jnp.exp(-distance / (2.0 * center_sigma * center_sigma)), 0.0)
    center_err = jnp.sum(jnp.square(predictions[0] - heat))
    offset_err = jnp.sum(
        jnp.where(
            counted,
            jnp.abs(predictions[1] - (centre_row - row_pos))
            + jnp.abs(predictions[2] - (centre_col - col_pos)),
            0.0,
        )
    )
    counted_local = jnp.sum(counted.astype(jnp.float32))
    local_totals = lax.optimization_barrier(jnp.stack([center_err, offset_err, counted_local]))
    totals = all_sum(local_totals, ("row", "tm"))
    center_total, offset_total, counted_total = totals[0], totals[1], totals[2]
    losses = jnp.stack(
        [
            center_total / (frame_count * height * columns),
            offset_weight * offset_total / jnp.maximum(counted_total, 1.0),
        ]
    )
    return (predictions[None], losses)


def solution(mesh):
    placed = (
        P(("grp", "tm"), None, "row", None),
        P("grp"),
        P(("grp", "tm"), "row", None),
        P(("grp", "tm"), "row", None),
        P(),
        P(),
        P(),
        P(),
        P(),
        P(),
    )
    return jax.shard_map(
        shards,
        mesh=mesh,
        in_specs=placed,
        out_specs=(P(("grp", "tm"), None, "row", None), P("grp")),
        check_vma=False,
    )
```

```python
import jax
import jax.numpy as jnp
from jax import lax
from jax.sharding import PartitionSpec as P
from jax.experimental import pallas as pl
from jax.experimental.pallas import tpu as pltpu

THING_FIRST = 11
INSTANCES = 64


DILATIONS = (6, 12, 18)
aspp_reach = 18
center_sigma = 8.0
offset_weight = 0.01


def padded_2(block, sides, width):
    for axis, dim in sides:
        count = lax.axis_size(axis)
        forward = [(i, i + 1) for i in range(count - 1)]
        backward = [(target, source) for source, target in forward]
        low = lax.ppermute(
            lax.slice_in_dim(block, block.shape[dim] - width, None, axis=dim), axis, forward
        )
        high = lax.ppermute(lax.slice_in_dim(block, 0, width, axis=dim), axis, backward)
        block = jnp.concatenate([low, block, high], axis=dim)
    return block


def with_rims(block, axis, dim, width):
    if lax.axis_size(axis) != 2:
        return padded_2(block, ((axis, dim),), width)
    first = lax.axis_index(axis) == 0
    size = block.shape[dim]
    sent = jnp.where(
        first,
        lax.slice_in_dim(block, size - width, None, axis=dim),
        lax.slice_in_dim(block, 0, width, axis=dim),
    )
    got = lax.ppermute(sent, axis, [(0, 1), (1, 0)])
    empty = jnp.zeros_like(got)
    low = jnp.where(first, empty, got)
    high = jnp.where(first, got, empty)
    return jnp.concatenate([low, block, high], axis=dim)


def shifted(value, axis, steps):
    count = lax.axis_size(axis)
    pairs = [(source, (source + steps) % count) for source in range(count)]
    return lax.ppermute(value, axis, pairs)


def all_sum(value, axes):
    for axis in axes:
        count = lax.axis_size(axis)
        if count & (count - 1):
            value = jax.tree.map(lambda v: lax.psum(v, axis), value)
            continue
        step = 1
        while step < count:
            pairs = [(i, i ^ step) for i in range(count)]
            other = lax.ppermute(value, axis, pairs)
            value = jax.tree.map(jnp.add, value, other)
            step *= 2
    return value


def aspp_pass(x, aspp_point, aspp_dilated, extra, geometry, part, finish):
    front, pitch, margin, block, blocks = geometry
    width = aspp_point.shape[0]
    channels = x.shape[1]
    lanes = pl.ds(part * channels, channels)
    contract = (((1,), (1,)), ((), ()))
    branches = 1 + len(DILATIONS)

    def body(x_ref, point_ref, dilated_ref, *rest):
        if finish:
            earlier_hbm, proj_ref, pool_ref, keep_ref, out_ref, earlier_ref, sems = rest
        else:
            out_hbm, out_ref, sems = rest

        def block_copy(index):
            rows = pl.ds(index * block, block)
            if finish:
                return pltpu.make_async_copy(
                    earlier_hbm.at[:, rows, :], earlier_ref.at[:, rows, :], sems.at[index]
                )
            return pltpu.make_async_copy(
                out_ref.at[:, rows, :], out_hbm.at[:, rows, :], sems.at[index]
            )

        if finish:
            for index in range(blocks):
                block_copy(index).start()
        for index in range(blocks):
            base = front + margin * pitch + index * block
            rows = pl.ds(index * block, block)
            if finish:
                block_copy(index).wait()

            def window(shift):
                return x_ref[pl.ds(base + shift, block), :]

            sums = [
                lax.dot_general(
                    window(0), point_ref[:, lanes], contract, preferred_element_type=jnp.float32
                )
            ]
            for branch, spread in enumerate(DILATIONS):
                total = None
                for vertical in range(3):
                    for lateral in range(3):
                        shift = (vertical - 1) * spread * pitch + (lateral - 1) * spread
                        term = lax.dot_general(
                            window(shift),
                            dilated_ref[branch, 3 * vertical + lateral, :, lanes],
                            contract,
                            preferred_element_type=jnp.float32,
                        )
                        total = term if total is None else total + term
                sums.append(total)
            if not finish:
                for branch, total in enumerate(sums):
                    out_ref[branch, rows, :] = total
                block_copy(index).start()
                continue
            mixed = None
            for branch, total in enumerate(sums):
                term = lax.dot_general(
                    relu_bf16(earlier_ref[branch, rows, :] + total),
                    proj_ref[:, branch * width : (branch + 1) * width],
                    contract,
                    preferred_element_type=jnp.float32,
                )
                mixed = term if mixed is None else mixed + term
            mixed = mixed + pool_ref[...]
            rounded = relu_bf16(mixed).astype(jnp.float32)
            out_ref[rows, :] = jnp.where(keep_ref[...] > 0.5, rounded, 0.0)
        if not finish:
            for index in range(blocks):
                block_copy(index).wait()

    taps = 1 + 9 * len(DILATIONS)
    flops = 2 * blocks * block * channels * width * taps
    sums_shape = (branches, blocks * block, width)
    vmem = pl.BlockSpec(memory_space=pltpu.VMEM)
    hbm = pl.BlockSpec(memory_space=pl.ANY)
    scratch = [pltpu.VMEM(sums_shape, jnp.float32), pltpu.SemaphoreType.DMA((blocks,))]
    if finish:
        flops += 2 * blocks * block * branches * width * width
        out_shape = jax.ShapeDtypeStruct((blocks * block, width), jnp.float32)
        in_specs = [vmem, vmem, vmem, hbm, vmem, vmem, vmem]
        out_specs = vmem
    else:
        out_shape = jax.ShapeDtypeStruct(sums_shape, jnp.float32)
        in_specs = [vmem, vmem, vmem]
        out_specs = hbm
    return pl.pallas_call(
        body,
        out_shape=out_shape,
        in_specs=in_specs,
        out_specs=out_specs,
        scratch_shapes=scratch,
        compiler_params=pltpu.CompilerParams(vmem_limit_bytes=56 * 1024 * 1024),
        cost_estimate=pl.CostEstimate(
            flops=flops,
            transcendentals=0,
            bytes_accessed=x.size * 2
            + aspp_dilated.size
            + branches * blocks * block * width * 4,
        ),
    )(x, aspp_point, aspp_dilated, *extra)


def head_kernel_call(x, head_weight, geometry):
    front, pitch, reach, block, blocks = geometry
    outputs = head_weight.shape[1]
    side = 2 * reach + 1
    contract = (((1,), (1,)), ((), ()))

    def body(x_ref, weight_ref, out_ref):
        for index in range(blocks):
            base = front + reach * pitch + index * block
            total = None
            for vertical in range(side):
                for lateral in range(side):
                    shift = (vertical - reach) * pitch + (lateral - reach)
                    term = lax.dot_general(
                        x_ref[pl.ds(base + shift, block), :].astype(jnp.bfloat16),
                        weight_ref[side * vertical + lateral],
                        contract,
                        preferred_element_type=jnp.float32,
                    )
                    total = term if total is None else total + term
            out_ref[pl.ds(index * block, block), :] = relu_bf16(total)

    return pl.pallas_call(
        body,
        out_shape=jax.ShapeDtypeStruct((blocks * block, outputs), jnp.bfloat16),
        compiler_params=pltpu.CompilerParams(vmem_limit_bytes=32 * 1024 * 1024),
        cost_estimate=pl.CostEstimate(
            flops=2 * blocks * block * x.shape[1] * outputs * side * side,
            transcendentals=0,
            bytes_accessed=x.size * 4 + head_weight.size * 2 + blocks * block * outputs * 2,
        ),
    )(x, head_weight)


def relu_bf16(values):
    return jnp.maximum(values, 0.0).astype(jnp.bfloat16)


def emit_heads(head_out, out_weight):
    groups = head_out.reshape(3, -1, head_out.shape[1], head_out.shape[2])
    center_map = jnp.einsum(
        "c,crw->rw", out_weight[0], groups[0], preferred_element_type=jnp.float32
    )
    offset_map = jnp.einsum(
        "oc,crw->orw", out_weight[1:3], groups[1], preferred_element_type=jnp.float32
    )
    depth_map = jnp.einsum(
        "c,crw->rw", out_weight[3], groups[2], preferred_element_type=jnp.float32
    )
    return jnp.concatenate([center_map[None], offset_map, depth_map[None]], 0)


def shards(
    frames,
    clip_start,
    semantic,
    instance,
    aspp_point,
    aspp_dilated,
    pool_weight,
    proj_weight,
    head_weight,
    out_weight,
):
    own_band = frames[0]
    channel_count, band_rows, columns = own_band.shape
    frame_count = clip_start.shape[0]
    height = band_rows * lax.axis_size("row")
    time_index = lax.axis_index("tm")
    row_index = lax.axis_index("row")
    ahead = (time_index + 1) % frame_count
    at_end = lax.dynamic_index_in_dim(clip_start, ahead, 0, keepdims=False) == 1
    later_band = jnp.where(at_end, own_band, shifted(own_band, "tm", -1))
    rim_rows = min(aspp_reach, band_rows)
    extra_rows = aspp_reach - rim_rows

    wide_rows = band_rows + 2 * aspp_reach
    pitch = -(-(columns + aspp_reach) // 16) * 16
    front = pitch
    block_rows = 8 if band_rows % 8 == 0 else band_rows
    block = block_rows * pitch
    blocks = band_rows // block_rows

    def flat_of(band):
        wide = jnp.pad(
            with_rims(band, "row", 1, rim_rows), ((0, 0), (extra_rows, extra_rows), (0, 0))
        )
        return jnp.pad(
            jnp.transpose(wide, (1, 2, 0)),
            ((1, 1), (pitch - columns, 0), (0, 0)),
        ).reshape((wide_rows + 2) * pitch, channel_count)

    geometry = (front, pitch, aspp_reach, block, blocks)
    own_sums = aspp_pass(
        flat_of(own_band), aspp_point, aspp_dilated, (), geometry, 0, False
    )

    counted = (semantic[0] >= THING_FIRST) & (instance[0] > 0)
    labels = jnp.arange(INSTANCES, dtype=jnp.int32)
    onehot = ((instance[0][None] == labels[:, None, None]) & counted[None]).astype(jnp.float32)
    row_pos = (row_index * band_rows + jnp.arange(band_rows, dtype=jnp.int32)).astype(jnp.float32)[
        :, None
    ] * jnp.ones((1, columns), jnp.float32)
    col_pos = jnp.arange(columns, dtype=jnp.float32)[None, :] * jnp.ones(
        (band_rows, 1), jnp.float32
    )
    local_stats = jnp.stack(
        [
            jnp.sum(onehot, axis=(1, 2)),
            jnp.sum(onehot * row_pos, axis=(1, 2)),
            jnp.sum(onehot * col_pos, axis=(1, 2)),
        ],
        0,
    )
    channel_sums = jnp.concatenate(
        [jnp.sum(band, axis=(1, 2), dtype=jnp.float32) for band in (own_band, later_band)]
    )
    frame_totals, inst_stats = all_sum((channel_sums, local_stats), ("row",))
    pooled = (frame_totals / (height * columns)).astype(jnp.bfloat16)
    pool_feature = relu_bf16(jnp.dot(pool_weight, pooled, preferred_element_type=jnp.float32))
    aspp_width = aspp_point.shape[0]
    pool_term = jnp.dot(
        proj_weight[:, 4 * aspp_width :], pool_feature, preferred_element_type=jnp.float32
    )[None]
    pad_columns = pitch - columns
    keep = (jnp.arange(block) % pitch >= pad_columns).astype(jnp.float32)[:, None]
    projected_flat = aspp_pass(
        flat_of(later_band),
        aspp_point,
        aspp_dilated,
        (own_sums, proj_weight, pool_term, keep),
        geometry,
        1,
        True,
    )
    head_reach = 2
    head_in = jnp.pad(
        with_rims(projected_flat, "row", 0, head_reach * pitch), ((pitch, pitch), (0, 0))
    )
    head_flat = head_kernel_call(head_in, head_weight, (pitch, pitch, head_reach, block, blocks))
    head_out = jnp.transpose(
        head_flat.reshape(band_rows, pitch, head_weight.shape[1])[:, pad_columns:], (2, 0, 1)
    )
    predictions = emit_heads(head_out, out_weight)
    pixel = jnp.einsum("sk,khw->shw", inst_stats, onehot, precision=lax.Precision.HIGHEST)
    counts = jnp.where(counted, pixel[0], 1.0)
    centre_row = pixel[1] / counts
    centre_col = pixel[2] / counts
    distance = (row_pos - centre_row) * (row_pos - centre_row) + (col_pos - centre_col) * (
        col_pos - centre_col
    )
    heat = jnp.where(counted, jnp.exp(-distance / (2.0 * center_sigma * center_sigma)), 0.0)
    center_err = jnp.sum(jnp.square(predictions[0] - heat))
    offset_err = jnp.sum(
        jnp.where(
            counted,
            jnp.abs(predictions[1] - (centre_row - row_pos))
            + jnp.abs(predictions[2] - (centre_col - col_pos)),
            0.0,
        )
    )
    counted_local = jnp.sum(counted.astype(jnp.float32))
    local_totals = lax.optimization_barrier(jnp.stack([center_err, offset_err, counted_local]))
    totals = all_sum(local_totals, ("row", "tm"))
    center_total, offset_total, counted_total = totals[0], totals[1], totals[2]
    losses = jnp.stack(
        [
            center_total / (frame_count * height * columns),
            offset_weight * offset_total / jnp.maximum(counted_total, 1.0),
        ]
    )
    return (predictions[None], losses)


def solution(mesh):
    placed = (
        P(("grp", "tm"), None, "row", None),
        P("grp"),
        P(("grp", "tm"), "row", None),
        P(("grp", "tm"), "row", None),
        P(),
        P(),
        P(),
        P(),
        P(),
        P(),
    )
    return jax.shard_map(
        shards,
        mesh=mesh,
        in_specs=placed,
        out_specs=(P(("grp", "tm"), None, "row", None), P("grp")),
        check_vma=False,
    )
```

```python
import jax
import jax.numpy as jnp
from jax import lax
from jax.sharding import PartitionSpec as P
from jax.experimental import pallas as pl
from jax.experimental.pallas import tpu as pltpu

THING_FIRST = 11
INSTANCES = 64


DILATIONS = (6, 12, 18)
aspp_reach = 18
center_sigma = 8.0
offset_weight = 0.01


def padded_2(block, sides, width):
    for axis, dim in sides:
        count = lax.axis_size(axis)
        forward = [(i, i + 1) for i in range(count - 1)]
        backward = [(target, source) for source, target in forward]
        low = lax.ppermute(
            lax.slice_in_dim(block, block.shape[dim] - width, None, axis=dim), axis, forward
        )
        high = lax.ppermute(lax.slice_in_dim(block, 0, width, axis=dim), axis, backward)
        block = jnp.concatenate([low, block, high], axis=dim)
    return block


def with_rims(block, axis, dim, width):
    if lax.axis_size(axis) != 2:
        return padded_2(block, ((axis, dim),), width)
    first = lax.axis_index(axis) == 0
    size = block.shape[dim]
    sent = jnp.where(
        first,
        lax.slice_in_dim(block, size - width, None, axis=dim),
        lax.slice_in_dim(block, 0, width, axis=dim),
    )
    got = lax.ppermute(sent, axis, [(0, 1), (1, 0)])
    empty = jnp.zeros_like(got)
    low = jnp.where(first, empty, got)
    high = jnp.where(first, got, empty)
    return jnp.concatenate([low, block, high], axis=dim)


def shifted(value, axis, steps):
    count = lax.axis_size(axis)
    pairs = [(source, (source + steps) % count) for source in range(count)]
    return lax.ppermute(value, axis, pairs)


def all_sum(value, axes):
    for axis in axes:
        count = lax.axis_size(axis)
        if count & (count - 1):
            value = jax.tree.map(lambda v: lax.psum(v, axis), value)
            continue
        step = 1
        while step < count:
            pairs = [(i, i ^ step) for i in range(count)]
            other = lax.ppermute(value, axis, pairs)
            value = jax.tree.map(jnp.add, value, other)
            step *= 2
    return value


def aspp_pass(x, aspp_point, aspp_dilated, extra, geometry, part, finish):
    front, pitch, margin, block, blocks = geometry
    width = aspp_point.shape[0]
    channels = x.shape[1]
    lanes = pl.ds(part * channels, channels)
    contract = (((1,), (1,)), ((), ()))
    branches = 1 + len(DILATIONS)

    def body(x_ref, point_ref, dilated_ref, *rest):
        if finish:
            earlier_hbm, proj_ref, pool_ref, keep_ref, out_ref, earlier_ref, sems = rest
        else:
            out_hbm, out_ref, sems = rest

        def block_copy(index):
            rows = pl.ds(index * block, block)
            if finish:
                return pltpu.make_async_copy(
                    earlier_hbm.at[:, rows, :], earlier_ref.at[:, rows, :], sems.at[index]
                )
            return pltpu.make_async_copy(
                out_ref.at[:, rows, :], out_hbm.at[:, rows, :], sems.at[index]
            )

        ahead = 2
        if finish:
            for index in range(min(ahead, blocks)):
                block_copy(index).start()
        for index in range(blocks):
            base = front + margin * pitch + index * block
            rows = pl.ds(index * block, block)
            if finish:
                block_copy(index).wait()
                if index + ahead < blocks:
                    block_copy(index + ahead).start()

            def window(shift):
                return x_ref[pl.ds(base + shift, block), :]

            sums = [
                lax.dot_general(
                    window(0), point_ref[:, lanes], contract, preferred_element_type=jnp.float32
                )
            ]
            for branch, spread in enumerate(DILATIONS):
                total = None
                for vertical in range(3):
                    for lateral in range(3):
                        shift = (vertical - 1) * spread * pitch + (lateral - 1) * spread
                        term = lax.dot_general(
                            window(shift),
                            dilated_ref[branch, 3 * vertical + lateral, :, lanes],
                            contract,
                            preferred_element_type=jnp.float32,
                        )
                        total = term if total is None else total + term
                sums.append(total)
            if not finish:
                for branch, total in enumerate(sums):
                    out_ref[branch, rows, :] = total
                block_copy(index).start()
                continue
            mixed = None
            for branch, total in enumerate(sums):
                term = lax.dot_general(
                    relu_bf16(earlier_ref[branch, rows, :] + total),
                    proj_ref[:, branch * width : (branch + 1) * width],
                    contract,
                    preferred_element_type=jnp.float32,
                )
                mixed = term if mixed is None else mixed + term
            mixed = mixed + pool_ref[...]
            rounded = relu_bf16(mixed).astype(jnp.float32)
            out_ref[rows, :] = jnp.where(keep_ref[...] > 0.5, rounded, 0.0)
        if not finish:
            for index in range(blocks):
                block_copy(index).wait()

    taps = 1 + 9 * len(DILATIONS)
    flops = 2 * blocks * block * channels * width * taps
    sums_shape = (branches, blocks * block, width)
    vmem = pl.BlockSpec(memory_space=pltpu.VMEM)
    hbm = pl.BlockSpec(memory_space=pl.ANY)
    scratch = [pltpu.VMEM(sums_shape, jnp.float32), pltpu.SemaphoreType.DMA((blocks,))]
    if finish:
        flops += 2 * blocks * block * branches * width * width
        out_shape = jax.ShapeDtypeStruct((blocks * block, width), jnp.float32)
        in_specs = [vmem, vmem, vmem, hbm, vmem, vmem, vmem]
        out_specs = vmem
    else:
        out_shape = jax.ShapeDtypeStruct(sums_shape, jnp.float32)
        in_specs = [vmem, vmem, vmem]
        out_specs = hbm
    return pl.pallas_call(
        body,
        out_shape=out_shape,
        in_specs=in_specs,
        out_specs=out_specs,
        scratch_shapes=scratch,
        compiler_params=pltpu.CompilerParams(vmem_limit_bytes=56 * 1024 * 1024),
        cost_estimate=pl.CostEstimate(
            flops=flops,
            transcendentals=0,
            bytes_accessed=x.size * 2
            + aspp_dilated.size
            + branches * blocks * block * width * 4,
        ),
    )(x, aspp_point, aspp_dilated, *extra)


def head_kernel_call(x, head_weight, geometry):
    front, pitch, reach, block, blocks = geometry
    outputs = head_weight.shape[1]
    side = 2 * reach + 1
    contract = (((1,), (1,)), ((), ()))

    def body(x_ref, weight_ref, out_ref):
        for index in range(blocks):
            base = front + reach * pitch + index * block
            total = None
            for vertical in range(side):
                for lateral in range(side):
                    shift = (vertical - reach) * pitch + (lateral - reach)
                    term = lax.dot_general(
                        x_ref[pl.ds(base + shift, block), :].astype(jnp.bfloat16),
                        weight_ref[side * vertical + lateral],
                        contract,
                        preferred_element_type=jnp.float32,
                    )
                    total = term if total is None else total + term
            out_ref[pl.ds(index * block, block), :] = relu_bf16(total)

    return pl.pallas_call(
        body,
        out_shape=jax.ShapeDtypeStruct((blocks * block, outputs), jnp.bfloat16),
        compiler_params=pltpu.CompilerParams(vmem_limit_bytes=32 * 1024 * 1024),
        cost_estimate=pl.CostEstimate(
            flops=2 * blocks * block * x.shape[1] * outputs * side * side,
            transcendentals=0,
            bytes_accessed=x.size * 4 + head_weight.size * 2 + blocks * block * outputs * 2,
        ),
    )(x, head_weight)


def relu_bf16(values):
    return jnp.maximum(values, 0.0).astype(jnp.bfloat16)


def emit_heads(head_out, out_weight):
    groups = head_out.reshape(3, -1, head_out.shape[1], head_out.shape[2])
    center_map = jnp.einsum(
        "c,crw->rw", out_weight[0], groups[0], preferred_element_type=jnp.float32
    )
    offset_map = jnp.einsum(
        "oc,crw->orw", out_weight[1:3], groups[1], preferred_element_type=jnp.float32
    )
    depth_map = jnp.einsum(
        "c,crw->rw", out_weight[3], groups[2], preferred_element_type=jnp.float32
    )
    return jnp.concatenate([center_map[None], offset_map, depth_map[None]], 0)


def shards(
    frames,
    clip_start,
    semantic,
    instance,
    aspp_point,
    aspp_dilated,
    pool_weight,
    proj_weight,
    head_weight,
    out_weight,
):
    own_band = frames[0]
    channel_count, band_rows, columns = own_band.shape
    frame_count = clip_start.shape[0]
    height = band_rows * lax.axis_size("row")
    time_index = lax.axis_index("tm")
    row_index = lax.axis_index("row")
    ahead = (time_index + 1) % frame_count
    at_end = lax.dynamic_index_in_dim(clip_start, ahead, 0, keepdims=False) == 1
    later_band = jnp.where(at_end, own_band, shifted(own_band, "tm", -1))
    rim_rows = min(aspp_reach, band_rows)
    extra_rows = aspp_reach - rim_rows

    wide_rows = band_rows + 2 * aspp_reach
    pitch = -(-(columns + aspp_reach) // 16) * 16
    front = pitch
    block_rows = 8 if band_rows % 8 == 0 else band_rows
    block = block_rows * pitch
    blocks = band_rows // block_rows

    def flat_of(band):
        wide = jnp.pad(
            with_rims(band, "row", 1, rim_rows), ((0, 0), (extra_rows, extra_rows), (0, 0))
        )
        return jnp.pad(
            jnp.transpose(wide, (1, 2, 0)),
            ((1, 1), (pitch - columns, 0), (0, 0)),
        ).reshape((wide_rows + 2) * pitch, channel_count)

    geometry = (front, pitch, aspp_reach, block, blocks)
    own_sums = aspp_pass(
        flat_of(own_band), aspp_point, aspp_dilated, (), geometry, 0, False
    )

    counted = (semantic[0] >= THING_FIRST) & (instance[0] > 0)
    labels = jnp.arange(INSTANCES, dtype=jnp.int32)
    onehot = ((instance[0][None] == labels[:, None, None]) & counted[None]).astype(jnp.float32)
    row_pos = (row_index * band_rows + jnp.arange(band_rows, dtype=jnp.int32)).astype(jnp.float32)[
        :, None
    ] * jnp.ones((1, columns), jnp.float32)
    col_pos = jnp.arange(columns, dtype=jnp.float32)[None, :] * jnp.ones(
        (band_rows, 1), jnp.float32
    )
    local_stats = jnp.stack(
        [
            jnp.sum(onehot, axis=(1, 2)),
            jnp.sum(onehot * row_pos, axis=(1, 2)),
            jnp.sum(onehot * col_pos, axis=(1, 2)),
        ],
        0,
    )
    channel_sums = jnp.concatenate(
        [jnp.sum(band, axis=(1, 2), dtype=jnp.float32) for band in (own_band, later_band)]
    )
    frame_totals, inst_stats = all_sum((channel_sums, local_stats), ("row",))
    pooled = (frame_totals / (height * columns)).astype(jnp.bfloat16)
    pool_feature = relu_bf16(jnp.dot(pool_weight, pooled, preferred_element_type=jnp.float32))
    aspp_width = aspp_point.shape[0]
    pool_term = jnp.dot(
        proj_weight[:, 4 * aspp_width :], pool_feature, preferred_element_type=jnp.float32
    )[None]
    pad_columns = pitch - columns
    keep = (jnp.arange(block) % pitch >= pad_columns).astype(jnp.float32)[:, None]
    projected_flat = aspp_pass(
        flat_of(later_band),
        aspp_point,
        aspp_dilated,
        (own_sums, proj_weight, pool_term, keep),
        geometry,
        1,
        True,
    )
    head_reach = 2
    head_in = jnp.pad(
        with_rims(projected_flat, "row", 0, head_reach * pitch), ((pitch, pitch), (0, 0))
    )
    head_flat = head_kernel_call(head_in, head_weight, (pitch, pitch, head_reach, block, blocks))
    head_out = jnp.transpose(
        head_flat.reshape(band_rows, pitch, head_weight.shape[1])[:, pad_columns:], (2, 0, 1)
    )
    predictions = emit_heads(head_out, out_weight)
    pixel = jnp.einsum("sk,khw->shw", inst_stats, onehot, precision=lax.Precision.HIGHEST)
    counts = jnp.where(counted, pixel[0], 1.0)
    centre_row = pixel[1] / counts
    centre_col = pixel[2] / counts
    distance = (row_pos - centre_row) * (row_pos - centre_row) + (col_pos - centre_col) * (
        col_pos - centre_col
    )
    heat = jnp.where(counted, jnp.exp(-distance / (2.0 * center_sigma * center_sigma)), 0.0)
    center_err = jnp.sum(jnp.square(predictions[0] - heat))
    offset_err = jnp.sum(
        jnp.where(
            counted,
            jnp.abs(predictions[1] - (centre_row - row_pos))
            + jnp.abs(predictions[2] - (centre_col - col_pos)),
            0.0,
        )
    )
    counted_local = jnp.sum(counted.astype(jnp.float32))
    local_totals = lax.optimization_barrier(jnp.stack([center_err, offset_err, counted_local]))
    totals = all_sum(local_totals, ("row", "tm"))
    center_total, offset_total, counted_total = totals[0], totals[1], totals[2]
    losses = jnp.stack(
        [
            center_total / (frame_count * height * columns),
            offset_weight * offset_total / jnp.maximum(counted_total, 1.0),
        ]
    )
    return (predictions[None], losses)


def solution(mesh):
    placed = (
        P(("grp", "tm"), None, "row", None),
        P("grp"),
        P(("grp", "tm"), "row", None),
        P(("grp", "tm"), "row", None),
        P(),
        P(),
        P(),
        P(),
        P(),
        P(),
    )
    return jax.shard_map(
        shards,
        mesh=mesh,
        in_specs=placed,
        out_specs=(P(("grp", "tm"), None, "row", None), P("grp")),
        check_vma=False,
    )
```

```python
import jax
import jax.numpy as jnp
from jax import lax
from jax.sharding import PartitionSpec as P
from jax.experimental import pallas as pl
from jax.experimental.pallas import tpu as pltpu

THING_FIRST = 11
INSTANCES = 64


DILATIONS = (6, 12, 18)
aspp_reach = 18
center_sigma = 8.0
offset_weight = 0.01


def padded_2(block, sides, width):
    for axis, dim in sides:
        count = lax.axis_size(axis)
        forward = [(i, i + 1) for i in range(count - 1)]
        backward = [(target, source) for source, target in forward]
        low = lax.ppermute(
            lax.slice_in_dim(block, block.shape[dim] - width, None, axis=dim), axis, forward
        )
        high = lax.ppermute(lax.slice_in_dim(block, 0, width, axis=dim), axis, backward)
        block = jnp.concatenate([low, block, high], axis=dim)
    return block


def with_rims(block, axis, dim, width):
    if lax.axis_size(axis) != 2:
        return padded_2(block, ((axis, dim),), width)
    first = lax.axis_index(axis) == 0
    size = block.shape[dim]
    sent = jnp.where(
        first,
        lax.slice_in_dim(block, size - width, None, axis=dim),
        lax.slice_in_dim(block, 0, width, axis=dim),
    )
    got = lax.ppermute(sent, axis, [(0, 1), (1, 0)])
    empty = jnp.zeros_like(got)
    low = jnp.where(first, empty, got)
    high = jnp.where(first, got, empty)
    return jnp.concatenate([low, block, high], axis=dim)


def shifted(value, axis, steps):
    count = lax.axis_size(axis)
    pairs = [(source, (source + steps) % count) for source in range(count)]
    return lax.ppermute(value, axis, pairs)


def all_sum(value, axes):
    for axis in axes:
        count = lax.axis_size(axis)
        if count & (count - 1):
            value = jax.tree.map(lambda v: lax.psum(v, axis), value)
            continue
        step = 1
        while step < count:
            pairs = [(i, i ^ step) for i in range(count)]
            other = lax.ppermute(value, axis, pairs)
            value = jax.tree.map(jnp.add, value, other)
            step *= 2
    return value


def aspp_pass(x, aspp_point, aspp_dilated, extra, geometry, part, finish):
    front, pitch, margin, block, blocks = geometry
    width = aspp_point.shape[0]
    channels = x.shape[1]
    lanes = pl.ds(part * channels, channels)
    contract = (((1,), (1,)), ((), ()))
    branches = 1 + len(DILATIONS)

    def body(x_ref, point_ref, dilated_ref, *rest):
        if finish:
            earlier_hbm, proj_ref, pool_ref, keep_ref, out_ref, earlier_ref, sems = rest
        else:
            out_hbm, out_ref, sems = rest

        def block_copy(index):
            rows = pl.ds(index * block, block)
            if finish:
                return pltpu.make_async_copy(
                    earlier_hbm.at[:, rows, :], earlier_ref.at[:, rows, :], sems.at[index]
                )
            return pltpu.make_async_copy(
                out_ref.at[:, rows, :], out_hbm.at[:, rows, :], sems.at[index]
            )

        ahead = 2
        if finish:
            for index in range(min(ahead, blocks)):
                block_copy(index).start()
        for index in range(blocks):
            base = front + margin * pitch + index * block
            rows = pl.ds(index * block, block)
            if finish:
                block_copy(index).wait()
                if index + ahead < blocks:
                    block_copy(index + ahead).start()

            def window(shift):
                return x_ref[pl.ds(base + shift, block), :]

            state = {"mixed": None}

            def consume(branch, total):
                if not finish:
                    out_ref[branch, rows, :] = total
                    return
                term = lax.dot_general(
                    relu_bf16(earlier_ref[branch, rows, :] + total),
                    proj_ref[:, branch * width : (branch + 1) * width],
                    contract,
                    preferred_element_type=jnp.float32,
                )
                mixed = state["mixed"]
                state["mixed"] = term if mixed is None else mixed + term

            consume(
                0,
                lax.dot_general(
                    window(0), point_ref[:, lanes], contract, preferred_element_type=jnp.float32
                ),
            )
            for branch, spread in enumerate(DILATIONS):
                total = None
                for vertical in range(3):
                    for lateral in range(3):
                        shift = (vertical - 1) * spread * pitch + (lateral - 1) * spread
                        term = lax.dot_general(
                            window(shift),
                            dilated_ref[branch, 3 * vertical + lateral, :, lanes],
                            contract,
                            preferred_element_type=jnp.float32,
                        )
                        total = term if total is None else total + term
                consume(branch + 1, total)
            if not finish:
                block_copy(index).start()
                continue
            mixed = state["mixed"]
            mixed = mixed + pool_ref[...]
            rounded = relu_bf16(mixed).astype(jnp.float32)
            out_ref[rows, :] = jnp.where(keep_ref[...] > 0.5, rounded, 0.0)
        if not finish:
            for index in range(blocks):
                block_copy(index).wait()

    taps = 1 + 9 * len(DILATIONS)
    flops = 2 * blocks * block * channels * width * taps
    sums_shape = (branches, blocks * block, width)
    vmem = pl.BlockSpec(memory_space=pltpu.VMEM)
    hbm = pl.BlockSpec(memory_space=pl.ANY)
    scratch = [pltpu.VMEM(sums_shape, jnp.float32), pltpu.SemaphoreType.DMA((blocks,))]
    if finish:
        flops += 2 * blocks * block * branches * width * width
        out_shape = jax.ShapeDtypeStruct((blocks * block, width), jnp.float32)
        in_specs = [vmem, vmem, vmem, hbm, vmem, vmem, vmem]
        out_specs = vmem
    else:
        out_shape = jax.ShapeDtypeStruct(sums_shape, jnp.float32)
        in_specs = [vmem, vmem, vmem]
        out_specs = hbm
    return pl.pallas_call(
        body,
        out_shape=out_shape,
        in_specs=in_specs,
        out_specs=out_specs,
        scratch_shapes=scratch,
        compiler_params=pltpu.CompilerParams(vmem_limit_bytes=56 * 1024 * 1024),
        cost_estimate=pl.CostEstimate(
            flops=flops,
            transcendentals=0,
            bytes_accessed=x.size * 2
            + aspp_dilated.size
            + branches * blocks * block * width * 4,
        ),
    )(x, aspp_point, aspp_dilated, *extra)


def head_kernel_call(x, head_weight, geometry):
    front, pitch, reach, block, blocks = geometry
    outputs = head_weight.shape[1]
    side = 2 * reach + 1
    contract = (((1,), (1,)), ((), ()))

    def body(x_ref, weight_ref, out_ref):
        for index in range(blocks):
            base = front + reach * pitch + index * block
            total = None
            for vertical in range(side):
                for lateral in range(side):
                    shift = (vertical - reach) * pitch + (lateral - reach)
                    term = lax.dot_general(
                        x_ref[pl.ds(base + shift, block), :].astype(jnp.bfloat16),
                        weight_ref[side * vertical + lateral],
                        contract,
                        preferred_element_type=jnp.float32,
                    )
                    total = term if total is None else total + term
            out_ref[pl.ds(index * block, block), :] = relu_bf16(total)

    return pl.pallas_call(
        body,
        out_shape=jax.ShapeDtypeStruct((blocks * block, outputs), jnp.bfloat16),
        compiler_params=pltpu.CompilerParams(vmem_limit_bytes=32 * 1024 * 1024),
        cost_estimate=pl.CostEstimate(
            flops=2 * blocks * block * x.shape[1] * outputs * side * side,
            transcendentals=0,
            bytes_accessed=x.size * 4 + head_weight.size * 2 + blocks * block * outputs * 2,
        ),
    )(x, head_weight)


def relu_bf16(values):
    return jnp.maximum(values, 0.0).astype(jnp.bfloat16)


def emit_heads(head_out, out_weight):
    groups = head_out.reshape(3, -1, head_out.shape[1], head_out.shape[2])
    center_map = jnp.einsum(
        "c,crw->rw", out_weight[0], groups[0], preferred_element_type=jnp.float32
    )
    offset_map = jnp.einsum(
        "oc,crw->orw", out_weight[1:3], groups[1], preferred_element_type=jnp.float32
    )
    depth_map = jnp.einsum(
        "c,crw->rw", out_weight[3], groups[2], preferred_element_type=jnp.float32
    )
    return jnp.concatenate([center_map[None], offset_map, depth_map[None]], 0)


def shards(
    frames,
    clip_start,
    semantic,
    instance,
    aspp_point,
    aspp_dilated,
    pool_weight,
    proj_weight,
    head_weight,
    out_weight,
):
    own_band = frames[0]
    channel_count, band_rows, columns = own_band.shape
    frame_count = clip_start.shape[0]
    height = band_rows * lax.axis_size("row")
    time_index = lax.axis_index("tm")
    row_index = lax.axis_index("row")
    ahead = (time_index + 1) % frame_count
    at_end = lax.dynamic_index_in_dim(clip_start, ahead, 0, keepdims=False) == 1
    later_band = jnp.where(at_end, own_band, shifted(own_band, "tm", -1))
    rim_rows = min(aspp_reach, band_rows)
    extra_rows = aspp_reach - rim_rows

    wide_rows = band_rows + 2 * aspp_reach
    pitch = -(-(columns + aspp_reach) // 16) * 16
    front = pitch
    block_rows = 8 if band_rows % 8 == 0 else band_rows
    block = block_rows * pitch
    blocks = band_rows // block_rows

    def flat_of(band):
        wide = jnp.pad(
            with_rims(band, "row", 1, rim_rows), ((0, 0), (extra_rows, extra_rows), (0, 0))
        )
        return jnp.pad(
            jnp.transpose(wide, (1, 2, 0)),
            ((1, 1), (pitch - columns, 0), (0, 0)),
        ).reshape((wide_rows + 2) * pitch, channel_count)

    geometry = (front, pitch, aspp_reach, block, blocks)
    own_sums = aspp_pass(
        flat_of(own_band), aspp_point, aspp_dilated, (), geometry, 0, False
    )

    counted = (semantic[0] >= THING_FIRST) & (instance[0] > 0)
    labels = jnp.arange(INSTANCES, dtype=jnp.int32)
    onehot = ((instance[0][None] == labels[:, None, None]) & counted[None]).astype(jnp.float32)
    row_pos = (row_index * band_rows + jnp.arange(band_rows, dtype=jnp.int32)).astype(jnp.float32)[
        :, None
    ] * jnp.ones((1, columns), jnp.float32)
    col_pos = jnp.arange(columns, dtype=jnp.float32)[None, :] * jnp.ones(
        (band_rows, 1), jnp.float32
    )
    local_stats = jnp.stack(
        [
            jnp.sum(onehot, axis=(1, 2)),
            jnp.sum(onehot * row_pos, axis=(1, 2)),
            jnp.sum(onehot * col_pos, axis=(1, 2)),
        ],
        0,
    )
    channel_sums = jnp.concatenate(
        [jnp.sum(band, axis=(1, 2), dtype=jnp.float32) for band in (own_band, later_band)]
    )
    frame_totals, inst_stats = all_sum((channel_sums, local_stats), ("row",))
    pooled = (frame_totals / (height * columns)).astype(jnp.bfloat16)
    pool_feature = relu_bf16(jnp.dot(pool_weight, pooled, preferred_element_type=jnp.float32))
    aspp_width = aspp_point.shape[0]
    pool_term = jnp.dot(
        proj_weight[:, 4 * aspp_width :], pool_feature, preferred_element_type=jnp.float32
    )[None]
    pad_columns = pitch - columns
    keep = (jnp.arange(block) % pitch >= pad_columns).astype(jnp.float32)[:, None]
    projected_flat = aspp_pass(
        flat_of(later_band),
        aspp_point,
        aspp_dilated,
        (own_sums, proj_weight, pool_term, keep),
        geometry,
        1,
        True,
    )
    head_reach = 2
    head_in = jnp.pad(
        with_rims(projected_flat, "row", 0, head_reach * pitch), ((pitch, pitch), (0, 0))
    )
    head_flat = head_kernel_call(head_in, head_weight, (pitch, pitch, head_reach, block, blocks))
    head_out = jnp.transpose(
        head_flat.reshape(band_rows, pitch, head_weight.shape[1])[:, pad_columns:], (2, 0, 1)
    )
    predictions = emit_heads(head_out, out_weight)
    pixel = jnp.einsum("sk,khw->shw", inst_stats, onehot, precision=lax.Precision.HIGHEST)
    counts = jnp.where(counted, pixel[0], 1.0)
    centre_row = pixel[1] / counts
    centre_col = pixel[2] / counts
    distance = (row_pos - centre_row) * (row_pos - centre_row) + (col_pos - centre_col) * (
        col_pos - centre_col
    )
    heat = jnp.where(counted, jnp.exp(-distance / (2.0 * center_sigma * center_sigma)), 0.0)
    center_err = jnp.sum(jnp.square(predictions[0] - heat))
    offset_err = jnp.sum(
        jnp.where(
            counted,
            jnp.abs(predictions[1] - (centre_row - row_pos))
            + jnp.abs(predictions[2] - (centre_col - col_pos)),
            0.0,
        )
    )
    counted_local = jnp.sum(counted.astype(jnp.float32))
    local_totals = lax.optimization_barrier(jnp.stack([center_err, offset_err, counted_local]))
    totals = all_sum(local_totals, ("row", "tm"))
    center_total, offset_total, counted_total = totals[0], totals[1], totals[2]
    losses = jnp.stack(
        [
            center_total / (frame_count * height * columns),
            offset_weight * offset_total / jnp.maximum(counted_total, 1.0),
        ]
    )
    return (predictions[None], losses)


def solution(mesh):
    placed = (
        P(("grp", "tm"), None, "row", None),
        P("grp"),
        P(("grp", "tm"), "row", None),
        P(("grp", "tm"), "row", None),
        P(),
        P(),
        P(),
        P(),
        P(),
        P(),
    )
    return jax.shard_map(
        shards,
        mesh=mesh,
        in_specs=placed,
        out_specs=(P(("grp", "tm"), None, "row", None), P("grp")),
        check_vma=False,
    )
```

```python
import jax
import jax.numpy as jnp
from jax import lax
from jax.sharding import PartitionSpec as P
from jax.experimental import pallas as pl
from jax.experimental.pallas import tpu as pltpu

THING_FIRST = 11
INSTANCES = 64


DILATIONS = (6, 12, 18)
aspp_reach = 18
center_sigma = 8.0
offset_weight = 0.01


def padded_2(block, sides, width):
    for axis, dim in sides:
        count = lax.axis_size(axis)
        forward = [(i, i + 1) for i in range(count - 1)]
        backward = [(target, source) for source, target in forward]
        low = lax.ppermute(
            lax.slice_in_dim(block, block.shape[dim] - width, None, axis=dim), axis, forward
        )
        high = lax.ppermute(lax.slice_in_dim(block, 0, width, axis=dim), axis, backward)
        block = jnp.concatenate([low, block, high], axis=dim)
    return block


def with_rims(block, axis, dim, width):
    if lax.axis_size(axis) != 2:
        return padded_2(block, ((axis, dim),), width)
    first = lax.axis_index(axis) == 0
    size = block.shape[dim]
    sent = jnp.where(
        first,
        lax.slice_in_dim(block, size - width, None, axis=dim),
        lax.slice_in_dim(block, 0, width, axis=dim),
    )
    got = lax.ppermute(sent, axis, [(0, 1), (1, 0)])
    empty = jnp.zeros_like(got)
    low = jnp.where(first, empty, got)
    high = jnp.where(first, got, empty)
    return jnp.concatenate([low, block, high], axis=dim)


def shifted(value, axis, steps):
    count = lax.axis_size(axis)
    pairs = [(source, (source + steps) % count) for source in range(count)]
    return lax.ppermute(value, axis, pairs)


def all_sum(value, axes):
    for axis in axes:
        count = lax.axis_size(axis)
        if count & (count - 1):
            value = jax.tree.map(lambda v: lax.psum(v, axis), value)
            continue
        step = 1
        while step < count:
            pairs = [(i, i ^ step) for i in range(count)]
            other = lax.ppermute(value, axis, pairs)
            value = jax.tree.map(jnp.add, value, other)
            step *= 2
    return value


def aspp_pass(x, aspp_point, aspp_dilated, extra, geometry, part, finish):
    front, pitch, margin, block, blocks = geometry
    width = aspp_point.shape[0]
    channels = x.shape[1]
    lanes = pl.ds(part * channels, channels)
    contract = (((1,), (1,)), ((), ()))
    branches = 1 + len(DILATIONS)

    def body(x_ref, point_ref, dilated_ref, *rest):
        if finish:
            earlier_hbm, proj_ref, pool_ref, keep_ref, out_ref, earlier_ref, sems = rest
        else:
            out_hbm, out_ref, sems = rest

        def block_copy(index):
            rows = pl.ds(index * block, block)
            if finish:
                return pltpu.make_async_copy(
                    earlier_hbm.at[:, rows, :], earlier_ref.at[:, rows, :], sems.at[index]
                )
            return pltpu.make_async_copy(
                out_ref.at[:, rows, :], out_hbm.at[:, rows, :], sems.at[index]
            )

        if finish:
            for index in range(blocks):
                block_copy(index).start()
        for index in range(blocks):
            base = front + margin * pitch + index * block
            rows = pl.ds(index * block, block)
            if finish:
                block_copy(index).wait()

            def window(shift):
                return x_ref[pl.ds(base + shift, block), :]

            sums = [
                lax.dot_general(
                    window(0), point_ref[:, lanes], contract, preferred_element_type=jnp.float32
                )
            ]
            for branch, spread in enumerate(DILATIONS):
                total = None
                for vertical in range(3):
                    for lateral in range(3):
                        shift = (vertical - 1) * spread * pitch + (lateral - 1) * spread
                        term = lax.dot_general(
                            window(shift),
                            dilated_ref[branch, 3 * vertical + lateral, :, lanes],
                            contract,
                            preferred_element_type=jnp.float32,
                        )
                        total = term if total is None else total + term
                sums.append(total)
            if not finish:
                for branch, total in enumerate(sums):
                    out_ref[branch, rows, :] = total
                block_copy(index).start()
                continue
            mixed = None
            for branch, total in enumerate(sums):
                term = lax.dot_general(
                    relu_bf16(earlier_ref[branch, rows, :] + total),
                    proj_ref[:, branch * width : (branch + 1) * width],
                    contract,
                    preferred_element_type=jnp.float32,
                )
                mixed = term if mixed is None else mixed + term
            mixed = mixed + pool_ref[...]
            rounded = relu_bf16(mixed).astype(jnp.float32)
            out_ref[rows, :] = jnp.where(keep_ref[...] > 0.5, rounded, 0.0)
        if not finish:
            for index in range(blocks):
                block_copy(index).wait()

    taps = 1 + 9 * len(DILATIONS)
    flops = 2 * blocks * block * channels * width * taps
    sums_shape = (branches, blocks * block, width)
    vmem = pl.BlockSpec(memory_space=pltpu.VMEM)
    hbm = pl.BlockSpec(memory_space=pl.ANY)
    scratch = [pltpu.VMEM(sums_shape, jnp.float32), pltpu.SemaphoreType.DMA((blocks,))]
    if finish:
        flops += 2 * blocks * block * branches * width * width
        out_shape = jax.ShapeDtypeStruct((blocks * block, width), jnp.float32)
        in_specs = [vmem, vmem, vmem, hbm, vmem, vmem, vmem]
        out_specs = vmem
    else:
        out_shape = jax.ShapeDtypeStruct(sums_shape, jnp.float32)
        in_specs = [vmem, vmem, vmem]
        out_specs = hbm
    return pl.pallas_call(
        body,
        out_shape=out_shape,
        in_specs=in_specs,
        out_specs=out_specs,
        scratch_shapes=scratch,
        compiler_params=pltpu.CompilerParams(vmem_limit_bytes=56 * 1024 * 1024),
        cost_estimate=pl.CostEstimate(
            flops=flops,
            transcendentals=0,
            bytes_accessed=x.size * 2
            + aspp_dilated.size
            + branches * blocks * block * width * 4,
        ),
    )(x, aspp_point, aspp_dilated, *extra)


def head_kernel_call(x, head_weight, geometry):
    front, pitch, reach, block, blocks = geometry
    outputs = head_weight.shape[1]
    side = 2 * reach + 1
    contract = (((1,), (1,)), ((), ()))

    def body(x_ref, weight_ref, out_ref):
        for index in range(blocks):
            base = front + reach * pitch + index * block
            total = None
            for vertical in range(side):
                for lateral in range(side):
                    shift = (vertical - reach) * pitch + (lateral - reach)
                    term = lax.dot_general(
                        x_ref[pl.ds(base + shift, block), :].astype(jnp.bfloat16),
                        weight_ref[side * vertical + lateral],
                        contract,
                        preferred_element_type=jnp.float32,
                    )
                    total = term if total is None else total + term
            out_ref[pl.ds(index * block, block), :] = relu_bf16(total)

    return pl.pallas_call(
        body,
        out_shape=jax.ShapeDtypeStruct((blocks * block, outputs), jnp.bfloat16),
        compiler_params=pltpu.CompilerParams(vmem_limit_bytes=32 * 1024 * 1024),
        cost_estimate=pl.CostEstimate(
            flops=2 * blocks * block * x.shape[1] * outputs * side * side,
            transcendentals=0,
            bytes_accessed=x.size * 4 + head_weight.size * 2 + blocks * block * outputs * 2,
        ),
    )(x, head_weight)


def relu_bf16(values):
    return jnp.maximum(values, 0.0).astype(jnp.bfloat16)


def emit_heads(head_out, out_weight):
    groups = head_out.reshape(3, -1, head_out.shape[1], head_out.shape[2])
    center_map = jnp.einsum(
        "c,crw->rw", out_weight[0], groups[0], preferred_element_type=jnp.float32
    )
    offset_map = jnp.einsum(
        "oc,crw->orw", out_weight[1:3], groups[1], preferred_element_type=jnp.float32
    )
    depth_map = jnp.einsum(
        "c,crw->rw", out_weight[3], groups[2], preferred_element_type=jnp.float32
    )
    return jnp.concatenate([center_map[None], offset_map, depth_map[None]], 0)


def shards(
    frames,
    clip_start,
    semantic,
    instance,
    aspp_point,
    aspp_dilated,
    pool_weight,
    proj_weight,
    head_weight,
    out_weight,
):
    own_band = frames[0]
    channel_count, band_rows, columns = own_band.shape
    frame_count = clip_start.shape[0]
    height = band_rows * lax.axis_size("row")
    time_index = lax.axis_index("tm")
    row_index = lax.axis_index("row")
    ahead = (time_index + 1) % frame_count
    at_end = jnp.sum(jnp.where(jnp.arange(frame_count) == ahead, clip_start, 0)) == 1
    later_band = jnp.where(at_end, own_band, shifted(own_band, "tm", -1))
    rim_rows = min(aspp_reach, band_rows)
    extra_rows = aspp_reach - rim_rows

    wide_rows = band_rows + 2 * aspp_reach
    pitch = -(-(columns + aspp_reach) // 16) * 16
    front = pitch
    block_rows = 8 if band_rows % 8 == 0 else band_rows
    block = block_rows * pitch
    blocks = band_rows // block_rows

    def flat_of(band):
        wide = jnp.pad(
            with_rims(band, "row", 1, rim_rows), ((0, 0), (extra_rows, extra_rows), (0, 0))
        )
        return jnp.pad(
            jnp.transpose(wide, (1, 2, 0)),
            ((1, 1), (pitch - columns, 0), (0, 0)),
        ).reshape((wide_rows + 2) * pitch, channel_count)

    geometry = (front, pitch, aspp_reach, block, blocks)
    own_sums = aspp_pass(
        flat_of(own_band), aspp_point, aspp_dilated, (), geometry, 0, False
    )

    counted = (semantic[0] >= THING_FIRST) & (instance[0] > 0)
    labels = jnp.arange(INSTANCES, dtype=jnp.int32)
    onehot = ((instance[0][None] == labels[:, None, None]) & counted[None]).astype(jnp.float32)
    row_pos = (row_index * band_rows + jnp.arange(band_rows, dtype=jnp.int32)).astype(jnp.float32)[
        :, None
    ] * jnp.ones((1, columns), jnp.float32)
    col_pos = jnp.arange(columns, dtype=jnp.float32)[None, :] * jnp.ones(
        (band_rows, 1), jnp.float32
    )
    local_stats = jnp.stack(
        [
            jnp.sum(onehot, axis=(1, 2)),
            jnp.sum(onehot * row_pos, axis=(1, 2)),
            jnp.sum(onehot * col_pos, axis=(1, 2)),
        ],
        0,
    )
    channel_sums = jnp.concatenate(
        [jnp.sum(band, axis=(1, 2), dtype=jnp.float32) for band in (own_band, later_band)]
    )
    frame_totals, inst_stats = all_sum((channel_sums, local_stats), ("row",))
    pooled = (frame_totals / (height * columns)).astype(jnp.bfloat16)
    pool_feature = relu_bf16(jnp.dot(pool_weight, pooled, preferred_element_type=jnp.float32))
    aspp_width = aspp_point.shape[0]
    pool_term = jnp.dot(
        proj_weight[:, 4 * aspp_width :], pool_feature, preferred_element_type=jnp.float32
    )[None]
    pad_columns = pitch - columns
    keep = (jnp.arange(block) % pitch >= pad_columns).astype(jnp.float32)[:, None]
    projected_flat = aspp_pass(
        flat_of(later_band),
        aspp_point,
        aspp_dilated,
        (own_sums, proj_weight, pool_term, keep),
        geometry,
        1,
        True,
    )
    head_reach = 2
    head_in = jnp.pad(
        with_rims(projected_flat, "row", 0, head_reach * pitch), ((pitch, pitch), (0, 0))
    )
    head_flat = head_kernel_call(head_in, head_weight, (pitch, pitch, head_reach, block, blocks))
    head_out = jnp.transpose(
        head_flat.reshape(band_rows, pitch, head_weight.shape[1])[:, pad_columns:], (2, 0, 1)
    )
    predictions = emit_heads(head_out, out_weight)
    pixel = jnp.sum(
        jnp.where(onehot[None] > 0.5, inst_stats[:, :, None, None], 0.0), axis=1
    )
    counts = jnp.where(counted, pixel[0], 1.0)
    centre_row = pixel[1] / counts
    centre_col = pixel[2] / counts
    distance = (row_pos - centre_row) * (row_pos - centre_row) + (col_pos - centre_col) * (
        col_pos - centre_col
    )
    heat = jnp.where(counted, jnp.exp(-distance / (2.0 * center_sigma * center_sigma)), 0.0)
    center_err = jnp.sum(jnp.square(predictions[0] - heat))
    offset_err = jnp.sum(
        jnp.where(
            counted,
            jnp.abs(predictions[1] - (centre_row - row_pos))
            + jnp.abs(predictions[2] - (centre_col - col_pos)),
            0.0,
        )
    )
    counted_local = jnp.sum(counted.astype(jnp.float32))
    local_totals = lax.optimization_barrier(jnp.stack([center_err, offset_err, counted_local]))
    totals = all_sum(local_totals, ("row", "tm"))
    center_total, offset_total, counted_total = totals[0], totals[1], totals[2]
    losses = jnp.stack(
        [
            center_total / (frame_count * height * columns),
            offset_weight * offset_total / jnp.maximum(counted_total, 1.0),
        ]
    )
    return (predictions[None], losses)


def solution(mesh):
    placed = (
        P(("grp", "tm"), None, "row", None),
        P("grp"),
        P(("grp", "tm"), "row", None),
        P(("grp", "tm"), "row", None),
        P(),
        P(),
        P(),
        P(),
        P(),
        P(),
    )
    return jax.shard_map(
        shards,
        mesh=mesh,
        in_specs=placed,
        out_specs=(P(("grp", "tm"), None, "row", None), P("grp")),
        check_vma=False,
    )
```

```python
import jax
import jax.numpy as jnp
from jax import lax
from jax.sharding import PartitionSpec as P
from jax.experimental import pallas as pl
from jax.experimental.pallas import tpu as pltpu

THING_FIRST = 11
INSTANCES = 64


DILATIONS = (6, 12, 18)
aspp_reach = 18
center_sigma = 8.0
offset_weight = 0.01


def padded_2(block, sides, width):
    for axis, dim in sides:
        count = lax.axis_size(axis)
        forward = [(i, i + 1) for i in range(count - 1)]
        backward = [(target, source) for source, target in forward]
        low = lax.ppermute(
            lax.slice_in_dim(block, block.shape[dim] - width, None, axis=dim), axis, forward
        )
        high = lax.ppermute(lax.slice_in_dim(block, 0, width, axis=dim), axis, backward)
        block = jnp.concatenate([low, block, high], axis=dim)
    return block


def with_rims(block, axis, dim, width):
    if lax.axis_size(axis) != 2:
        return padded_2(block, ((axis, dim),), width)
    first = lax.axis_index(axis) == 0
    size = block.shape[dim]
    sent = lax.dynamic_slice_in_dim(block, jnp.where(first, size - width, 0), width, axis=dim)
    got = lax.ppermute(sent, axis, [(0, 1), (1, 0)])
    empty = jnp.zeros_like(got)
    low = jnp.where(first, empty, got)
    high = jnp.where(first, got, empty)
    return jnp.concatenate([low, block, high], axis=dim)


def shifted(value, axis, steps):
    count = lax.axis_size(axis)
    pairs = [(source, (source + steps) % count) for source in range(count)]
    return lax.ppermute(value, axis, pairs)


def all_sum(value, axes):
    for axis in axes:
        count = lax.axis_size(axis)
        if count & (count - 1):
            value = jax.tree.map(lambda v: lax.psum(v, axis), value)
            continue
        step = 1
        while step < count:
            pairs = [(i, i ^ step) for i in range(count)]
            other = lax.ppermute(value, axis, pairs)
            value = jax.tree.map(jnp.add, value, other)
            step *= 2
    return value


def aspp_pass(x, aspp_point, aspp_dilated, extra, geometry, part, finish):
    front, pitch, margin, block, blocks = geometry
    width = aspp_point.shape[0]
    channels = x.shape[1]
    lanes = pl.ds(part * channels, channels)
    contract = (((1,), (1,)), ((), ()))
    branches = 1 + len(DILATIONS)

    def body(x_ref, point_ref, dilated_ref, *rest):
        if finish:
            earlier_hbm, proj_ref, pool_ref, keep_ref, out_ref, earlier_ref, sems = rest
        else:
            out_hbm, out_ref, sems = rest

        def block_copy(index):
            rows = pl.ds(index * block, block)
            if finish:
                return pltpu.make_async_copy(
                    earlier_hbm.at[:, rows, :], earlier_ref.at[:, rows, :], sems.at[index]
                )
            return pltpu.make_async_copy(
                out_ref.at[:, rows, :], out_hbm.at[:, rows, :], sems.at[index]
            )

        if finish:
            for index in range(blocks):
                block_copy(index).start()
        for index in range(blocks):
            base = front + margin * pitch + index * block
            rows = pl.ds(index * block, block)
            if finish:
                block_copy(index).wait()

            def window(shift):
                return x_ref[pl.ds(base + shift, block), :]

            sums = [
                lax.dot_general(
                    window(0), point_ref[:, lanes], contract, preferred_element_type=jnp.float32
                )
            ]
            for branch, spread in enumerate(DILATIONS):
                total = None
                for vertical in range(3):
                    for lateral in range(3):
                        shift = (vertical - 1) * spread * pitch + (lateral - 1) * spread
                        term = lax.dot_general(
                            window(shift),
                            dilated_ref[branch, 3 * vertical + lateral, :, lanes],
                            contract,
                            preferred_element_type=jnp.float32,
                        )
                        total = term if total is None else total + term
                sums.append(total)
            if not finish:
                for branch, total in enumerate(sums):
                    out_ref[branch, rows, :] = total
                block_copy(index).start()
                continue
            mixed = None
            for branch, total in enumerate(sums):
                term = lax.dot_general(
                    relu_bf16(earlier_ref[branch, rows, :] + total),
                    proj_ref[:, branch * width : (branch + 1) * width],
                    contract,
                    preferred_element_type=jnp.float32,
                )
                mixed = term if mixed is None else mixed + term
            mixed = mixed + pool_ref[...]
            rounded = relu_bf16(mixed).astype(jnp.float32)
            out_ref[rows, :] = jnp.where(keep_ref[...] > 0.5, rounded, 0.0)
        if not finish:
            for index in range(blocks):
                block_copy(index).wait()

    taps = 1 + 9 * len(DILATIONS)
    flops = 2 * blocks * block * channels * width * taps
    sums_shape = (branches, blocks * block, width)
    vmem = pl.BlockSpec(memory_space=pltpu.VMEM)
    hbm = pl.BlockSpec(memory_space=pl.ANY)
    scratch = [pltpu.VMEM(sums_shape, jnp.float32), pltpu.SemaphoreType.DMA((blocks,))]
    if finish:
        flops += 2 * blocks * block * branches * width * width
        out_shape = jax.ShapeDtypeStruct((blocks * block, width), jnp.float32)
        in_specs = [vmem, vmem, vmem, hbm, vmem, vmem, vmem]
        out_specs = vmem
    else:
        out_shape = jax.ShapeDtypeStruct(sums_shape, jnp.float32)
        in_specs = [vmem, vmem, vmem]
        out_specs = hbm
    return pl.pallas_call(
        body,
        out_shape=out_shape,
        in_specs=in_specs,
        out_specs=out_specs,
        scratch_shapes=scratch,
        compiler_params=pltpu.CompilerParams(vmem_limit_bytes=56 * 1024 * 1024),
        cost_estimate=pl.CostEstimate(
            flops=flops,
            transcendentals=0,
            bytes_accessed=x.size * 2
            + aspp_dilated.size
            + branches * blocks * block * width * 4,
        ),
    )(x, aspp_point, aspp_dilated, *extra)


def head_kernel_call(x, head_weight, geometry):
    front, pitch, reach, block, blocks = geometry
    outputs = head_weight.shape[1]
    side = 2 * reach + 1
    contract = (((1,), (1,)), ((), ()))

    def body(x_ref, weight_ref, out_ref):
        for index in range(blocks):
            base = front + reach * pitch + index * block
            total = None
            for vertical in range(side):
                for lateral in range(side):
                    shift = (vertical - reach) * pitch + (lateral - reach)
                    term = lax.dot_general(
                        x_ref[pl.ds(base + shift, block), :].astype(jnp.bfloat16),
                        weight_ref[side * vertical + lateral],
                        contract,
                        preferred_element_type=jnp.float32,
                    )
                    total = term if total is None else total + term
            out_ref[pl.ds(index * block, block), :] = relu_bf16(total)

    return pl.pallas_call(
        body,
        out_shape=jax.ShapeDtypeStruct((blocks * block, outputs), jnp.bfloat16),
        compiler_params=pltpu.CompilerParams(vmem_limit_bytes=32 * 1024 * 1024),
        cost_estimate=pl.CostEstimate(
            flops=2 * blocks * block * x.shape[1] * outputs * side * side,
            transcendentals=0,
            bytes_accessed=x.size * 4 + head_weight.size * 2 + blocks * block * outputs * 2,
        ),
    )(x, head_weight)


def relu_bf16(values):
    return jnp.maximum(values, 0.0).astype(jnp.bfloat16)


def emit_heads(head_out, out_weight):
    groups = head_out.reshape(3, -1, head_out.shape[1], head_out.shape[2])
    center_map = jnp.einsum(
        "c,crw->rw", out_weight[0], groups[0], preferred_element_type=jnp.float32
    )
    offset_map = jnp.einsum(
        "oc,crw->orw", out_weight[1:3], groups[1], preferred_element_type=jnp.float32
    )
    depth_map = jnp.einsum(
        "c,crw->rw", out_weight[3], groups[2], preferred_element_type=jnp.float32
    )
    return jnp.concatenate([center_map[None], offset_map, depth_map[None]], 0)


def shards(
    frames,
    clip_start,
    semantic,
    instance,
    aspp_point,
    aspp_dilated,
    pool_weight,
    proj_weight,
    head_weight,
    out_weight,
):
    own_band = frames[0]
    channel_count, band_rows, columns = own_band.shape
    frame_count = clip_start.shape[0]
    height = band_rows * lax.axis_size("row")
    time_index = lax.axis_index("tm")
    row_index = lax.axis_index("row")
    ahead = (time_index + 1) % frame_count
    at_end = jnp.sum(jnp.where(jnp.arange(frame_count) == ahead, clip_start, 0)) == 1
    later_band = jnp.where(at_end, own_band, shifted(own_band, "tm", -1))
    rim_rows = min(aspp_reach, band_rows)
    extra_rows = aspp_reach - rim_rows

    wide_rows = band_rows + 2 * aspp_reach
    pitch = -(-(columns + aspp_reach) // 16) * 16
    front = pitch
    block_rows = 8 if band_rows % 8 == 0 else band_rows
    block = block_rows * pitch
    blocks = band_rows // block_rows

    def flat_of(band):
        wide = jnp.pad(
            with_rims(band, "row", 1, rim_rows), ((0, 0), (extra_rows, extra_rows), (0, 0))
        )
        return jnp.pad(
            jnp.transpose(wide, (1, 2, 0)),
            ((1, 1), (pitch - columns, 0), (0, 0)),
        ).reshape((wide_rows + 2) * pitch, channel_count)

    geometry = (front, pitch, aspp_reach, block, blocks)
    own_sums = aspp_pass(
        flat_of(own_band), aspp_point, aspp_dilated, (), geometry, 0, False
    )

    counted = (semantic[0] >= THING_FIRST) & (instance[0] > 0)
    labels = jnp.arange(INSTANCES, dtype=jnp.int32)
    onehot = ((instance[0][None] == labels[:, None, None]) & counted[None]).astype(jnp.float32)
    row_pos = (row_index * band_rows + jnp.arange(band_rows, dtype=jnp.int32)).astype(jnp.float32)[
        :, None
    ] * jnp.ones((1, columns), jnp.float32)
    col_pos = jnp.arange(columns, dtype=jnp.float32)[None, :] * jnp.ones(
        (band_rows, 1), jnp.float32
    )
    local_stats = jnp.stack(
        [
            jnp.sum(onehot, axis=(1, 2)),
            jnp.sum(onehot * row_pos, axis=(1, 2)),
            jnp.sum(onehot * col_pos, axis=(1, 2)),
        ],
        0,
    )
    channel_sums = jnp.concatenate(
        [jnp.sum(band, axis=(1, 2), dtype=jnp.float32) for band in (own_band, later_band)]
    )
    frame_totals, inst_stats = all_sum((channel_sums, local_stats), ("row",))
    pooled = (frame_totals / (height * columns)).astype(jnp.bfloat16)
    pool_feature = relu_bf16(jnp.dot(pool_weight, pooled, preferred_element_type=jnp.float32))
    aspp_width = aspp_point.shape[0]
    pool_term = jnp.dot(
        proj_weight[:, 4 * aspp_width :], pool_feature, preferred_element_type=jnp.float32
    )[None]
    pad_columns = pitch - columns
    keep = (jnp.arange(block) % pitch >= pad_columns).astype(jnp.float32)[:, None]
    projected_flat = aspp_pass(
        flat_of(later_band),
        aspp_point,
        aspp_dilated,
        (own_sums, proj_weight, pool_term, keep),
        geometry,
        1,
        True,
    )
    head_reach = 2
    head_in = jnp.pad(
        with_rims(projected_flat, "row", 0, head_reach * pitch), ((pitch, pitch), (0, 0))
    )
    head_flat = head_kernel_call(head_in, head_weight, (pitch, pitch, head_reach, block, blocks))
    head_out = jnp.transpose(
        head_flat.reshape(band_rows, pitch, head_weight.shape[1])[:, pad_columns:], (2, 0, 1)
    )
    predictions = emit_heads(head_out, out_weight)
    pixel = jnp.sum(
        jnp.where(onehot[None] > 0.5, inst_stats[:, :, None, None], 0.0), axis=1
    )
    counts = jnp.where(counted, pixel[0], 1.0)
    centre_row = pixel[1] / counts
    centre_col = pixel[2] / counts
    distance = (row_pos - centre_row) * (row_pos - centre_row) + (col_pos - centre_col) * (
        col_pos - centre_col
    )
    heat = jnp.where(counted, jnp.exp(-distance / (2.0 * center_sigma * center_sigma)), 0.0)
    center_err = jnp.sum(jnp.square(predictions[0] - heat))
    offset_err = jnp.sum(
        jnp.where(
            counted,
            jnp.abs(predictions[1] - (centre_row - row_pos))
            + jnp.abs(predictions[2] - (centre_col - col_pos)),
            0.0,
        )
    )
    counted_local = jnp.sum(counted.astype(jnp.float32))
    local_totals = lax.optimization_barrier(jnp.stack([center_err, offset_err, counted_local]))
    totals = all_sum(local_totals, ("row", "tm"))
    center_total, offset_total, counted_total = totals[0], totals[1], totals[2]
    losses = jnp.stack(
        [
            center_total / (frame_count * height * columns),
            offset_weight * offset_total / jnp.maximum(counted_total, 1.0),
        ]
    )
    return (predictions[None], losses)


def solution(mesh):
    placed = (
        P(("grp", "tm"), None, "row", None),
        P("grp"),
        P(("grp", "tm"), "row", None),
        P(("grp", "tm"), "row", None),
        P(),
        P(),
        P(),
        P(),
        P(),
        P(),
    )
    return jax.shard_map(
        shards,
        mesh=mesh,
        in_specs=placed,
        out_specs=(P(("grp", "tm"), None, "row", None), P("grp")),
        check_vma=False,
    )
```

```python
import jax
import jax.numpy as jnp
from jax import lax
from jax.sharding import PartitionSpec as P
from jax.experimental import pallas as pl
from jax.experimental.pallas import tpu as pltpu

THING_FIRST = 11
INSTANCES = 64


DILATIONS = (6, 12, 18)
aspp_reach = 18
center_sigma = 8.0
offset_weight = 0.01


def padded_2(block, sides, width):
    for axis, dim in sides:
        count = lax.axis_size(axis)
        forward = [(i, i + 1) for i in range(count - 1)]
        backward = [(target, source) for source, target in forward]
        low = lax.ppermute(
            lax.slice_in_dim(block, block.shape[dim] - width, None, axis=dim), axis, forward
        )
        high = lax.ppermute(lax.slice_in_dim(block, 0, width, axis=dim), axis, backward)
        block = jnp.concatenate([low, block, high], axis=dim)
    return block


def with_rims(block, axis, dim, width):
    if lax.axis_size(axis) != 2:
        return padded_2(block, ((axis, dim),), width)
    first = lax.axis_index(axis) == 0
    size = block.shape[dim]
    sent = jnp.where(
        first,
        lax.slice_in_dim(block, size - width, None, axis=dim),
        lax.slice_in_dim(block, 0, width, axis=dim),
    )
    got = lax.ppermute(sent, axis, [(0, 1), (1, 0)])
    empty = jnp.zeros_like(got)
    low = jnp.where(first, empty, got)
    high = jnp.where(first, got, empty)
    return jnp.concatenate([low, block, high], axis=dim)


def shifted(value, axis, steps):
    count = lax.axis_size(axis)
    pairs = [(source, (source + steps) % count) for source in range(count)]
    return lax.ppermute(value, axis, pairs)


def all_sum(value, axes):
    for axis in axes:
        count = lax.axis_size(axis)
        if count & (count - 1):
            value = jax.tree.map(lambda v: lax.psum(v, axis), value)
            continue
        step = 1
        while step < count:
            pairs = [(i, i ^ step) for i in range(count)]
            other = lax.ppermute(value, axis, pairs)
            value = jax.tree.map(jnp.add, value, other)
            step *= 2
    return value


def aspp_pass(x, aspp_point, aspp_dilated, extra, geometry, part, finish):
    front, pitch, margin, block, blocks = geometry
    width = aspp_point.shape[0]
    channels = x.shape[1]
    lanes = pl.ds(part * channels, channels)
    contract = (((1,), (1,)), ((), ()))
    branches = 1 + len(DILATIONS)

    def body(x_ref, point_ref, dilated_ref, *rest):
        if finish:
            earlier_hbm, proj_ref, pool_ref, keep_ref, out_ref, earlier_ref, sems = rest
        else:
            out_hbm, out_ref, sems = rest

        def block_copy(index):
            rows = pl.ds(index * block, block)
            if finish:
                return pltpu.make_async_copy(
                    earlier_hbm.at[:, rows, :], earlier_ref.at[:, rows, :], sems.at[index]
                )
            return pltpu.make_async_copy(
                out_ref.at[:, rows, :], out_hbm.at[:, rows, :], sems.at[index]
            )

        if finish:
            for index in range(blocks):
                block_copy(index).start()
        for index in range(blocks):
            base = front + margin * pitch + index * block
            rows = pl.ds(index * block, block)
            if finish:
                block_copy(index).wait()

            def window(shift):
                return x_ref[pl.ds(base + shift, block), :]

            sums = [
                lax.dot_general(
                    window(0), point_ref[:, lanes], contract, preferred_element_type=jnp.float32
                )
            ]
            for branch, spread in enumerate(DILATIONS):
                total = None
                for vertical in range(3):
                    for lateral in range(3):
                        shift = (vertical - 1) * spread * pitch + (lateral - 1) * spread
                        term = lax.dot_general(
                            window(shift),
                            dilated_ref[branch, 3 * vertical + lateral, :, lanes],
                            contract,
                            preferred_element_type=jnp.float32,
                        )
                        total = term if total is None else total + term
                sums.append(total)
            if not finish:
                for branch, total in enumerate(sums):
                    out_ref[branch, rows, :] = total
                block_copy(index).start()
                continue
            mixed = None
            for branch, total in enumerate(sums):
                term = lax.dot_general(
                    relu_bf16(earlier_ref[branch, rows, :] + total),
                    proj_ref[:, branch * width : (branch + 1) * width],
                    contract,
                    preferred_element_type=jnp.float32,
                )
                mixed = term if mixed is None else mixed + term
            mixed = mixed + pool_ref[...]
            rounded = relu_bf16(mixed)
            out_ref[rows, :] = jnp.where(keep_ref[...] > 0.5, rounded, jnp.zeros_like(rounded))
        if not finish:
            for index in range(blocks):
                block_copy(index).wait()

    taps = 1 + 9 * len(DILATIONS)
    flops = 2 * blocks * block * channels * width * taps
    sums_shape = (branches, blocks * block, width)
    vmem = pl.BlockSpec(memory_space=pltpu.VMEM)
    hbm = pl.BlockSpec(memory_space=pl.ANY)
    scratch = [pltpu.VMEM(sums_shape, jnp.float32), pltpu.SemaphoreType.DMA((blocks,))]
    if finish:
        flops += 2 * blocks * block * branches * width * width
        out_shape = jax.ShapeDtypeStruct((blocks * block, width), jnp.bfloat16)
        in_specs = [vmem, vmem, vmem, hbm, vmem, vmem, vmem]
        out_specs = vmem
    else:
        out_shape = jax.ShapeDtypeStruct(sums_shape, jnp.float32)
        in_specs = [vmem, vmem, vmem]
        out_specs = hbm
    return pl.pallas_call(
        body,
        out_shape=out_shape,
        in_specs=in_specs,
        out_specs=out_specs,
        scratch_shapes=scratch,
        compiler_params=pltpu.CompilerParams(vmem_limit_bytes=56 * 1024 * 1024),
        cost_estimate=pl.CostEstimate(
            flops=flops,
            transcendentals=0,
            bytes_accessed=x.size * 2
            + aspp_dilated.size
            + branches * blocks * block * width * 4,
        ),
    )(x, aspp_point, aspp_dilated, *extra)


def head_kernel_call(x, head_weight, geometry):
    front, pitch, reach, block, blocks = geometry
    outputs = head_weight.shape[1]
    side = 2 * reach + 1
    contract = (((1,), (1,)), ((), ()))

    def body(x_ref, weight_ref, out_ref):
        for index in range(blocks):
            base = front + reach * pitch + index * block
            total = None
            for vertical in range(side):
                for lateral in range(side):
                    shift = (vertical - reach) * pitch + (lateral - reach)
                    term = lax.dot_general(
                        x_ref[pl.ds(base + shift, block), :],
                        weight_ref[side * vertical + lateral],
                        contract,
                        preferred_element_type=jnp.float32,
                    )
                    total = term if total is None else total + term
            out_ref[pl.ds(index * block, block), :] = relu_bf16(total)

    return pl.pallas_call(
        body,
        out_shape=jax.ShapeDtypeStruct((blocks * block, outputs), jnp.bfloat16),
        compiler_params=pltpu.CompilerParams(vmem_limit_bytes=32 * 1024 * 1024),
        cost_estimate=pl.CostEstimate(
            flops=2 * blocks * block * x.shape[1] * outputs * side * side,
            transcendentals=0,
            bytes_accessed=x.size * 2 + head_weight.size * 2 + blocks * block * outputs * 2,
        ),
    )(x, head_weight)


def relu_bf16(values):
    return jnp.maximum(values, 0.0).astype(jnp.bfloat16)


def emit_heads(head_out, out_weight):
    groups = head_out.reshape(3, -1, head_out.shape[1], head_out.shape[2])
    center_map = jnp.einsum(
        "c,crw->rw", out_weight[0], groups[0], preferred_element_type=jnp.float32
    )
    offset_map = jnp.einsum(
        "oc,crw->orw", out_weight[1:3], groups[1], preferred_element_type=jnp.float32
    )
    depth_map = jnp.einsum(
        "c,crw->rw", out_weight[3], groups[2], preferred_element_type=jnp.float32
    )
    return jnp.concatenate([center_map[None], offset_map, depth_map[None]], 0)


def shards(
    frames,
    clip_start,
    semantic,
    instance,
    aspp_point,
    aspp_dilated,
    pool_weight,
    proj_weight,
    head_weight,
    out_weight,
):
    own_band = frames[0]
    channel_count, band_rows, columns = own_band.shape
    frame_count = clip_start.shape[0]
    height = band_rows * lax.axis_size("row")
    time_index = lax.axis_index("tm")
    row_index = lax.axis_index("row")
    ahead = (time_index + 1) % frame_count
    at_end = jnp.sum(jnp.where(jnp.arange(frame_count) == ahead, clip_start, 0)) == 1
    later_band = jnp.where(at_end, own_band, shifted(own_band, "tm", -1))
    rim_rows = min(aspp_reach, band_rows)
    extra_rows = aspp_reach - rim_rows

    wide_rows = band_rows + 2 * aspp_reach
    pitch = -(-(columns + aspp_reach) // 16) * 16
    front = pitch
    block_rows = 8 if band_rows % 8 == 0 else band_rows
    block = block_rows * pitch
    blocks = band_rows // block_rows

    def flat_of(band):
        wide = jnp.pad(
            with_rims(band, "row", 1, rim_rows), ((0, 0), (extra_rows, extra_rows), (0, 0))
        )
        return jnp.pad(
            jnp.transpose(wide, (1, 2, 0)),
            ((1, 1), (pitch - columns, 0), (0, 0)),
        ).reshape((wide_rows + 2) * pitch, channel_count)

    geometry = (front, pitch, aspp_reach, block, blocks)
    own_sums = aspp_pass(
        flat_of(own_band), aspp_point, aspp_dilated, (), geometry, 0, False
    )

    counted = (semantic[0] >= THING_FIRST) & (instance[0] > 0)
    labels = jnp.arange(INSTANCES, dtype=jnp.int32)
    onehot = ((instance[0][None] == labels[:, None, None]) & counted[None]).astype(jnp.float32)
    row_pos = (row_index * band_rows + jnp.arange(band_rows, dtype=jnp.int32)).astype(jnp.float32)[
        :, None
    ] * jnp.ones((1, columns), jnp.float32)
    col_pos = jnp.arange(columns, dtype=jnp.float32)[None, :] * jnp.ones(
        (band_rows, 1), jnp.float32
    )
    local_stats = jnp.stack(
        [
            jnp.sum(onehot, axis=(1, 2)),
            jnp.sum(onehot * row_pos, axis=(1, 2)),
            jnp.sum(onehot * col_pos, axis=(1, 2)),
        ],
        0,
    )
    channel_sums = jnp.concatenate(
        [jnp.sum(band, axis=(1, 2), dtype=jnp.float32) for band in (own_band, later_band)]
    )
    frame_totals, inst_stats = all_sum((channel_sums, local_stats), ("row",))
    pooled = (frame_totals / (height * columns)).astype(jnp.bfloat16)
    pool_feature = relu_bf16(jnp.dot(pool_weight, pooled, preferred_element_type=jnp.float32))
    aspp_width = aspp_point.shape[0]
    pool_term = jnp.dot(
        proj_weight[:, 4 * aspp_width :], pool_feature, preferred_element_type=jnp.float32
    )[None]
    pad_columns = pitch - columns
    keep = (jnp.arange(block) % pitch >= pad_columns).astype(jnp.float32)[:, None]
    projected_flat = aspp_pass(
        flat_of(later_band),
        aspp_point,
        aspp_dilated,
        (own_sums, proj_weight, pool_term, keep),
        geometry,
        1,
        True,
    )
    head_reach = 2
    head_in = jnp.pad(
        with_rims(projected_flat, "row", 0, head_reach * pitch), ((pitch, pitch), (0, 0))
    )
    head_flat = head_kernel_call(head_in, head_weight, (pitch, pitch, head_reach, block, blocks))
    head_out = jnp.transpose(
        head_flat.reshape(band_rows, pitch, head_weight.shape[1])[:, pad_columns:], (2, 0, 1)
    )
    predictions = emit_heads(head_out, out_weight)
    pixel = jnp.sum(
        jnp.where(onehot[None] > 0.5, inst_stats[:, :, None, None], 0.0), axis=1
    )
    counts = jnp.where(counted, pixel[0], 1.0)
    centre_row = pixel[1] / counts
    centre_col = pixel[2] / counts
    distance = (row_pos - centre_row) * (row_pos - centre_row) + (col_pos - centre_col) * (
        col_pos - centre_col
    )
    heat = jnp.where(counted, jnp.exp(-distance / (2.0 * center_sigma * center_sigma)), 0.0)
    center_err = jnp.sum(jnp.square(predictions[0] - heat))
    offset_err = jnp.sum(
        jnp.where(
            counted,
            jnp.abs(predictions[1] - (centre_row - row_pos))
            + jnp.abs(predictions[2] - (centre_col - col_pos)),
            0.0,
        )
    )
    counted_local = jnp.sum(counted.astype(jnp.float32))
    local_totals = lax.optimization_barrier(jnp.stack([center_err, offset_err, counted_local]))
    totals = all_sum(local_totals, ("row", "tm"))
    center_total, offset_total, counted_total = totals[0], totals[1], totals[2]
    losses = jnp.stack(
        [
            center_total / (frame_count * height * columns),
            offset_weight * offset_total / jnp.maximum(counted_total, 1.0),
        ]
    )
    return (predictions[None], losses)


def solution(mesh):
    placed = (
        P(("grp", "tm"), None, "row", None),
        P("grp"),
        P(("grp", "tm"), "row", None),
        P(("grp", "tm"), "row", None),
        P(),
        P(),
        P(),
        P(),
        P(),
        P(),
    )
    return jax.shard_map(
        shards,
        mesh=mesh,
        in_specs=placed,
        out_specs=(P(("grp", "tm"), None, "row", None), P("grp")),
        check_vma=False,
    )
```

```python
import jax
import jax.numpy as jnp
from jax import lax
from jax.sharding import PartitionSpec as P
from jax.experimental import pallas as pl
from jax.experimental.pallas import tpu as pltpu

THING_FIRST = 11
INSTANCES = 64


DILATIONS = (6, 12, 18)
aspp_reach = 18
center_sigma = 8.0
offset_weight = 0.01


def padded_2(block, sides, width):
    for axis, dim in sides:
        count = lax.axis_size(axis)
        forward = [(i, i + 1) for i in range(count - 1)]
        backward = [(target, source) for source, target in forward]
        low = lax.ppermute(
            lax.slice_in_dim(block, block.shape[dim] - width, None, axis=dim), axis, forward
        )
        high = lax.ppermute(lax.slice_in_dim(block, 0, width, axis=dim), axis, backward)
        block = jnp.concatenate([low, block, high], axis=dim)
    return block


def with_rims(block, axis, dim, width):
    if lax.axis_size(axis) != 2:
        return padded_2(block, ((axis, dim),), width)
    first = lax.axis_index(axis) == 0
    size = block.shape[dim]
    sent = jnp.where(
        first,
        lax.slice_in_dim(block, size - width, None, axis=dim),
        lax.slice_in_dim(block, 0, width, axis=dim),
    )
    got = lax.ppermute(sent, axis, [(0, 1), (1, 0)])
    empty = jnp.zeros_like(got)
    low = jnp.where(first, empty, got)
    high = jnp.where(first, got, empty)
    return jnp.concatenate([low, block, high], axis=dim)


def shifted(value, axis, steps):
    count = lax.axis_size(axis)
    pairs = [(source, (source + steps) % count) for source in range(count)]
    return lax.ppermute(value, axis, pairs)


def all_sum(value, axes):
    for axis in axes:
        count = lax.axis_size(axis)
        if count & (count - 1):
            value = jax.tree.map(lambda v: lax.psum(v, axis), value)
            continue
        step = 1
        while step < count:
            pairs = [(i, i ^ step) for i in range(count)]
            other = lax.ppermute(value, axis, pairs)
            value = jax.tree.map(jnp.add, value, other)
            step *= 2
    return value


def aspp_pass(x, aspp_point, aspp_dilated, extra, geometry, part, finish):
    front, pitch, margin, block, blocks = geometry
    width = aspp_point.shape[0]
    channels = x.shape[1]
    lanes = pl.ds(part * channels, channels)
    contract = (((1,), (1,)), ((), ()))
    branches = 1 + len(DILATIONS)

    def body(x_ref, point_ref, dilated_ref, *rest):
        if finish:
            earlier_hbm, proj_ref, pool_ref, keep_ref, out_ref, earlier_ref, sems = rest
        else:
            out_hbm, out_ref, sems = rest

        def block_copy(index):
            rows = pl.ds(index * block, block)
            if finish:
                return pltpu.make_async_copy(
                    earlier_hbm.at[:, rows, :], earlier_ref.at[:, rows, :], sems.at[index]
                )
            return pltpu.make_async_copy(
                out_ref.at[:, rows, :], out_hbm.at[:, rows, :], sems.at[index]
            )

        if finish:
            for index in range(blocks):
                block_copy(index).start()
        for index in range(blocks):
            base = front + margin * pitch + index * block
            rows = pl.ds(index * block, block)
            if finish:
                block_copy(index).wait()

            def window(shift):
                return x_ref[pl.ds(base + shift, block), :]

            sums = [
                lax.dot_general(
                    window(0), point_ref[:, lanes], contract, preferred_element_type=jnp.float32
                )
            ]
            for branch, spread in enumerate(DILATIONS):
                total = None
                for vertical in range(3):
                    for lateral in range(3):
                        shift = (vertical - 1) * spread * pitch + (lateral - 1) * spread
                        term = lax.dot_general(
                            window(shift),
                            dilated_ref[branch, 3 * vertical + lateral, :, lanes],
                            contract,
                            preferred_element_type=jnp.float32,
                        )
                        total = term if total is None else total + term
                sums.append(total)
            if not finish:
                for branch, total in enumerate(sums):
                    out_ref[branch, rows, :] = total
                block_copy(index).start()
                continue
            mixed = None
            for branch, total in enumerate(sums):
                term = lax.dot_general(
                    relu_bf16(earlier_ref[branch, rows, :] + total),
                    proj_ref[:, branch * width : (branch + 1) * width],
                    contract,
                    preferred_element_type=jnp.float32,
                )
                mixed = term if mixed is None else mixed + term
            mixed = mixed + lax.dot_general(
                pool_ref[...],
                proj_ref[:, branches * width : (branches + 1) * width],
                contract,
                preferred_element_type=jnp.float32,
            )
            rounded = relu_bf16(mixed)
            out_ref[rows, :] = jnp.where(keep_ref[...] > 0.5, rounded, jnp.zeros_like(rounded))
        if not finish:
            for index in range(blocks):
                block_copy(index).wait()

    taps = 1 + 9 * len(DILATIONS)
    flops = 2 * blocks * block * channels * width * taps
    sums_shape = (branches, blocks * block, width)
    vmem = pl.BlockSpec(memory_space=pltpu.VMEM)
    hbm = pl.BlockSpec(memory_space=pl.ANY)
    scratch = [pltpu.VMEM(sums_shape, jnp.float32), pltpu.SemaphoreType.DMA((blocks,))]
    if finish:
        flops += 2 * blocks * block * branches * width * width
        out_shape = jax.ShapeDtypeStruct((blocks * block, width), jnp.bfloat16)
        in_specs = [vmem, vmem, vmem, hbm, vmem, vmem, vmem]
        out_specs = vmem
    else:
        out_shape = jax.ShapeDtypeStruct(sums_shape, jnp.float32)
        in_specs = [vmem, vmem, vmem]
        out_specs = hbm
    return pl.pallas_call(
        body,
        out_shape=out_shape,
        in_specs=in_specs,
        out_specs=out_specs,
        scratch_shapes=scratch,
        compiler_params=pltpu.CompilerParams(vmem_limit_bytes=56 * 1024 * 1024),
        cost_estimate=pl.CostEstimate(
            flops=flops,
            transcendentals=0,
            bytes_accessed=x.size * 2
            + aspp_dilated.size
            + branches * blocks * block * width * 4,
        ),
    )(x, aspp_point, aspp_dilated, *extra)


def head_kernel_call(x, head_weight, geometry):
    front, pitch, reach, block, blocks = geometry
    outputs = head_weight.shape[1]
    side = 2 * reach + 1
    contract = (((1,), (1,)), ((), ()))

    def body(x_ref, weight_ref, out_ref):
        for index in range(blocks):
            base = front + reach * pitch + index * block
            total = None
            for vertical in range(side):
                for lateral in range(side):
                    shift = (vertical - reach) * pitch + (lateral - reach)
                    term = lax.dot_general(
                        x_ref[pl.ds(base + shift, block), :],
                        weight_ref[side * vertical + lateral],
                        contract,
                        preferred_element_type=jnp.float32,
                    )
                    total = term if total is None else total + term
            out_ref[pl.ds(index * block, block), :] = relu_bf16(total)

    return pl.pallas_call(
        body,
        out_shape=jax.ShapeDtypeStruct((blocks * block, outputs), jnp.bfloat16),
        compiler_params=pltpu.CompilerParams(vmem_limit_bytes=32 * 1024 * 1024),
        cost_estimate=pl.CostEstimate(
            flops=2 * blocks * block * x.shape[1] * outputs * side * side,
            transcendentals=0,
            bytes_accessed=x.size * 2 + head_weight.size * 2 + blocks * block * outputs * 2,
        ),
    )(x, head_weight)


def relu_bf16(values):
    return jnp.maximum(values, 0.0).astype(jnp.bfloat16)


def emit_heads(head_out, out_weight):
    groups = head_out.reshape(3, -1, head_out.shape[1], head_out.shape[2])
    center_map = jnp.einsum(
        "c,crw->rw", out_weight[0], groups[0], preferred_element_type=jnp.float32
    )
    offset_map = jnp.einsum(
        "oc,crw->orw", out_weight[1:3], groups[1], preferred_element_type=jnp.float32
    )
    depth_map = jnp.einsum(
        "c,crw->rw", out_weight[3], groups[2], preferred_element_type=jnp.float32
    )
    return jnp.concatenate([center_map[None], offset_map, depth_map[None]], 0)


def shards(
    frames,
    clip_start,
    semantic,
    instance,
    aspp_point,
    aspp_dilated,
    pool_weight,
    proj_weight,
    head_weight,
    out_weight,
):
    own_band = frames[0]
    channel_count, band_rows, columns = own_band.shape
    frame_count = clip_start.shape[0]
    height = band_rows * lax.axis_size("row")
    time_index = lax.axis_index("tm")
    row_index = lax.axis_index("row")
    ahead = (time_index + 1) % frame_count
    at_end = jnp.sum(jnp.where(jnp.arange(frame_count) == ahead, clip_start, 0)) == 1
    later_band = jnp.where(at_end, own_band, shifted(own_band, "tm", -1))
    rim_rows = min(aspp_reach, band_rows)
    extra_rows = aspp_reach - rim_rows

    wide_rows = band_rows + 2 * aspp_reach
    pitch = -(-(columns + aspp_reach) // 16) * 16
    front = pitch
    block_rows = 8 if band_rows % 8 == 0 else band_rows
    block = block_rows * pitch
    blocks = band_rows // block_rows

    def flat_of(band):
        wide = jnp.pad(
            with_rims(band, "row", 1, rim_rows), ((0, 0), (extra_rows, extra_rows), (0, 0))
        )
        return jnp.pad(
            jnp.transpose(wide, (1, 2, 0)),
            ((1, 1), (pitch - columns, 0), (0, 0)),
        ).reshape((wide_rows + 2) * pitch, channel_count)

    geometry = (front, pitch, aspp_reach, block, blocks)
    own_sums = aspp_pass(
        flat_of(own_band), aspp_point, aspp_dilated, (), geometry, 0, False
    )

    counted = (semantic[0] >= THING_FIRST) & (instance[0] > 0)
    labels = jnp.arange(INSTANCES, dtype=jnp.int32)
    onehot = ((instance[0][None] == labels[:, None, None]) & counted[None]).astype(jnp.float32)
    row_pos = (row_index * band_rows + jnp.arange(band_rows, dtype=jnp.int32)).astype(jnp.float32)[
        :, None
    ] * jnp.ones((1, columns), jnp.float32)
    col_pos = jnp.arange(columns, dtype=jnp.float32)[None, :] * jnp.ones(
        (band_rows, 1), jnp.float32
    )
    local_stats = jnp.stack(
        [
            jnp.sum(onehot, axis=(1, 2)),
            jnp.sum(onehot * row_pos, axis=(1, 2)),
            jnp.sum(onehot * col_pos, axis=(1, 2)),
        ],
        0,
    )
    channel_sums = jnp.concatenate(
        [jnp.sum(band, axis=(1, 2), dtype=jnp.float32) for band in (own_band, later_band)]
    )
    frame_totals, inst_stats = all_sum((channel_sums, local_stats), ("row",))
    pooled = (frame_totals / (height * columns)).astype(jnp.bfloat16)
    pool_feature = relu_bf16(jnp.dot(pool_weight, pooled, preferred_element_type=jnp.float32))
    aspp_width = aspp_point.shape[0]
    pool_term = pool_feature[None]
    pad_columns = pitch - columns
    keep = (jnp.arange(block) % pitch >= pad_columns).astype(jnp.float32)[:, None]
    projected_flat = aspp_pass(
        flat_of(later_band),
        aspp_point,
        aspp_dilated,
        (own_sums, proj_weight, pool_term, keep),
        geometry,
        1,
        True,
    )
    head_reach = 2
    head_in = jnp.pad(
        with_rims(projected_flat, "row", 0, head_reach * pitch), ((pitch, pitch), (0, 0))
    )
    head_flat = head_kernel_call(head_in, head_weight, (pitch, pitch, head_reach, block, blocks))
    head_out = jnp.transpose(
        head_flat.reshape(band_rows, pitch, head_weight.shape[1])[:, pad_columns:], (2, 0, 1)
    )
    predictions = emit_heads(head_out, out_weight)
    pixel = jnp.sum(
        jnp.where(onehot[None] > 0.5, inst_stats[:, :, None, None], 0.0), axis=1
    )
    counts = jnp.where(counted, pixel[0], 1.0)
    centre_row = pixel[1] / counts
    centre_col = pixel[2] / counts
    distance = (row_pos - centre_row) * (row_pos - centre_row) + (col_pos - centre_col) * (
        col_pos - centre_col
    )
    heat = jnp.where(counted, jnp.exp(-distance / (2.0 * center_sigma * center_sigma)), 0.0)
    center_err = jnp.sum(jnp.square(predictions[0] - heat))
    offset_err = jnp.sum(
        jnp.where(
            counted,
            jnp.abs(predictions[1] - (centre_row - row_pos))
            + jnp.abs(predictions[2] - (centre_col - col_pos)),
            0.0,
        )
    )
    counted_local = jnp.sum(counted.astype(jnp.float32))
    local_totals = lax.optimization_barrier(jnp.stack([center_err, offset_err, counted_local]))
    totals = all_sum(local_totals, ("row", "tm"))
    center_total, offset_total, counted_total = totals[0], totals[1], totals[2]
    losses = jnp.stack(
        [
            center_total / (frame_count * height * columns),
            offset_weight * offset_total / jnp.maximum(counted_total, 1.0),
        ]
    )
    return (predictions[None], losses)


def solution(mesh):
    placed = (
        P(("grp", "tm"), None, "row", None),
        P("grp"),
        P(("grp", "tm"), "row", None),
        P(("grp", "tm"), "row", None),
        P(),
        P(),
        P(),
        P(),
        P(),
        P(),
    )
    return jax.shard_map(
        shards,
        mesh=mesh,
        in_specs=placed,
        out_specs=(P(("grp", "tm"), None, "row", None), P("grp")),
        check_vma=False,
    )
```
